256 devices in a mesh: row: 8 (over y, core), col: 8 (over z_hi, x), page: 4 (over z_lo).
Axes of the slice: x: 4, y: 4, z: 8 (z_hi: 2, z_lo: 4; z = z_hi * 4 + z_lo), core: 2. Of those that a mesh axis runs over, the one named last changes fastest.
Arguments:
- tokens: bfloat16 [32, 512, 2048], P(('row', 'page'), None, 'col'), may hold values from -6 to 6
- lengths: int32 [32], P(('row', 'page')), may hold values from 1 to 512, 4096 in all
- page_slot: int32 [32, 4], P('row'), may hold values from 0 to 15, as said below
- w_query: float32 [2048, 1024], P(('row', 'page'), 'col'), may hold values from -0.125 to 0.125
- w_keyval: float32 [2, 2048, 256], P(None, ('row', 'page')), may hold values from -0.125 to 0.125
- w_out: float32 [1024, 2048], P('col', ('row', 'page')), may hold values from -0.1875 to 0.1875
- w_gateup: float32 [2, 2048, 5120], P(None, ('row', 'page'), 'col'), may hold values from -0.125 to 0.125
- w_down: float32 [5120, 2048], P('col', ('row', 'page')), may hold values from -0.078125 to 0.078125
- attn_gain: float32 [2048], replicated, may hold values from 0.1 to 1.9
- ffn_gain: float32 [2048], replicated, may hold values from 0.1 to 1.9
- query_gain: float32 [64], replicated, may hold values from 0.1 to 1.9
- key_gain: float32 [64], replicated, may hold values from 0.1 to 1.9
Outputs:
- layer_out: bfloat16 [32, 512, 2048], P(('row', 'page'), None, 'col')
- kv_pages: bfloat16 [2, 128, 128, 1024], P(None, ('row', 'page'), None, 'col')
The draws below stay inside these ranges and needn't reach their ends.
Inputs may be any that keep to these rules, and one draw needn't show every extreme that they name: `lengths`: each prompt's real tokens; in every draw some prompt has exactly 512. `page_slot`: within the prompts of one index of row the values are a permutation; page v belongs to index v // 4 of page; the 4 blocks of the prompts of one device send the same number of blocks to each of the 4 indices of page.
All inputs are finite; a program needn't handle non-finite values. No bound on the sum of `lengths` on one device may be relied on, other than what follows from the above.
Results may differ from the reference program's by a relative error of at most 0.012.
Values may be sent and summed in bfloat16 or wider, within the bound.
No kernel may reach another device: no remote copies, remote signals or barrier semaphores. Data moves between devices by JAX's collectives and lax.ppermute only.
A program may use at most 64 MiB of HBM per device.

```python
import math
import jax
import jax.numpy as jnp
import numpy as np
from jax import lax

D = 2048
H = 16
KVH = 4
HD = 64
FF = 5120
LEN = 512
PAGE_LEN = 128
PR_DEV = 1
PROMPTS = 32
BLOCKS = 4
N_ROW = 8
N_COL = 8
N_PAGE = 4


def draw_page_slot(key, part):
    per_device = PR_DEV * BLOCKS
    capacity = per_device // N_PAGE

    def one_sender(sender_key):
        owners = jax.random.permutation(sender_key, jnp.arange(per_device, dtype=jnp.int32) % N_PAGE)
        same_owner = owners[:, None] == owners[None, :]
        earlier = jnp.arange(per_device, dtype=jnp.int32)[None, :] < jnp.arange(per_device, dtype=jnp.int32)[:, None]
        order_in = jnp.sum((same_owner & earlier).astype(jnp.int32), axis=1)
        return (owners, order_in)

    def one_perm(owner_key):
        return jax.random.permutation(owner_key, per_device).astype(jnp.int32)

    def one_group(group_key):
        sender_keys = jax.random.split(jax.random.fold_in(group_key, 1), N_PAGE)
        owners, order_in = jax.vmap(one_sender)(sender_keys)
        recv_pos = jnp.arange(N_PAGE, dtype=jnp.int32)[:, None] * capacity + order_in
        owner_keys = jax.random.split(jax.random.fold_in(group_key, 2), N_PAGE)
        slot_perm = jax.vmap(one_perm)(owner_keys)
        return owners * per_device + slot_perm[owners, recv_pos]
    group_keys = jax.random.split(jax.random.fold_in(key, 7), N_ROW)
    slot_table = jax.vmap(one_group)(group_keys)
    return slot_table.reshape(PROMPTS, BLOCKS).astype(jnp.int32)


def shard_levels(stream_key, extent, pieces, low, top_value):
    level, own = 1.0, jax.random.fold_in(stream_key, 6)
    for axis_at, parts in pieces:
        draws = jnp.exp(jax.random.uniform(jax.random.fold_in(own, axis_at), (parts,), jnp.float32, low / len(pieces), top_value / len(pieces)))
        level = level * jnp.repeat(draws, extent[axis_at] // parts).reshape([-1 if axis == axis_at else 1 for axis in range(len(extent))])
    return level


def length_profile(number_of, total, bound, slope):
    weights = [(1 << 20) // math.isqrt(grade ** slope) + 1 for grade in range(2, number_of + 1)]
    spare, counts = total - bound - (number_of - 1), [1] * (number_of - 1)
    while spare > 0:
        movable = [i for i in range(number_of - 1) if counts[i] < bound]
        mass, budget = sum([weights[i] for i in movable]), spare
        for i in movable:
            extra = min(bound - counts[i], max(1, budget * weights[i] // mass), spare)
            counts[i] = counts[i] + extra
            spare = spare - extra
    return np.array([bound] + counts)


def uneven(stream_key, amount, total, limit, lean):
    if amount == 2:
        one = jax.random.randint(stream_key, (), max(1, total - limit), min(limit, total - 1) + 1)
        return jnp.stack([one, total - one])
    sizes = jnp.asarray(length_profile(amount, total, limit, lean), jnp.int32)
    pairs = (amount - 1) // 2
    source_of, taker = sizes[1:1 + 2 * pairs:2], sizes[2:2 + 2 * pairs:2]
    slack = jnp.minimum(source_of - 1, limit - taker)
    passed = jax.random.randint(jax.random.fold_in(stream_key, 1), (pairs,), 0, 1 << 20) % (slack + 1)
    sizes = sizes.at[1:1 + 2 * pairs:2].set(source_of - passed).at[2:2 + 2 * pairs:2].set(taker + passed)
    return sizes[jax.random.permutation(jax.random.fold_in(stream_key, 2), amount)]


def bell_draw(stream_key, extent, scale, reach, shards=(), held_as=jnp.bfloat16):
    values = jax.random.normal(stream_key, extent, jnp.float32) * scale
    if len(shards) > 0:
        values = shard_levels(stream_key, extent, shards, -0.22, 0.18) * values
    return jnp.clip(values, min=-reach, max=reach).astype(held_as)


def setup_inputs(seed: int = 0) -> dict:
    arg_keys = jax.random.split(jax.random.key(seed), 13)
    tokens = bell_draw(arg_keys[0], (PROMPTS, LEN, D), 1.0, 6.0, ((0, 32), (2, 8)))
    lengths = uneven(arg_keys[1], PROMPTS, PROMPTS * LEN // 4, LEN, 2).astype(jnp.int32)
    page_slot = draw_page_slot(jax.random.fold_in(arg_keys[12], 71), 0)
    w_query = bell_draw(arg_keys[3], (D, H * HD), D ** -0.5, 0.125, ((0, 32), (1, 8)), jnp.float32)
    w_keyval = bell_draw(arg_keys[4], (2, D, KVH * HD), D ** -0.5, 0.125, ((1, 32),), jnp.float32)
    w_out = bell_draw(arg_keys[5], (H * HD, D), (H * HD) ** -0.5, 0.1875, ((0, 8), (1, 32)), jnp.float32)
    w_gateup = bell_draw(arg_keys[6], (2, D, FF), D ** -0.5, 0.125, ((1, 32), (2, 8)), jnp.float32)
    w_down = bell_draw(arg_keys[7], (FF, D), FF ** -0.5, 0.078125, ((0, 8), (1, 32)), jnp.float32)
    attn_gain = jnp.clip(1.0 + 0.18 * jax.random.normal(arg_keys[8], (D,), jnp.float32), 0.1, 1.9)
    ffn_gain = jnp.clip(1.0 + 0.18 * jax.random.normal(arg_keys[9], (D,), jnp.float32), 0.1, 1.9)
    query_gain = jnp.clip(1.0 + 0.18 * jax.random.normal(arg_keys[10], (HD,), jnp.float32), 0.1, 1.9)
    key_gain = jnp.clip(1.0 + 0.18 * jax.random.normal(arg_keys[11], (HD,), jnp.float32), 0.1, 1.9)
    return dict(tokens=tokens, lengths=lengths, page_slot=page_slot, w_query=w_query, w_keyval=w_keyval, w_out=w_out, w_gateup=w_gateup, w_down=w_down, attn_gain=attn_gain, ffn_gain=ffn_gain, query_gain=query_gain, key_gain=key_gain)


def normalize(values, norm_gain):
    mean_sq = lax.optimization_barrier(jnp.mean(values * values, axis=-1, keepdims=True))
    return values * lax.rsqrt(mean_sq + 1e-06) * norm_gain

def rotate(values):
    row_count = values.shape[-3]
    head_dim = values.shape[-1]
    half_dim = head_dim // 2
    frequency = 10000.0 ** (-2.0 * jnp.arange(half_dim, dtype=jnp.float32) / head_dim)
    angles = jnp.arange(row_count, dtype=jnp.float32)[:, None] * frequency[None, :]
    cosine = jnp.cos(angles)[:, None, :]
    sine_table = jnp.sin(angles)[:, None, :]
    leading = values[..., :half_dim]
    trailing = values[..., half_dim:]
    return jnp.concatenate([leading * cosine - trailing * sine_table, trailing * cosine + leading * sine_table], axis=-1)

def attend(query_rows, key_rows, value_rows, length):
    row_count = query_rows.shape[0]
    scores = jnp.einsum('qhd,khd->hqk', query_rows.astype(jnp.float32), key_rows.astype(jnp.float32)) * query_rows.shape[2] ** (-0.5)
    positions = jnp.arange(row_count, dtype=jnp.int32)
    seen_keys = (positions[None, :] <= positions[:, None]) & (positions[None, :] < length)
    exp_scores = jnp.where(seen_keys[None], jnp.exp(scores), jnp.zeros_like(scores))
    attn_probs = (exp_scores / lax.optimization_barrier(jnp.sum(exp_scores, axis=-1, keepdims=True))).astype(jnp.bfloat16)
    attended = jnp.einsum('hqk,khd->qhd', attn_probs.astype(jnp.float32), value_rows.astype(jnp.float32))
    live_rows = (positions < length)[:, None, None]
    return jnp.where(live_rows, attended, jnp.zeros_like(attended)).astype(jnp.bfloat16)

def reference(tokens, lengths, page_slot, w_query, w_keyval, w_out, w_gateup, w_down, attn_gain, ffn_gain, query_gain, key_gain):
    query_server = w_query.astype(jnp.bfloat16)
    keyval_server = w_keyval.astype(jnp.bfloat16)
    out_server = w_out.astype(jnp.bfloat16)
    gateup_server = w_gateup.astype(jnp.bfloat16)
    down_server = w_down.astype(jnp.bfloat16)
    kv_index = jnp.arange(H, dtype=jnp.int32) // (H // KVH)
    columns = (kv_index[:, None] * HD + jnp.arange(HD, dtype=jnp.int32)[None, :]).reshape(-1)
    key_server = jnp.take(keyval_server[0], columns, axis=1)
    value_server = jnp.take(keyval_server[1], columns, axis=1)
    group_cols = H // N_COL * HD
    group_units = FF // N_COL

    def one_prompt(packed):
        prompt, length = packed
        attn_in = normalize(prompt.astype(jnp.float32), attn_gain).astype(jnp.bfloat16)
        q_raw = jnp.dot(attn_in, query_server, preferred_element_type=jnp.float32).reshape(LEN, H, HD)
        k_raw = jnp.dot(attn_in, key_server, preferred_element_type=jnp.float32).reshape(LEN, H, HD)
        v_raw = jnp.dot(attn_in, value_server, preferred_element_type=jnp.float32).reshape(LEN, H, HD)
        queries = rotate(normalize(q_raw, query_gain)).astype(jnp.bfloat16)
        keys_rot = rotate(normalize(k_raw, key_gain)).astype(jnp.bfloat16)
        values_in = v_raw.astype(jnp.bfloat16)
        attended = attend(queries, keys_rot, values_in, length).reshape(LEN, H * HD)
        attn_sum = jnp.zeros((LEN, D), jnp.float32)
        for group_num in range(N_COL):
            lower = group_num * group_cols
            term_part = jnp.dot(attended[:, lower:lower + group_cols], out_server[lower:lower + group_cols], preferred_element_type=jnp.float32)
            attn_sum = attn_sum + lax.optimization_barrier(term_part.astype(jnp.bfloat16)).astype(jnp.float32)
        residual = (prompt.astype(jnp.float32) + attn_sum).astype(jnp.bfloat16)
        ffn_in = normalize(residual.astype(jnp.float32), ffn_gain).astype(jnp.bfloat16)
        gate_proj = jnp.dot(ffn_in, gateup_server[0], preferred_element_type=jnp.float32)
        up_proj = jnp.dot(ffn_in, gateup_server[1], preferred_element_type=jnp.float32)
        hidden = (jax.nn.silu(gate_proj) * up_proj).astype(jnp.bfloat16)
        ffn_sum = jnp.zeros((LEN, D), jnp.float32)
        for group_num in range(N_COL):
            lower = group_num * group_units
            term_part = jnp.dot(hidden[:, lower:lower + group_units], down_server[lower:lower + group_units], preferred_element_type=jnp.float32)
            ffn_sum = ffn_sum + lax.optimization_barrier(term_part.astype(jnp.bfloat16)).astype(jnp.float32)
        layer_rows = (residual.astype(jnp.float32) + ffn_sum).astype(jnp.bfloat16)
        live_rows = (jnp.arange(LEN, dtype=jnp.int32) < length)[:, None, None]
        page_keys = jnp.where(live_rows, keys_rot, jnp.zeros_like(keys_rot)).reshape(BLOCKS, PAGE_LEN, H * HD)
        page_values = jnp.where(live_rows, values_in, jnp.zeros_like(values_in)).reshape(BLOCKS, PAGE_LEN, H * HD)
        return (layer_rows, jnp.stack([page_keys, page_values]))
    layer_out, blocks = lax.map(one_prompt, (tokens, lengths))
    group_base = jnp.arange(PROMPTS, dtype=jnp.int32) // (N_PAGE * PR_DEV) * (N_PAGE * PR_DEV * BLOCKS)
    targets = (group_base[:, None] + page_slot.astype(jnp.int32)).reshape(-1).astype(jnp.int32)
    ordered = jnp.transpose(blocks, (1, 0, 2, 3, 4)).reshape(2, PROMPTS * BLOCKS, PAGE_LEN, H * HD)
    kv_pages = jnp.zeros_like(ordered).at[:, targets].set(ordered)
    return (layer_out, kv_pages)
```

```python
import jax
import jax.numpy as jnp
from jax import lax
from jax.sharding import PartitionSpec as P

PAGE_LEN = 128


def normalize(values, norm_gain):
    mean_sq = jnp.mean(values * values, axis=-1, keepdims=True)
    return values * lax.rsqrt(mean_sq + 1e-06) * norm_gain


def rotate(values):
    row_count = values.shape[-3]
    head_dim = values.shape[-1]
    half_dim = head_dim // 2
    frequency = 10000.0 ** (-2.0 * jnp.arange(half_dim, dtype=jnp.float32) / head_dim)
    angles = jnp.arange(row_count, dtype=jnp.float32)[:, None] * frequency[None, :]
    cosine = jnp.cos(angles)[:, None, :]
    sine_table = jnp.sin(angles)[:, None, :]
    leading = values[..., :half_dim]
    trailing = values[..., half_dim:]
    return jnp.concatenate(
        [leading * cosine - trailing * sine_table, trailing * cosine + leading * sine_table],
        axis=-1,
    )


def attend(query_rows, key_rows, value_rows, length):
    row_count = query_rows.shape[0]
    scores = jnp.einsum(
        "qhd,khd->hqk", query_rows, key_rows, preferred_element_type=jnp.float32
    ) * query_rows.shape[2] ** (-0.5)
    positions = jnp.arange(row_count, dtype=jnp.int32)
    seen_keys = (positions[None, :] <= positions[:, None]) & (positions[None, :] < length)
    exp_scores = jnp.where(seen_keys[None], jnp.exp(scores), 0.0)
    attn_probs = (exp_scores / jnp.sum(exp_scores, axis=-1, keepdims=True)).astype(jnp.bfloat16)
    attended = jnp.einsum(
        "hqk,khd->qhd", attn_probs, value_rows, preferred_element_type=jnp.float32
    )
    live_rows = (positions < length)[:, None, None]
    return jnp.where(live_rows, attended, 0.0).astype(jnp.bfloat16)


def contract_rows(lhs, rhs_t):
    return lax.dot_general(
        lhs, rhs_t, (((1,), (1,)), ((), ())), preferred_element_type=jnp.float32
    )


def on_device(
    tokens,
    lengths,
    page_slot,
    w_query,
    w_keyval,
    w_out,
    w_gateup,
    w_down,
    attn_gain,
    ffn_gain,
    query_gain,
    key_gain,
):
    col_count = lax.axis_size("col")
    col_index = lax.axis_index("col")
    head_dim = query_gain.shape[0]
    local_width = w_query.shape[1]
    local_heads = local_width // head_dim
    kv_heads = w_keyval.shape[2] // head_dim
    group_size = local_heads * col_count // kv_heads
    assert group_size % local_heads == 0
    kv_head = (col_index * local_heads) // group_size
    unit_count = w_gateup.shape[2]
    kv_piece = lax.dynamic_slice_in_dim(w_keyval, kv_head * head_dim, head_dim, axis=2)
    pieces = [
        w_query.astype(jnp.bfloat16),
        jnp.transpose(kv_piece.astype(jnp.bfloat16), (1, 0, 2)).reshape(kv_piece.shape[1], -1),
        jnp.transpose(w_out.astype(jnp.bfloat16)),
        jnp.transpose(w_gateup.astype(jnp.bfloat16), (1, 0, 2)).reshape(w_gateup.shape[1], -1),
        jnp.transpose(w_down.astype(jnp.bfloat16)),
    ]
    widths = [p.shape[1] for p in pieces]
    packed = jnp.concatenate(pieces, axis=1)
    full = lax.all_gather(packed, ("row", "page"), axis=0, tiled=True)
    offsets = [sum(widths[:i]) for i in range(len(widths) + 1)]
    qkv_w = full[:, offsets[0] : offsets[2]]
    out_t = full[:, offsets[2] : offsets[3]]
    gateup_w = full[:, offsets[3] : offsets[4]]
    down_t = full[:, offsets[4] : offsets[5]]

    prompt_count, seq_len, local_feat = tokens.shape
    gathered = lax.all_gather(tokens, "col", axis=2, tiled=True)
    model_width = gathered.shape[2]
    attn_in = normalize(gathered.astype(jnp.float32), attn_gain).astype(jnp.bfloat16)
    projected = jnp.dot(
        attn_in.reshape(-1, model_width), qkv_w, preferred_element_type=jnp.float32
    )
    projected = projected.reshape(prompt_count, seq_len, local_heads + 2, head_dim)
    queries = rotate(normalize(projected[:, :, :local_heads], query_gain)).astype(jnp.bfloat16)
    keys_one = rotate(normalize(projected[:, :, local_heads : local_heads + 1], key_gain)).astype(
        jnp.bfloat16
    )
    values_one = projected[:, :, local_heads + 1 : local_heads + 2].astype(jnp.bfloat16)
    keys_rot = jnp.broadcast_to(keys_one, queries.shape)
    values_in = jnp.broadcast_to(values_one, queries.shape)
    attended = jnp.stack(
        [
            attend(queries[i], keys_rot[i], values_in[i], lengths[i]).reshape(seq_len, local_width)
            for i in range(prompt_count)
        ]
    )
    attn_terms = contract_rows(attended.reshape(-1, local_width), out_t)
    attn_terms = attn_terms.reshape(prompt_count, seq_len, model_width).astype(jnp.bfloat16)
    attn_sum = lax.psum(attn_terms, "col").astype(jnp.float32)
    residual_all = (gathered.astype(jnp.float32) + attn_sum).astype(jnp.bfloat16)
    residual = lax.dynamic_slice_in_dim(residual_all, col_index * local_feat, local_feat, axis=2)
    ffn_in = normalize(residual_all.astype(jnp.float32), ffn_gain).astype(jnp.bfloat16)
    gate_up = jnp.dot(
        ffn_in.reshape(-1, model_width), gateup_w, preferred_element_type=jnp.float32
    )
    hidden = (jax.nn.silu(gate_up[:, :unit_count]) * gate_up[:, unit_count:]).astype(jnp.bfloat16)
    ffn_terms = contract_rows(hidden, down_t).reshape(prompt_count, seq_len, model_width)
    ffn_sum = lax.psum_scatter(
        ffn_terms.astype(jnp.bfloat16), "col", scatter_dimension=2, tiled=True
    ).astype(jnp.float32)
    layer_out = (residual.astype(jnp.float32) + ffn_sum).astype(jnp.bfloat16)
    page_count = lax.axis_size("page")
    page_index = lax.axis_index("page")
    blocks_each = prompt_count * (seq_len // PAGE_LEN)
    capacity = blocks_each // page_count
    owners = page_slot // blocks_each
    local_slot = page_slot % blocks_each
    same_owner = owners[:, :, None] == owners[:, None, :]
    earlier = (
        jnp.arange(blocks_each, dtype=jnp.int32)[None, :]
        < jnp.arange(blocks_each, dtype=jnp.int32)[:, None]
    )
    order_in = jnp.sum((same_owner & earlier[None]).astype(jnp.int32), axis=2)
    my_owners = lax.dynamic_index_in_dim(owners, page_index, 0, keepdims=False)
    my_order = lax.dynamic_index_in_dim(order_in, page_index, 0, keepdims=False)
    send_pos = my_owners * capacity + my_order
    live_rows = (jnp.arange(seq_len, dtype=jnp.int32)[None, :] < lengths[:, None])[:, :, None, None]
    page_keys = jnp.where(live_rows, keys_rot, jnp.zeros_like(keys_rot)).reshape(
        blocks_each, PAGE_LEN, local_width
    )
    page_values = jnp.where(live_rows, values_in, jnp.zeros_like(values_in)).reshape(
        blocks_each, PAGE_LEN, local_width
    )
    stacked = jnp.stack([page_keys, page_values])
    outgoing = jnp.zeros_like(stacked).at[:, send_pos].set(stacked)
    incoming = lax.all_to_all(outgoing, "page", split_axis=1, concat_axis=1, tiled=True)
    arrival_hit = (owners[:, None, :] == page_index) & (
        order_in[:, None, :] == jnp.arange(capacity, dtype=jnp.int32)[None, :, None]
    )
    arrival_slot = jnp.sum(jnp.where(arrival_hit, local_slot[:, None, :], 0), axis=2).reshape(
        blocks_each
    )
    kv_pages = jnp.zeros_like(incoming).at[:, arrival_slot].set(incoming)
    return (layer_out, kv_pages)


def solution(mesh):
    in_specs = (
        P(("row", "page"), None, "col"),
        P(("row", "page")),
        P("row", None),
        P(("row", "page"), "col"),
        P(None, ("row", "page"), None),
        P("col", ("row", "page")),
        P(None, ("row", "page"), "col"),
        P("col", ("row", "page")),
        P(),
        P(),
        P(),
        P(),
    )
    out_specs = (P(("row", "page"), None, "col"), P(None, ("row", "page"), None, "col"))
    return jax.shard_map(
        on_device, mesh=mesh, in_specs=in_specs, out_specs=out_specs, check_vma=False
    )
```

```python
import jax
import jax.numpy as jnp
from jax import lax
from jax.sharding import PartitionSpec as P

PAGE_LEN = 128


def normalize(values, norm_gain):
    mean_sq = jnp.mean(values * values, axis=-1, keepdims=True)
    return values * lax.rsqrt(mean_sq + 1e-06) * norm_gain


def rotate(values):
    row_count = values.shape[-3]
    head_dim = values.shape[-1]
    half_dim = head_dim // 2
    frequency = 10000.0 ** (-2.0 * jnp.arange(half_dim, dtype=jnp.float32) / head_dim)
    angles = jnp.arange(row_count, dtype=jnp.float32)[:, None] * frequency[None, :]
    cosine = jnp.cos(angles)[:, None, :]
    sine_table = jnp.sin(angles)[:, None, :]
    leading = values[..., :half_dim]
    trailing = values[..., half_dim:]
    return jnp.concatenate(
        [leading * cosine - trailing * sine_table, trailing * cosine + leading * sine_table],
        axis=-1,
    )


def attend(query_rows, key_rows, value_rows, length):
    row_count = query_rows.shape[0]
    scores = jnp.einsum(
        "qhd,khd->hqk", query_rows, key_rows, preferred_element_type=jnp.float32
    ) * query_rows.shape[2] ** (-0.5)
    positions = jnp.arange(row_count, dtype=jnp.int32)
    seen_keys = (positions[None, :] <= positions[:, None]) & (positions[None, :] < length)
    exp_scores = jnp.where(seen_keys[None], jnp.exp(scores), 0.0)
    attn_probs = (exp_scores / jnp.sum(exp_scores, axis=-1, keepdims=True)).astype(jnp.bfloat16)
    attended = jnp.einsum(
        "hqk,khd->qhd", attn_probs, value_rows, preferred_element_type=jnp.float32
    )
    live_rows = (positions < length)[:, None, None]
    return jnp.where(live_rows, attended, 0.0).astype(jnp.bfloat16)


def contract_rows(lhs, rhs_t):
    return lax.dot_general(
        lhs, rhs_t, (((1,), (1,)), ((), ())), preferred_element_type=jnp.float32
    )


def gather_a2a(x, axis_name, axis):
    count = lax.axis_size(axis_name)
    copies = jnp.broadcast_to(x[None], (count,) + x.shape)
    got = lax.all_to_all(copies, axis_name, 0, 0, tiled=True)
    got = jnp.moveaxis(got, 0, axis)
    shape = list(x.shape)
    shape[axis] *= count
    return got.reshape(shape)


def scatter_sum_a2a(x, axis_name, axis):
    count = lax.axis_size(axis_name)
    shape = list(x.shape)
    split = shape[:axis] + [count, shape[axis] // count] + shape[axis + 1 :]
    got = lax.all_to_all(x.reshape(split), axis_name, axis, axis, tiled=True)
    return jnp.sum(got.astype(jnp.float32), axis=axis)


def on_device(
    tokens,
    lengths,
    page_slot,
    w_query,
    w_keyval,
    w_out,
    w_gateup,
    w_down,
    attn_gain,
    ffn_gain,
    query_gain,
    key_gain,
):
    col_count = lax.axis_size("col")
    col_index = lax.axis_index("col")
    head_dim = query_gain.shape[0]
    local_width = w_query.shape[1]
    local_heads = local_width // head_dim
    kv_heads = w_keyval.shape[2] // head_dim
    group_size = local_heads * col_count // kv_heads
    assert group_size % local_heads == 0
    kv_head = (col_index * local_heads) // group_size
    unit_count = w_gateup.shape[2]
    kv_piece = lax.dynamic_slice_in_dim(w_keyval, kv_head * head_dim, head_dim, axis=2)
    pieces = [
        w_query.astype(jnp.bfloat16),
        jnp.transpose(kv_piece.astype(jnp.bfloat16), (1, 0, 2)).reshape(kv_piece.shape[1], -1),
        jnp.transpose(w_out.astype(jnp.bfloat16)),
        jnp.transpose(w_gateup.astype(jnp.bfloat16), (1, 0, 2)).reshape(w_gateup.shape[1], -1),
        jnp.transpose(w_down.astype(jnp.bfloat16)),
    ]
    widths = [p.shape[1] for p in pieces]
    offsets = [sum(widths[:i]) for i in range(len(widths) + 1)]
    attn_full = lax.all_gather(jnp.concatenate(pieces[:3], axis=1), ("row", "page"), axis=0, tiled=True)
    ffn_full = lax.all_gather(jnp.concatenate(pieces[3:], axis=1), ("row", "page"), axis=0, tiled=True)
    qkv_w = attn_full[:, offsets[0] : offsets[2]]
    out_t = attn_full[:, offsets[2] : offsets[3]]
    gateup_w = ffn_full[:, : offsets[4] - offsets[3]]
    down_t = ffn_full[:, offsets[4] - offsets[3] :]

    prompt_count, seq_len, local_feat = tokens.shape
    gathered = gather_a2a(tokens, "col", 2)
    model_width = gathered.shape[2]
    attn_in = normalize(gathered.astype(jnp.float32), attn_gain).astype(jnp.bfloat16)
    projected = jnp.dot(
        attn_in.reshape(-1, model_width), qkv_w, preferred_element_type=jnp.float32
    )
    projected = projected.reshape(prompt_count, seq_len, local_heads + 2, head_dim)
    queries = rotate(normalize(projected[:, :, :local_heads], query_gain)).astype(jnp.bfloat16)
    keys_one = rotate(normalize(projected[:, :, local_heads : local_heads + 1], key_gain)).astype(
        jnp.bfloat16
    )
    values_one = projected[:, :, local_heads + 1 : local_heads + 2].astype(jnp.bfloat16)
    keys_rot = jnp.broadcast_to(keys_one, queries.shape)
    values_in = jnp.broadcast_to(values_one, queries.shape)
    attended = jnp.stack(
        [
            attend(queries[i], keys_rot[i], values_in[i], lengths[i]).reshape(seq_len, local_width)
            for i in range(prompt_count)
        ]
    )
    attn_terms = contract_rows(attended.reshape(-1, local_width), out_t)
    attn_terms = attn_terms.reshape(prompt_count, seq_len, model_width).astype(jnp.bfloat16)
    attn_sum = scatter_sum_a2a(attn_terms, "col", 2)
    residual = (tokens.astype(jnp.float32) + attn_sum).astype(jnp.bfloat16)
    residual_all = gather_a2a(residual, "col", 2)
    ffn_in = normalize(residual_all.astype(jnp.float32), ffn_gain).astype(jnp.bfloat16)
    gate_up = jnp.dot(
        ffn_in.reshape(-1, model_width), gateup_w, preferred_element_type=jnp.float32
    )
    hidden = (jax.nn.silu(gate_up[:, :unit_count]) * gate_up[:, unit_count:]).astype(jnp.bfloat16)
    ffn_terms = contract_rows(hidden, down_t).reshape(prompt_count, seq_len, model_width)
    ffn_sum = scatter_sum_a2a(ffn_terms.astype(jnp.bfloat16), "col", 2)
    layer_out = (residual.astype(jnp.float32) + ffn_sum).astype(jnp.bfloat16)
    page_count = lax.axis_size("page")
    page_index = lax.axis_index("page")
    blocks_each = prompt_count * (seq_len // PAGE_LEN)
    capacity = blocks_each // page_count
    owners = page_slot // blocks_each
    local_slot = page_slot % blocks_each
    same_owner = owners[:, :, None] == owners[:, None, :]
    earlier = (
        jnp.arange(blocks_each, dtype=jnp.int32)[None, :]
        < jnp.arange(blocks_each, dtype=jnp.int32)[:, None]
    )
    order_in = jnp.sum((same_owner & earlier[None]).astype(jnp.int32), axis=2)
    my_owners = lax.dynamic_index_in_dim(owners, page_index, 0, keepdims=False)
    my_order = lax.dynamic_index_in_dim(order_in, page_index, 0, keepdims=False)
    send_pos = my_owners * capacity + my_order
    live_rows = (jnp.arange(seq_len, dtype=jnp.int32)[None, :] < lengths[:, None])[:, :, None, None]
    page_keys = jnp.where(live_rows, keys_rot, jnp.zeros_like(keys_rot)).reshape(
        blocks_each, PAGE_LEN, local_width
    )
    page_values = jnp.where(live_rows, values_in, jnp.zeros_like(values_in)).reshape(
        blocks_each, PAGE_LEN, local_width
    )
    stacked = jnp.stack([page_keys, page_values])
    outgoing = jnp.zeros_like(stacked).at[:, send_pos].set(stacked)
    incoming = lax.all_to_all(outgoing, "page", split_axis=1, concat_axis=1, tiled=True)
    arrival_hit = (owners[:, None, :] == page_index) & (
        order_in[:, None, :] == jnp.arange(capacity, dtype=jnp.int32)[None, :, None]
    )
    arrival_slot = jnp.sum(jnp.where(arrival_hit, local_slot[:, None, :], 0), axis=2).reshape(
        blocks_each
    )
    kv_pages = jnp.zeros_like(incoming).at[:, arrival_slot].set(incoming)
    return (layer_out, kv_pages)


def solution(mesh):
    in_specs = (
        P(("row", "page"), None, "col"),
        P(("row", "page")),
        P("row", None),
        P(("row", "page"), "col"),
        P(None, ("row", "page"), None),
        P("col", ("row", "page")),
        P(None, ("row", "page"), "col"),
        P("col", ("row", "page")),
        P(),
        P(),
        P(),
        P(),
    )
    out_specs = (P(("row", "page"), None, "col"), P(None, ("row", "page"), None, "col"))
    return jax.shard_map(
        on_device, mesh=mesh, in_specs=in_specs, out_specs=out_specs, check_vma=False
    )
```

```python
import jax
import jax.numpy as jnp
from jax import lax
from jax.sharding import PartitionSpec as P

PAGE_LEN = 128


def normalize(values, norm_gain):
    mean_sq = jnp.mean(values * values, axis=-1, keepdims=True)
    return values * lax.rsqrt(mean_sq + 1e-06) * norm_gain


def rotate(values):
    row_count = values.shape[-3]
    head_dim = values.shape[-1]
    half_dim = head_dim // 2
    frequency = 10000.0 ** (-2.0 * jnp.arange(half_dim, dtype=jnp.float32) / head_dim)
    angles = jnp.arange(row_count, dtype=jnp.float32)[:, None] * frequency[None, :]
    cosine = jnp.cos(angles)[:, None, :]
    sine_table = jnp.sin(angles)[:, None, :]
    leading = values[..., :half_dim]
    trailing = values[..., half_dim:]
    return jnp.concatenate(
        [leading * cosine - trailing * sine_table, trailing * cosine + leading * sine_table],
        axis=-1,
    )


def attend(query_rows, key_rows, value_rows, length):
    row_count = query_rows.shape[0]
    scores = jnp.einsum(
        "qhd,khd->hqk", query_rows, key_rows, preferred_element_type=jnp.float32
    ) * query_rows.shape[2] ** (-0.5)
    positions = jnp.arange(row_count, dtype=jnp.int32)
    seen_keys = (positions[None, :] <= positions[:, None]) & (positions[None, :] < length)
    exp_scores = jnp.where(seen_keys[None], jnp.exp(scores), 0.0)
    attn_probs = (exp_scores / jnp.sum(exp_scores, axis=-1, keepdims=True)).astype(jnp.bfloat16)
    attended = jnp.einsum(
        "hqk,khd->qhd", attn_probs, value_rows, preferred_element_type=jnp.float32
    )
    live_rows = (positions < length)[:, None, None]
    return jnp.where(live_rows, attended, 0.0).astype(jnp.bfloat16)


def contract_rows(lhs, rhs_t):
    return lax.dot_general(
        lhs, rhs_t, (((1,), (1,)), ((), ())), preferred_element_type=jnp.float32
    )


def gather_a2a(x, axis_name, axis):
    count = lax.axis_size(axis_name)
    copies = jnp.broadcast_to(x[None], (count,) + x.shape)
    got = lax.all_to_all(copies, axis_name, 0, 0, tiled=True)
    got = jnp.moveaxis(got, 0, axis)
    shape = list(x.shape)
    shape[axis] *= count
    return got.reshape(shape)


def scatter_sum_a2a(x, axis_name, axis):
    count = lax.axis_size(axis_name)
    shape = list(x.shape)
    split = shape[:axis] + [count, shape[axis] // count] + shape[axis + 1 :]
    got = lax.all_to_all(x.reshape(split), axis_name, axis, axis, tiled=True)
    return jnp.sum(got.astype(jnp.float32), axis=axis)


def on_device(
    tokens,
    lengths,
    page_slot,
    w_query,
    w_keyval,
    w_out,
    w_gateup,
    w_down,
    attn_gain,
    ffn_gain,
    query_gain,
    key_gain,
):
    col_count = lax.axis_size("col")
    col_index = lax.axis_index("col")
    head_dim = query_gain.shape[0]
    local_width = w_query.shape[1]
    local_heads = local_width // head_dim
    kv_heads = w_keyval.shape[2] // head_dim
    group_size = local_heads * col_count // kv_heads
    assert group_size % local_heads == 0
    kv_head = (col_index * local_heads) // group_size
    unit_count = w_gateup.shape[2]
    kv_piece = lax.dynamic_slice_in_dim(w_keyval, kv_head * head_dim, head_dim, axis=2)
    pieces = [
        w_query.astype(jnp.bfloat16),
        jnp.transpose(kv_piece.astype(jnp.bfloat16), (1, 0, 2)).reshape(kv_piece.shape[1], -1),
        jnp.transpose(w_out.astype(jnp.bfloat16)),
        jnp.transpose(w_gateup.astype(jnp.bfloat16), (1, 0, 2)).reshape(w_gateup.shape[1], -1),
        jnp.transpose(w_down.astype(jnp.bfloat16)),
    ]
    widths = [p.shape[1] for p in pieces]
    offsets = [sum(widths[:i]) for i in range(len(widths) + 1)]
    full = lax.all_gather(jnp.concatenate(pieces, axis=1), ("row", "page"), axis=0, tiled=True)
    qkv_w = full[:, offsets[0] : offsets[2]]
    out_t = full[:, offsets[2] : offsets[3]]
    gateup_w = full[:, offsets[3] : offsets[4]]
    down_t = full[:, offsets[4] : offsets[5]]

    prompt_count, seq_len, local_feat = tokens.shape
    gathered = gather_a2a(tokens, "col", 2)
    model_width = gathered.shape[2]
    attn_in = normalize(gathered.astype(jnp.float32), attn_gain).astype(jnp.bfloat16)
    projected = jnp.dot(
        attn_in.reshape(-1, model_width), qkv_w, preferred_element_type=jnp.float32
    )
    projected = projected.reshape(prompt_count, seq_len, local_heads + 2, head_dim)
    queries = rotate(normalize(projected[:, :, :local_heads], query_gain)).astype(jnp.bfloat16)
    keys_one = rotate(normalize(projected[:, :, local_heads : local_heads + 1], key_gain)).astype(
        jnp.bfloat16
    )
    values_one = projected[:, :, local_heads + 1 : local_heads + 2].astype(jnp.bfloat16)
    keys_rot = jnp.broadcast_to(keys_one, queries.shape)
    values_in = jnp.broadcast_to(values_one, queries.shape)
    attended = jnp.stack(
        [
            attend(queries[i], keys_rot[i], values_in[i], lengths[i]).reshape(seq_len, local_width)
            for i in range(prompt_count)
        ]
    )
    attn_terms = contract_rows(attended.reshape(-1, local_width), out_t)
    attn_terms = attn_terms.reshape(prompt_count, seq_len, model_width).astype(jnp.bfloat16)
    attn_sum = scatter_sum_a2a(attn_terms, "col", 2)
    residual = (tokens.astype(jnp.float32) + attn_sum).astype(jnp.bfloat16)
    residual_all = gather_a2a(residual, "col", 2)
    ffn_in = normalize(residual_all.astype(jnp.float32), ffn_gain).astype(jnp.bfloat16)
    gate_up = jnp.dot(
        ffn_in.reshape(-1, model_width), gateup_w, preferred_element_type=jnp.float32
    )
    hidden = (jax.nn.silu(gate_up[:, :unit_count]) * gate_up[:, unit_count:]).astype(jnp.bfloat16)
    ffn_terms = contract_rows(hidden, down_t).reshape(prompt_count, seq_len, model_width)
    ffn_sum = scatter_sum_a2a(ffn_terms.astype(jnp.bfloat16), "col", 2)
    layer_out = (residual.astype(jnp.float32) + ffn_sum).astype(jnp.bfloat16)
    page_count = lax.axis_size("page")
    page_index = lax.axis_index("page")
    blocks_each = prompt_count * (seq_len // PAGE_LEN)
    capacity = blocks_each // page_count
    owners = page_slot // blocks_each
    local_slot = page_slot % blocks_each
    same_owner = owners[:, :, None] == owners[:, None, :]
    earlier = (
        jnp.arange(blocks_each, dtype=jnp.int32)[None, :]
        < jnp.arange(blocks_each, dtype=jnp.int32)[:, None]
    )
    order_in = jnp.sum((same_owner & earlier[None]).astype(jnp.int32), axis=2)
    my_owners = lax.dynamic_index_in_dim(owners, page_index, 0, keepdims=False)
    my_order = lax.dynamic_index_in_dim(order_in, page_index, 0, keepdims=False)
    send_pos = my_owners * capacity + my_order
    live_rows = (jnp.arange(seq_len, dtype=jnp.int32)[None, :] < lengths[:, None])[:, :, None, None]
    page_keys = jnp.where(live_rows, keys_rot, jnp.zeros_like(keys_rot)).reshape(
        blocks_each, PAGE_LEN, local_width
    )
    page_values = jnp.where(live_rows, values_in, jnp.zeros_like(values_in)).reshape(
        blocks_each, PAGE_LEN, local_width
    )
    stacked = jnp.stack([page_keys, page_values])
    outgoing = jnp.zeros_like(stacked).at[:, send_pos].set(stacked)
    incoming = lax.all_to_all(outgoing, "page", split_axis=1, concat_axis=1, tiled=True)
    arrival_hit = (owners[:, None, :] == page_index) & (
        order_in[:, None, :] == jnp.arange(capacity, dtype=jnp.int32)[None, :, None]
    )
    arrival_slot = jnp.sum(jnp.where(arrival_hit, local_slot[:, None, :], 0), axis=2).reshape(
        blocks_each
    )
    kv_pages = jnp.zeros_like(incoming).at[:, arrival_slot].set(incoming)
    return (layer_out, kv_pages)


def solution(mesh):
    in_specs = (
        P(("row", "page"), None, "col"),
        P(("row", "page")),
        P("row", None),
        P(("row", "page"), "col"),
        P(None, ("row", "page"), None),
        P("col", ("row", "page")),
        P(None, ("row", "page"), "col"),
        P("col", ("row", "page")),
        P(),
        P(),
        P(),
        P(),
    )
    out_specs = (P(("row", "page"), None, "col"), P(None, ("row", "page"), None, "col"))
    return jax.shard_map(
        on_device, mesh=mesh, in_specs=in_specs, out_specs=out_specs, check_vma=False
    )
```

```python
import jax
import jax.numpy as jnp
from jax import lax
from jax.sharding import Mesh, PartitionSpec as P

PAGE_LEN = 128
ROW = ("ry", "rc")
COL = ("zh", "xx")
ROWPAGE = ("ry", "rc", "page")


def normalize(values, norm_gain):
    mean_sq = jnp.mean(values * values, axis=-1, keepdims=True)
    return values * lax.rsqrt(mean_sq + 1e-06) * norm_gain


def rotate(values):
    row_count = values.shape[-3]
    head_dim = values.shape[-1]
    half_dim = head_dim // 2
    frequency = 10000.0 ** (-2.0 * jnp.arange(half_dim, dtype=jnp.float32) / head_dim)
    angles = jnp.arange(row_count, dtype=jnp.float32)[:, None] * frequency[None, :]
    cosine = jnp.cos(angles)[:, None, :]
    sine_table = jnp.sin(angles)[:, None, :]
    leading = values[..., :half_dim]
    trailing = values[..., half_dim:]
    return jnp.concatenate(
        [leading * cosine - trailing * sine_table, trailing * cosine + leading * sine_table],
        axis=-1,
    )


def attend(query_rows, key_rows, value_rows, length):
    row_count = query_rows.shape[0]
    scores = jnp.einsum(
        "qhd,khd->hqk", query_rows, key_rows, preferred_element_type=jnp.float32
    ) * query_rows.shape[2] ** (-0.5)
    positions = jnp.arange(row_count, dtype=jnp.int32)
    seen_keys = (positions[None, :] <= positions[:, None]) & (positions[None, :] < length)
    exp_scores = jnp.where(seen_keys[None], jnp.exp(scores), 0.0)
    attn_probs = (exp_scores / jnp.sum(exp_scores, axis=-1, keepdims=True)).astype(jnp.bfloat16)
    attended = jnp.einsum(
        "hqk,khd->qhd", attn_probs, value_rows, preferred_element_type=jnp.float32
    )
    live_rows = (positions < length)[:, None, None]
    return jnp.where(live_rows, attended, 0.0).astype(jnp.bfloat16)


def contract_rows(lhs, rhs_t):
    return lax.dot_general(
        lhs, rhs_t, (((1,), (1,)), ((), ())), preferred_element_type=jnp.float32
    )


def gather_a2a(x, axis_name, axis):
    count = lax.axis_size(axis_name)
    copies = jnp.broadcast_to(x[None], (count,) + x.shape)
    got = lax.all_to_all(copies, axis_name, 0, 0, tiled=True)
    got = jnp.moveaxis(got, 0, axis)
    shape = list(x.shape)
    shape[axis] *= count
    return got.reshape(shape)


def scatter_sum_a2a(x, axis_name, axis):
    count = lax.axis_size(axis_name)
    shape = list(x.shape)
    split = shape[:axis] + [count, shape[axis] // count] + shape[axis + 1 :]
    got = lax.all_to_all(x.reshape(split), axis_name, axis, axis, tiled=True)
    return jnp.sum(got.astype(jnp.float32), axis=axis)


def on_device(
    tokens,
    lengths,
    page_slot,
    w_query,
    w_keyval,
    w_out,
    w_gateup,
    w_down,
    attn_gain,
    ffn_gain,
    query_gain,
    key_gain,
):
    col_count = lax.axis_size(COL)
    col_index = lax.axis_index(COL)
    head_dim = query_gain.shape[0]
    local_width = w_query.shape[1]
    local_heads = local_width // head_dim
    kv_heads = w_keyval.shape[2] // head_dim
    group_size = local_heads * col_count // kv_heads
    assert group_size % local_heads == 0
    kv_head = (col_index * local_heads) // group_size
    unit_count = w_gateup.shape[2]
    kv_piece = lax.dynamic_slice_in_dim(w_keyval, kv_head * head_dim, head_dim, axis=2)
    pieces = [
        w_query.astype(jnp.bfloat16),
        jnp.transpose(kv_piece.astype(jnp.bfloat16), (1, 0, 2)).reshape(kv_piece.shape[1], -1),
        jnp.transpose(w_out.astype(jnp.bfloat16)),
        jnp.transpose(w_gateup.astype(jnp.bfloat16), (1, 0, 2)).reshape(w_gateup.shape[1], -1),
        jnp.transpose(w_down.astype(jnp.bfloat16)),
    ]
    widths = [p.shape[1] for p in pieces]
    offsets = [sum(widths[:i]) for i in range(len(widths) + 1)]
    across = lax.all_gather(jnp.concatenate(pieces, axis=1), ("ry", "page"), axis=0, tiled=True)
    chips = lax.axis_size("ry")
    across = across.reshape(chips, -1, across.shape[1])
    full = lax.all_gather(across, "rc", axis=1, tiled=True).reshape(-1, across.shape[2])
    qkv_w = full[:, offsets[0] : offsets[2]]
    out_t = full[:, offsets[2] : offsets[3]]
    gateup_w = full[:, offsets[3] : offsets[4]]
    down_t = full[:, offsets[4] : offsets[5]]

    prompt_count, seq_len, local_feat = tokens.shape
    gathered = gather_a2a(tokens, COL, 2)
    model_width = gathered.shape[2]
    attn_in = normalize(gathered.astype(jnp.float32), attn_gain).astype(jnp.bfloat16)
    projected = jnp.dot(
        attn_in.reshape(-1, model_width), qkv_w, preferred_element_type=jnp.float32
    )
    projected = projected.reshape(prompt_count, seq_len, local_heads + 2, head_dim)
    queries = rotate(normalize(projected[:, :, :local_heads], query_gain)).astype(jnp.bfloat16)
    keys_one = rotate(normalize(projected[:, :, local_heads : local_heads + 1], key_gain)).astype(
        jnp.bfloat16
    )
    values_one = projected[:, :, local_heads + 1 : local_heads + 2].astype(jnp.bfloat16)
    keys_rot = jnp.broadcast_to(keys_one, queries.shape)
    values_in = jnp.broadcast_to(values_one, queries.shape)
    attended = jnp.stack(
        [
            attend(queries[i], keys_rot[i], values_in[i], lengths[i]).reshape(seq_len, local_width)
            for i in range(prompt_count)
        ]
    )
    attn_terms = contract_rows(attended.reshape(-1, local_width), out_t)
    attn_terms = attn_terms.reshape(prompt_count, seq_len, model_width).astype(jnp.bfloat16)
    attn_sum = scatter_sum_a2a(attn_terms, COL, 2)
    residual = (tokens.astype(jnp.float32) + attn_sum).astype(jnp.bfloat16)
    residual_all = gather_a2a(residual, COL, 2)
    ffn_in = normalize(residual_all.astype(jnp.float32), ffn_gain).astype(jnp.bfloat16)
    gate_up = jnp.dot(
        ffn_in.reshape(-1, model_width), gateup_w, preferred_element_type=jnp.float32
    )
    hidden = (jax.nn.silu(gate_up[:, :unit_count]) * gate_up[:, unit_count:]).astype(jnp.bfloat16)
    ffn_terms = contract_rows(hidden, down_t).reshape(prompt_count, seq_len, model_width)
    ffn_sum = scatter_sum_a2a(ffn_terms.astype(jnp.bfloat16), COL, 2)
    layer_out = (residual.astype(jnp.float32) + ffn_sum).astype(jnp.bfloat16)
    page_count = lax.axis_size("page")
    page_index = lax.axis_index("page")
    blocks_each = prompt_count * (seq_len // PAGE_LEN)
    capacity = blocks_each // page_count
    owners = page_slot // blocks_each
    local_slot = page_slot % blocks_each
    same_owner = owners[:, :, None] == owners[:, None, :]
    earlier = (
        jnp.arange(blocks_each, dtype=jnp.int32)[None, :]
        < jnp.arange(blocks_each, dtype=jnp.int32)[:, None]
    )
    order_in = jnp.sum((same_owner & earlier[None]).astype(jnp.int32), axis=2)
    my_owners = lax.dynamic_index_in_dim(owners, page_index, 0, keepdims=False)
    my_order = lax.dynamic_index_in_dim(order_in, page_index, 0, keepdims=False)
    send_pos = my_owners * capacity + my_order
    live_rows = (jnp.arange(seq_len, dtype=jnp.int32)[None, :] < lengths[:, None])[:, :, None, None]
    page_keys = jnp.where(live_rows, keys_rot, jnp.zeros_like(keys_rot)).reshape(
        blocks_each, PAGE_LEN, local_width
    )
    page_values = jnp.where(live_rows, values_in, jnp.zeros_like(values_in)).reshape(
        blocks_each, PAGE_LEN, local_width
    )
    stacked = jnp.stack([page_keys, page_values])
    outgoing = jnp.zeros_like(stacked).at[:, send_pos].set(stacked)
    incoming = lax.all_to_all(outgoing, "page", split_axis=1, concat_axis=1, tiled=True)
    arrival_hit = (owners[:, None, :] == page_index) & (
        order_in[:, None, :] == jnp.arange(capacity, dtype=jnp.int32)[None, :, None]
    )
    arrival_slot = jnp.sum(jnp.where(arrival_hit, local_slot[:, None, :], 0), axis=2).reshape(
        blocks_each
    )
    kv_pages = jnp.zeros_like(incoming).at[:, arrival_slot].set(incoming)
    return (layer_out, kv_pages)


def solution(mesh):
    in_specs = (
        P(ROWPAGE, None, COL),
        P(ROWPAGE),
        P(ROW, None),
        P(ROWPAGE, COL),
        P(None, ROWPAGE, None),
        P(COL, ROWPAGE),
        P(None, ROWPAGE, COL),
        P(COL, ROWPAGE),
        P(),
        P(),
        P(),
        P(),
    )
    out_specs = (P(ROWPAGE, None, COL), P(None, ROWPAGE, None, COL))
    fine = Mesh(
        mesh.devices.reshape(
            mesh.shape["row"] // 2, 2, 2, mesh.shape["col"] // 2, mesh.shape["page"]
        ),
        ("ry", "rc", "zh", "xx", "page"),
    )
    return jax.shard_map(
        on_device, mesh=fine, in_specs=in_specs, out_specs=out_specs, check_vma=False
    )
```

```python
import jax
import jax.numpy as jnp
from jax import lax
from jax.sharding import Mesh, PartitionSpec as P

PAGE_LEN = 128
ROW = ("ry", "rc")
COL = ("zh", "xx")
ROWPAGE = ("ry", "rc", "page")


def normalize(values, norm_gain):
    mean_sq = jnp.mean(values * values, axis=-1, keepdims=True)
    return values * lax.rsqrt(mean_sq + 1e-06) * norm_gain


def rotate(values):
    row_count = values.shape[-3]
    head_dim = values.shape[-1]
    half_dim = head_dim // 2
    frequency = 10000.0 ** (-2.0 * jnp.arange(half_dim, dtype=jnp.float32) / head_dim)
    angles = jnp.arange(row_count, dtype=jnp.float32)[:, None] * frequency[None, :]
    cosine = jnp.cos(angles)[:, None, :]
    sine_table = jnp.sin(angles)[:, None, :]
    leading = values[..., :half_dim]
    trailing = values[..., half_dim:]
    return jnp.concatenate(
        [leading * cosine - trailing * sine_table, trailing * cosine + leading * sine_table],
        axis=-1,
    )


def attend(query_rows, key_rows, value_rows, length):
    row_count = query_rows.shape[0]
    scores = jnp.einsum(
        "qhd,khd->hqk", query_rows, key_rows, preferred_element_type=jnp.float32
    ) * query_rows.shape[2] ** (-0.5)
    positions = jnp.arange(row_count, dtype=jnp.int32)
    seen_keys = (positions[None, :] <= positions[:, None]) & (positions[None, :] < length)
    exp_scores = jnp.where(seen_keys[None], jnp.exp(scores), 0.0)
    attn_probs = (exp_scores / jnp.sum(exp_scores, axis=-1, keepdims=True)).astype(jnp.bfloat16)
    attended = jnp.einsum(
        "hqk,khd->qhd", attn_probs, value_rows, preferred_element_type=jnp.float32
    )
    live_rows = (positions < length)[:, None, None]
    return jnp.where(live_rows, attended, 0.0).astype(jnp.bfloat16)


def contract_rows(lhs, rhs_t):
    return lax.dot_general(
        lhs, rhs_t, (((1,), (1,)), ((), ())), preferred_element_type=jnp.float32
    )


def gather_a2a(x, axis_name, axis):
    count = lax.axis_size(axis_name)
    copies = jnp.broadcast_to(x[None], (count,) + x.shape)
    got = lax.all_to_all(copies, axis_name, 0, 0, tiled=True)
    got = jnp.moveaxis(got, 0, axis)
    shape = list(x.shape)
    shape[axis] *= count
    return got.reshape(shape)


def scatter_sum_a2a(x, axis_name, axis):
    count = lax.axis_size(axis_name)
    shape = list(x.shape)
    split = shape[:axis] + [count, shape[axis] // count] + shape[axis + 1 :]
    got = lax.all_to_all(x.reshape(split), axis_name, axis, axis, tiled=True)
    return jnp.sum(got.astype(jnp.float32), axis=axis)


def swap_halves(x):
    return lax.ppermute(x, "zh", [(0, 1), (1, 0)])


def gather_col(x, axis):
    half = lax.axis_index("zh")
    other = swap_halves(x)
    pair = jnp.stack([jnp.where(half == 0, x, other), jnp.where(half == 0, other, x)])
    count = lax.axis_size("xx")
    copies = jnp.broadcast_to(pair[None], (count,) + pair.shape)
    got = lax.all_to_all(copies, "xx", 0, 0, tiled=True)
    got = jnp.moveaxis(jnp.swapaxes(got, 0, 1).reshape((-1,) + x.shape), 0, axis)
    shape = list(x.shape)
    shape[axis] *= 2 * count
    return got.reshape(shape)


def scatter_sum_col(x, axis):
    count = lax.axis_size("xx")
    shape = list(x.shape)
    split = shape[:axis] + [2, count, shape[axis] // (2 * count)] + shape[axis + 1 :]
    got = lax.all_to_all(x.reshape(split), "xx", axis + 1, axis + 1, tiled=True)
    part = jnp.sum(got.astype(jnp.float32), axis=axis + 1)
    half = lax.axis_index("zh")
    mine = jnp.take(part, half, axis=axis)
    theirs = swap_halves(jnp.take(part, 1 - half, axis=axis))
    return mine + theirs


def on_device(
    tokens,
    lengths,
    page_slot,
    w_query,
    w_keyval,
    w_out,
    w_gateup,
    w_down,
    attn_gain,
    ffn_gain,
    query_gain,
    key_gain,
):
    col_count = lax.axis_size(COL)
    col_index = lax.axis_index(COL)
    head_dim = query_gain.shape[0]
    local_width = w_query.shape[1]
    local_heads = local_width // head_dim
    kv_heads = w_keyval.shape[2] // head_dim
    group_size = local_heads * col_count // kv_heads
    assert group_size % local_heads == 0
    kv_head = (col_index * local_heads) // group_size
    unit_count = w_gateup.shape[2]
    kv_piece = lax.dynamic_slice_in_dim(w_keyval, kv_head * head_dim, head_dim, axis=2)
    pieces = [
        w_query.astype(jnp.bfloat16),
        jnp.transpose(kv_piece.astype(jnp.bfloat16), (1, 0, 2)).reshape(kv_piece.shape[1], -1),
        jnp.transpose(w_out.astype(jnp.bfloat16)),
        jnp.transpose(w_gateup.astype(jnp.bfloat16), (1, 0, 2)).reshape(w_gateup.shape[1], -1),
        jnp.transpose(w_down.astype(jnp.bfloat16)),
    ]
    widths = [p.shape[1] for p in pieces]
    offsets = [sum(widths[:i]) for i in range(len(widths) + 1)]
    full = lax.all_gather(jnp.concatenate(pieces, axis=1), ROWPAGE, axis=0, tiled=True)
    qkv_w = full[:, offsets[0] : offsets[2]]
    out_t = full[:, offsets[2] : offsets[3]]
    gateup_w = full[:, offsets[3] : offsets[4]]
    down_t = full[:, offsets[4] : offsets[5]]

    prompt_count, seq_len, local_feat = tokens.shape
    gathered = gather_col(tokens, 2)
    model_width = gathered.shape[2]
    attn_in = normalize(gathered.astype(jnp.float32), attn_gain).astype(jnp.bfloat16)
    projected = jnp.dot(
        attn_in.reshape(-1, model_width), qkv_w, preferred_element_type=jnp.float32
    )
    projected = projected.reshape(prompt_count, seq_len, local_heads + 2, head_dim)
    queries = rotate(normalize(projected[:, :, :local_heads], query_gain)).astype(jnp.bfloat16)
    keys_one = rotate(normalize(projected[:, :, local_heads : local_heads + 1], key_gain)).astype(
        jnp.bfloat16
    )
    values_one = projected[:, :, local_heads + 1 : local_heads + 2].astype(jnp.bfloat16)
    keys_rot = jnp.broadcast_to(keys_one, queries.shape)
    values_in = jnp.broadcast_to(values_one, queries.shape)
    attended = jnp.stack(
        [
            attend(queries[i], keys_rot[i], values_in[i], lengths[i]).reshape(seq_len, local_width)
            for i in range(prompt_count)
        ]
    )
    attn_terms = contract_rows(attended.reshape(-1, local_width), out_t)
    attn_terms = attn_terms.reshape(prompt_count, seq_len, model_width).astype(jnp.bfloat16)
    attn_sum = scatter_sum_col(attn_terms, 2)
    residual = (tokens.astype(jnp.float32) + attn_sum).astype(jnp.bfloat16)
    residual_all = gather_col(residual, 2)
    ffn_in = normalize(residual_all.astype(jnp.float32), ffn_gain).astype(jnp.bfloat16)
    gate_up = jnp.dot(
        ffn_in.reshape(-1, model_width), gateup_w, preferred_element_type=jnp.float32
    )
    hidden = (jax.nn.silu(gate_up[:, :unit_count]) * gate_up[:, unit_count:]).astype(jnp.bfloat16)
    ffn_terms = contract_rows(hidden, down_t).reshape(prompt_count, seq_len, model_width)
    ffn_sum = scatter_sum_col(ffn_terms.astype(jnp.bfloat16), 2)
    layer_out = (residual.astype(jnp.float32) + ffn_sum).astype(jnp.bfloat16)
    page_count = lax.axis_size("page")
    page_index = lax.axis_index("page")
    blocks_each = prompt_count * (seq_len // PAGE_LEN)
    capacity = blocks_each // page_count
    owners = page_slot // blocks_each
    local_slot = page_slot % blocks_each
    same_owner = owners[:, :, None] == owners[:, None, :]
    earlier = (
        jnp.arange(blocks_each, dtype=jnp.int32)[None, :]
        < jnp.arange(blocks_each, dtype=jnp.int32)[:, None]
    )
    order_in = jnp.sum((same_owner & earlier[None]).astype(jnp.int32), axis=2)
    my_owners = lax.dynamic_index_in_dim(owners, page_index, 0, keepdims=False)
    my_order = lax.dynamic_index_in_dim(order_in, page_index, 0, keepdims=False)
    send_pos = my_owners * capacity + my_order
    live_rows = (jnp.arange(seq_len, dtype=jnp.int32)[None, :] < lengths[:, None])[:, :, None, None]
    page_keys = jnp.where(live_rows, keys_rot, jnp.zeros_like(keys_rot)).reshape(
        blocks_each, PAGE_LEN, local_width
    )
    page_values = jnp.where(live_rows, values_in, jnp.zeros_like(values_in)).reshape(
        blocks_each, PAGE_LEN, local_width
    )
    stacked = jnp.stack([page_keys, page_values])
    outgoing = jnp.zeros_like(stacked).at[:, send_pos].set(stacked)
    incoming = lax.all_to_all(outgoing, "page", split_axis=1, concat_axis=1, tiled=True)
    arrival_hit = (owners[:, None, :] == page_index) & (
        order_in[:, None, :] == jnp.arange(capacity, dtype=jnp.int32)[None, :, None]
    )
    arrival_slot = jnp.sum(jnp.where(arrival_hit, local_slot[:, None, :], 0), axis=2).reshape(
        blocks_each
    )
    kv_pages = jnp.zeros_like(incoming).at[:, arrival_slot].set(incoming)
    return (layer_out, kv_pages)


def solution(mesh):
    in_specs = (
        P(ROWPAGE, None, COL),
        P(ROWPAGE),
        P(ROW, None),
        P(ROWPAGE, COL),
        P(None, ROWPAGE, None),
        P(COL, ROWPAGE),
        P(None, ROWPAGE, COL),
        P(COL, ROWPAGE),
        P(),
        P(),
        P(),
        P(),
    )
    out_specs = (P(ROWPAGE, None, COL), P(None, ROWPAGE, None, COL))
    fine = Mesh(
        mesh.devices.reshape(
            mesh.shape["row"] // 2, 2, 2, mesh.shape["col"] // 2, mesh.shape["page"]
        ),
        ("ry", "rc", "zh", "xx", "page"),
    )
    return jax.shard_map(
        on_device, mesh=fine, in_specs=in_specs, out_specs=out_specs, check_vma=False
    )
```

```python
import jax
import jax.numpy as jnp
from jax import lax
from jax.sharding import Mesh, PartitionSpec as P

PAGE_LEN = 128
ROW = ("ry", "rc")
COL = ("zh", "xx")
ROWPAGE = ("ry", "rc", "page")


def normalize(values, norm_gain):
    mean_sq = jnp.mean(values * values, axis=-1, keepdims=True)
    return values * lax.rsqrt(mean_sq + 1e-06) * norm_gain


def rotate(values):
    row_count = values.shape[-3]
    head_dim = values.shape[-1]
    half_dim = head_dim // 2
    frequency = 10000.0 ** (-2.0 * jnp.arange(half_dim, dtype=jnp.float32) / head_dim)
    angles = jnp.arange(row_count, dtype=jnp.float32)[:, None] * frequency[None, :]
    cosine = jnp.cos(angles)[:, None, :]
    sine_table = jnp.sin(angles)[:, None, :]
    leading = values[..., :half_dim]
    trailing = values[..., half_dim:]
    return jnp.concatenate(
        [leading * cosine - trailing * sine_table, trailing * cosine + leading * sine_table],
        axis=-1,
    )


def attend(query_rows, key_rows, value_rows, length):
    row_count = query_rows.shape[0]
    scores = jnp.einsum(
        "qhd,khd->hqk", query_rows, key_rows, preferred_element_type=jnp.float32
    ) * query_rows.shape[2] ** (-0.5)
    positions = jnp.arange(row_count, dtype=jnp.int32)
    seen_keys = (positions[None, :] <= positions[:, None]) & (positions[None, :] < length)
    exp_scores = jnp.where(seen_keys[None], jnp.exp(scores), 0.0)
    attn_probs = (exp_scores / jnp.sum(exp_scores, axis=-1, keepdims=True)).astype(jnp.bfloat16)
    attended = jnp.einsum(
        "hqk,khd->qhd", attn_probs, value_rows, preferred_element_type=jnp.float32
    )
    live_rows = (positions < length)[:, None, None]
    return jnp.where(live_rows, attended, 0.0).astype(jnp.bfloat16)


def contract_rows(lhs, rhs_t):
    return lax.dot_general(
        lhs, rhs_t, (((1,), (1,)), ((), ())), preferred_element_type=jnp.float32
    )


def gather_a2a(x, axis_name, axis):
    count = lax.axis_size(axis_name)
    copies = jnp.broadcast_to(x[None], (count,) + x.shape)
    got = lax.all_to_all(copies, axis_name, 0, 0, tiled=True)
    got = jnp.moveaxis(got, 0, axis)
    shape = list(x.shape)
    shape[axis] *= count
    return got.reshape(shape)


def scatter_sum_a2a(x, axis_name, axis):
    count = lax.axis_size(axis_name)
    shape = list(x.shape)
    split = shape[:axis] + [count, shape[axis] // count] + shape[axis + 1 :]
    got = lax.all_to_all(x.reshape(split), axis_name, axis, axis, tiled=True)
    return jnp.sum(got.astype(jnp.float32), axis=axis)


def swap_halves(x):
    return lax.ppermute(x, "zh", [(0, 1), (1, 0)])


def gather_col(x, axis):
    half = lax.axis_index("zh")
    other = swap_halves(x)
    pair = jnp.stack([jnp.where(half == 0, x, other), jnp.where(half == 0, other, x)])
    count = lax.axis_size("xx")
    copies = jnp.broadcast_to(pair[None], (count,) + pair.shape)
    got = lax.all_to_all(copies, "xx", 0, 0, tiled=True)
    got = jnp.moveaxis(jnp.swapaxes(got, 0, 1).reshape((-1,) + x.shape), 0, axis)
    shape = list(x.shape)
    shape[axis] *= 2 * count
    return got.reshape(shape)


def scatter_sum_col(x, axis):
    count = lax.axis_size("xx")
    shape = list(x.shape)
    split = shape[:axis] + [2, count, shape[axis] // (2 * count)] + shape[axis + 1 :]
    got = lax.all_to_all(x.reshape(split), "xx", axis + 1, axis + 1, tiled=True)
    part = jnp.sum(got.astype(jnp.float32), axis=axis + 1)
    half = lax.axis_index("zh")
    mine = jnp.take(part, half, axis=axis)
    theirs = swap_halves(jnp.take(part, 1 - half, axis=axis))
    return mine + theirs


def gather_rows(x):
    pages = lax.axis_size("page")
    got = lax.all_to_all(jnp.broadcast_to(x[None], (pages,) + x.shape), "page", 0, 0, tiled=True)
    got = got.reshape((-1,) + x.shape[1:])
    chips = lax.axis_size("ry")
    got = lax.all_to_all(jnp.broadcast_to(got[None], (chips,) + got.shape), "ry", 0, 0, tiled=True)
    cores = lax.axis_size("rc")
    got = jnp.broadcast_to(got[:, None], (chips, cores) + got.shape[1:])
    got = lax.all_to_all(got, "rc", 1, 1, tiled=True)
    return got.reshape((-1,) + x.shape[1:])


def on_device(
    tokens,
    lengths,
    page_slot,
    w_query,
    w_keyval,
    w_out,
    w_gateup,
    w_down,
    attn_gain,
    ffn_gain,
    query_gain,
    key_gain,
):
    col_count = lax.axis_size(COL)
    col_index = lax.axis_index(COL)
    head_dim = query_gain.shape[0]
    local_width = w_query.shape[1]
    local_heads = local_width // head_dim
    kv_heads = w_keyval.shape[2] // head_dim
    group_size = local_heads * col_count // kv_heads
    assert group_size % local_heads == 0
    kv_head = (col_index * local_heads) // group_size
    unit_count = w_gateup.shape[2]
    kv_piece = lax.dynamic_slice_in_dim(w_keyval, kv_head * head_dim, head_dim, axis=2)
    pieces = [
        w_query.astype(jnp.bfloat16),
        jnp.transpose(kv_piece.astype(jnp.bfloat16), (1, 0, 2)).reshape(kv_piece.shape[1], -1),
        jnp.transpose(w_out.astype(jnp.bfloat16)),
        jnp.transpose(w_gateup.astype(jnp.bfloat16), (1, 0, 2)).reshape(w_gateup.shape[1], -1),
        jnp.transpose(w_down.astype(jnp.bfloat16)),
    ]
    widths = [p.shape[1] for p in pieces]
    offsets = [sum(widths[:i]) for i in range(len(widths) + 1)]
    full = gather_rows(jnp.concatenate(pieces, axis=1))
    qkv_w = full[:, offsets[0] : offsets[2]]
    out_t = full[:, offsets[2] : offsets[3]]
    gateup_w = full[:, offsets[3] : offsets[4]]
    down_t = full[:, offsets[4] : offsets[5]]

    prompt_count, seq_len, local_feat = tokens.shape
    gathered = gather_col(tokens, 2)
    model_width = gathered.shape[2]
    attn_in = normalize(gathered.astype(jnp.float32), attn_gain).astype(jnp.bfloat16)
    projected = jnp.dot(
        attn_in.reshape(-1, model_width), qkv_w, preferred_element_type=jnp.float32
    )
    projected = projected.reshape(prompt_count, seq_len, local_heads + 2, head_dim)
    queries = rotate(normalize(projected[:, :, :local_heads], query_gain)).astype(jnp.bfloat16)
    keys_one = rotate(normalize(projected[:, :, local_heads : local_heads + 1], key_gain)).astype(
        jnp.bfloat16
    )
    values_one = projected[:, :, local_heads + 1 : local_heads + 2].astype(jnp.bfloat16)
    keys_rot = jnp.broadcast_to(keys_one, queries.shape)
    values_in = jnp.broadcast_to(values_one, queries.shape)
    attended = jnp.stack(
        [
            attend(queries[i], keys_rot[i], values_in[i], lengths[i]).reshape(seq_len, local_width)
            for i in range(prompt_count)
        ]
    )
    attn_terms = contract_rows(attended.reshape(-1, local_width), out_t)
    attn_terms = attn_terms.reshape(prompt_count, seq_len, model_width).astype(jnp.bfloat16)
    attn_sum = scatter_sum_col(attn_terms, 2)
    residual = (tokens.astype(jnp.float32) + attn_sum).astype(jnp.bfloat16)
    residual_all = gather_col(residual, 2)
    ffn_in = normalize(residual_all.astype(jnp.float32), ffn_gain).astype(jnp.bfloat16)
    gate_up = jnp.dot(
        ffn_in.reshape(-1, model_width), gateup_w, preferred_element_type=jnp.float32
    )
    hidden = (jax.nn.silu(gate_up[:, :unit_count]) * gate_up[:, unit_count:]).astype(jnp.bfloat16)
    ffn_terms = contract_rows(hidden, down_t).reshape(prompt_count, seq_len, model_width)
    ffn_sum = scatter_sum_col(ffn_terms.astype(jnp.bfloat16), 2)
    layer_out = (residual.astype(jnp.float32) + ffn_sum).astype(jnp.bfloat16)
    page_count = lax.axis_size("page")
    page_index = lax.axis_index("page")
    blocks_each = prompt_count * (seq_len // PAGE_LEN)
    capacity = blocks_each // page_count
    owners = page_slot // blocks_each
    local_slot = page_slot % blocks_each
    same_owner = owners[:, :, None] == owners[:, None, :]
    earlier = (
        jnp.arange(blocks_each, dtype=jnp.int32)[None, :]
        < jnp.arange(blocks_each, dtype=jnp.int32)[:, None]
    )
    order_in = jnp.sum((same_owner & earlier[None]).astype(jnp.int32), axis=2)
    my_owners = lax.dynamic_index_in_dim(owners, page_index, 0, keepdims=False)
    my_order = lax.dynamic_index_in_dim(order_in, page_index, 0, keepdims=False)
    send_pos = my_owners * capacity + my_order
    live_rows = (jnp.arange(seq_len, dtype=jnp.int32)[None, :] < lengths[:, None])[:, :, None, None]
    page_keys = jnp.where(live_rows, keys_rot, jnp.zeros_like(keys_rot)).reshape(
        blocks_each, PAGE_LEN, local_width
    )
    page_values = jnp.where(live_rows, values_in, jnp.zeros_like(values_in)).reshape(
        blocks_each, PAGE_LEN, local_width
    )
    stacked = jnp.stack([page_keys, page_values])
    outgoing = jnp.zeros_like(stacked).at[:, send_pos].set(stacked)
    incoming = lax.all_to_all(outgoing, "page", split_axis=1, concat_axis=1, tiled=True)
    arrival_hit = (owners[:, None, :] == page_index) & (
        order_in[:, None, :] == jnp.arange(capacity, dtype=jnp.int32)[None, :, None]
    )
    arrival_slot = jnp.sum(jnp.where(arrival_hit, local_slot[:, None, :], 0), axis=2).reshape(
        blocks_each
    )
    kv_pages = jnp.zeros_like(incoming).at[:, arrival_slot].set(incoming)
    return (layer_out, kv_pages)


def solution(mesh):
    in_specs = (
        P(ROWPAGE, None, COL),
        P(ROWPAGE),
        P(ROW, None),
        P(ROWPAGE, COL),
        P(None, ROWPAGE, None),
        P(COL, ROWPAGE),
        P(None, ROWPAGE, COL),
        P(COL, ROWPAGE),
        P(),
        P(),
        P(),
        P(),
    )
    out_specs = (P(ROWPAGE, None, COL), P(None, ROWPAGE, None, COL))
    fine = Mesh(
        mesh.devices.reshape(
            mesh.shape["row"] // 2, 2, 2, mesh.shape["col"] // 2, mesh.shape["page"]
        ),
        ("ry", "rc", "zh", "xx", "page"),
    )
    return jax.shard_map(
        on_device, mesh=fine, in_specs=in_specs, out_specs=out_specs, check_vma=False
    )
```

```python
import jax
import jax.numpy as jnp
from jax import lax
from jax.sharding import Mesh, PartitionSpec as P

PAGE_LEN = 128
ROW = ("ry", "rc")
COL = ("zh", "xx")
ROWPAGE = ("ry", "rc", "page")


def normalize(values, norm_gain):
    mean_sq = jnp.mean(values * values, axis=-1, keepdims=True)
    return values * lax.rsqrt(mean_sq + 1e-06) * norm_gain


def rotate(values):
    row_count = values.shape[-3]
    head_dim = values.shape[-1]
    half_dim = head_dim // 2
    frequency = 10000.0 ** (-2.0 * jnp.arange(half_dim, dtype=jnp.float32) / head_dim)
    angles = jnp.arange(row_count, dtype=jnp.float32)[:, None] * frequency[None, :]
    cosine = jnp.cos(angles)[:, None, :]
    sine_table = jnp.sin(angles)[:, None, :]
    leading = values[..., :half_dim]
    trailing = values[..., half_dim:]
    return jnp.concatenate(
        [leading * cosine - trailing * sine_table, trailing * cosine + leading * sine_table],
        axis=-1,
    )


def attend(query_rows, key_rows, value_rows, length):
    row_count = query_rows.shape[0]
    scores = jnp.einsum(
        "qhd,khd->hqk", query_rows, key_rows, preferred_element_type=jnp.float32
    ) * query_rows.shape[2] ** (-0.5)
    positions = jnp.arange(row_count, dtype=jnp.int32)
    seen_keys = (positions[None, :] <= positions[:, None]) & (positions[None, :] < length)
    exp_scores = jnp.where(seen_keys[None], jnp.exp(scores), 0.0)
    attn_probs = (exp_scores / jnp.sum(exp_scores, axis=-1, keepdims=True)).astype(jnp.bfloat16)
    attended = jnp.einsum(
        "hqk,khd->qhd", attn_probs, value_rows, preferred_element_type=jnp.float32
    )
    live_rows = (positions < length)[:, None, None]
    return jnp.where(live_rows, attended, 0.0).astype(jnp.bfloat16)


def contract_rows(lhs, rhs_t):
    return lax.dot_general(
        lhs, rhs_t, (((1,), (1,)), ((), ())), preferred_element_type=jnp.float32
    )


def gather_a2a(x, axis_name, axis):
    count = lax.axis_size(axis_name)
    copies = jnp.broadcast_to(x[None], (count,) + x.shape)
    got = lax.all_to_all(copies, axis_name, 0, 0, tiled=True)
    got = jnp.moveaxis(got, 0, axis)
    shape = list(x.shape)
    shape[axis] *= count
    return got.reshape(shape)


def scatter_sum_a2a(x, axis_name, axis):
    count = lax.axis_size(axis_name)
    shape = list(x.shape)
    split = shape[:axis] + [count, shape[axis] // count] + shape[axis + 1 :]
    got = lax.all_to_all(x.reshape(split), axis_name, axis, axis, tiled=True)
    return jnp.sum(got.astype(jnp.float32), axis=axis)


def swap_halves(x):
    return lax.ppermute(x, "zh", [(0, 1), (1, 0)])


def gather_col(x, axis):
    half = lax.axis_index("zh")
    other = swap_halves(x)
    pair = jnp.stack([jnp.where(half == 0, x, other), jnp.where(half == 0, other, x)])
    count = lax.axis_size("xx")
    copies = jnp.broadcast_to(pair[None], (count,) + pair.shape)
    got = lax.all_to_all(copies, "xx", 0, 0, tiled=True)
    got = jnp.moveaxis(jnp.swapaxes(got, 0, 1).reshape((-1,) + x.shape), 0, axis)
    shape = list(x.shape)
    shape[axis] *= 2 * count
    return got.reshape(shape)


def scatter_sum_col(x, axis):
    count = lax.axis_size("xx")
    shape = list(x.shape)
    split = shape[:axis] + [2, count, shape[axis] // (2 * count)] + shape[axis + 1 :]
    got = lax.all_to_all(x.reshape(split), "xx", axis + 1, axis + 1, tiled=True)
    part = jnp.sum(got.astype(jnp.float32), axis=axis + 1)
    half = lax.axis_index("zh")
    mine = jnp.take(part, half, axis=axis)
    theirs = swap_halves(jnp.take(part, 1 - half, axis=axis))
    return mine + theirs


def gather_rows(x):
    pages = lax.axis_size("page")
    got = lax.all_to_all(jnp.broadcast_to(x[None], (pages,) + x.shape), "page", 0, 0, tiled=True)
    got = got.reshape((-1,) + x.shape[1:])
    chips = lax.axis_size("ry")
    got = lax.all_to_all(jnp.broadcast_to(got[None], (chips,) + got.shape), "ry", 0, 0, tiled=True)
    cores = lax.axis_size("rc")
    got = jnp.broadcast_to(got[:, None], (chips, cores) + got.shape[1:])
    got = lax.all_to_all(got, "rc", 1, 1, tiled=True)
    return got.reshape((-1,) + x.shape[1:])


def on_device(
    tokens,
    lengths,
    page_slot,
    w_query,
    w_keyval,
    w_out,
    w_gateup,
    w_down,
    attn_gain,
    ffn_gain,
    query_gain,
    key_gain,
):
    col_count = lax.axis_size(COL)
    col_index = lax.axis_index(COL)
    head_dim = query_gain.shape[0]
    local_width = w_query.shape[1]
    local_heads = local_width // head_dim
    kv_heads = w_keyval.shape[2] // head_dim
    group_size = local_heads * col_count // kv_heads
    assert group_size % local_heads == 0
    kv_head = (col_index * local_heads) // group_size
    unit_count = w_gateup.shape[2]
    kv_piece = lax.dynamic_slice_in_dim(w_keyval, kv_head * head_dim, head_dim, axis=2)
    pieces = [
        w_query.astype(jnp.bfloat16),
        jnp.transpose(kv_piece.astype(jnp.bfloat16), (1, 0, 2)).reshape(kv_piece.shape[1], -1),
        jnp.transpose(w_out.astype(jnp.bfloat16)),
        jnp.transpose(w_gateup.astype(jnp.bfloat16), (1, 0, 2)).reshape(w_gateup.shape[1], -1),
        jnp.transpose(w_down.astype(jnp.bfloat16)),
    ]
    widths = [p.shape[1] for p in pieces]
    offsets = [sum(widths[:i]) for i in range(len(widths) + 1)]
    attn_full = gather_rows(jnp.concatenate(pieces[:3], axis=1))
    ffn_full = lax.all_gather(jnp.concatenate(pieces[3:], axis=1), ROWPAGE, axis=0, tiled=True)
    qkv_w = attn_full[:, offsets[0] : offsets[2]]
    out_t = attn_full[:, offsets[2] : offsets[3]]
    gateup_w = ffn_full[:, : offsets[4] - offsets[3]]
    down_t = ffn_full[:, offsets[4] - offsets[3] :]

    prompt_count, seq_len, local_feat = tokens.shape
    gathered = gather_col(tokens, 2)
    model_width = gathered.shape[2]
    attn_in = normalize(gathered.astype(jnp.float32), attn_gain).astype(jnp.bfloat16)
    projected = jnp.dot(
        attn_in.reshape(-1, model_width), qkv_w, preferred_element_type=jnp.float32
    )
    projected = projected.reshape(prompt_count, seq_len, local_heads + 2, head_dim)
    queries = rotate(normalize(projected[:, :, :local_heads], query_gain)).astype(jnp.bfloat16)
    keys_one = rotate(normalize(projected[:, :, local_heads : local_heads + 1], key_gain)).astype(
        jnp.bfloat16
    )
    values_one = projected[:, :, local_heads + 1 : local_heads + 2].astype(jnp.bfloat16)
    keys_rot = jnp.broadcast_to(keys_one, queries.shape)
    values_in = jnp.broadcast_to(values_one, queries.shape)
    attended = jnp.stack(
        [
            attend(queries[i], keys_rot[i], values_in[i], lengths[i]).reshape(seq_len, local_width)
            for i in range(prompt_count)
        ]
    )
    attn_terms = contract_rows(attended.reshape(-1, local_width), out_t)
    attn_terms = attn_terms.reshape(prompt_count, seq_len, model_width).astype(jnp.bfloat16)
    attn_sum = scatter_sum_col(attn_terms, 2)
    residual = (tokens.astype(jnp.float32) + attn_sum).astype(jnp.bfloat16)
    residual_all = gather_col(residual, 2)
    ffn_in = normalize(residual_all.astype(jnp.float32), ffn_gain).astype(jnp.bfloat16)
    gate_up = jnp.dot(
        ffn_in.reshape(-1, model_width), gateup_w, preferred_element_type=jnp.float32
    )
    hidden = (jax.nn.silu(gate_up[:, :unit_count]) * gate_up[:, unit_count:]).astype(jnp.bfloat16)
    ffn_terms = contract_rows(hidden, down_t).reshape(prompt_count, seq_len, model_width)
    ffn_sum = scatter_sum_col(ffn_terms.astype(jnp.bfloat16), 2)
    layer_out = (residual.astype(jnp.float32) + ffn_sum).astype(jnp.bfloat16)
    page_count = lax.axis_size("page")
    page_index = lax.axis_index("page")
    blocks_each = prompt_count * (seq_len // PAGE_LEN)
    capacity = blocks_each // page_count
    owners = page_slot // blocks_each
    local_slot = page_slot % blocks_each
    same_owner = owners[:, :, None] == owners[:, None, :]
    earlier = (
        jnp.arange(blocks_each, dtype=jnp.int32)[None, :]
        < jnp.arange(blocks_each, dtype=jnp.int32)[:, None]
    )
    order_in = jnp.sum((same_owner & earlier[None]).astype(jnp.int32), axis=2)
    my_owners = lax.dynamic_index_in_dim(owners, page_index, 0, keepdims=False)
    my_order = lax.dynamic_index_in_dim(order_in, page_index, 0, keepdims=False)
    send_pos = my_owners * capacity + my_order
    live_rows = (jnp.arange(seq_len, dtype=jnp.int32)[None, :] < lengths[:, None])[:, :, None, None]
    page_keys = jnp.where(live_rows, keys_rot, jnp.zeros_like(keys_rot)).reshape(
        blocks_each, PAGE_LEN, local_width
    )
    page_values = jnp.where(live_rows, values_in, jnp.zeros_like(values_in)).reshape(
        blocks_each, PAGE_LEN, local_width
    )
    stacked = jnp.stack([page_keys, page_values])
    outgoing = jnp.zeros_like(stacked).at[:, send_pos].set(stacked)
    incoming = lax.all_to_all(outgoing, "page", split_axis=1, concat_axis=1, tiled=True)
    arrival_hit = (owners[:, None, :] == page_index) & (
        order_in[:, None, :] == jnp.arange(capacity, dtype=jnp.int32)[None, :, None]
    )
    arrival_slot = jnp.sum(jnp.where(arrival_hit, local_slot[:, None, :], 0), axis=2).reshape(
        blocks_each
    )
    kv_pages = jnp.zeros_like(incoming).at[:, arrival_slot].set(incoming)
    return (layer_out, kv_pages)


def solution(mesh):
    in_specs = (
        P(ROWPAGE, None, COL),
        P(ROWPAGE),
        P(ROW, None),
        P(ROWPAGE, COL),
        P(None, ROWPAGE, None),
        P(COL, ROWPAGE),
        P(None, ROWPAGE, COL),
        P(COL, ROWPAGE),
        P(),
        P(),
        P(),
        P(),
    )
    out_specs = (P(ROWPAGE, None, COL), P(None, ROWPAGE, None, COL))
    fine = Mesh(
        mesh.devices.reshape(
            mesh.shape["row"] // 2, 2, 2, mesh.shape["col"] // 2, mesh.shape["page"]
        ),
        ("ry", "rc", "zh", "xx", "page"),
    )
    return jax.shard_map(
        on_device, mesh=fine, in_specs=in_specs, out_specs=out_specs, check_vma=False
    )
```

```python
import jax
import jax.numpy as jnp
from jax import lax
from jax.sharding import Mesh, PartitionSpec as P

PAGE_LEN = 128
ROW = ("ry", "rc")
COL = ("zh", "xx")
ROWPAGE = ("ry", "rc", "page")


def normalize(values, norm_gain):
    mean_sq = jnp.mean(values * values, axis=-1, keepdims=True)
    return values * lax.rsqrt(mean_sq + 1e-06) * norm_gain


def rotate(values):
    row_count = values.shape[-3]
    head_dim = values.shape[-1]
    half_dim = head_dim // 2
    frequency = 10000.0 ** (-2.0 * jnp.arange(half_dim, dtype=jnp.float32) / head_dim)
    angles = jnp.arange(row_count, dtype=jnp.float32)[:, None] * frequency[None, :]
    cosine = jnp.cos(angles)[:, None, :]
    sine_table = jnp.sin(angles)[:, None, :]
    leading = values[..., :half_dim]
    trailing = values[..., half_dim:]
    return jnp.concatenate(
        [leading * cosine - trailing * sine_table, trailing * cosine + leading * sine_table],
        axis=-1,
    )


def attend(query_rows, key_rows, value_rows, length):
    row_count = query_rows.shape[0]
    scores = jnp.einsum(
        "qhd,khd->hqk", query_rows, key_rows, preferred_element_type=jnp.float32
    ) * query_rows.shape[2] ** (-0.5)
    positions = jnp.arange(row_count, dtype=jnp.int32)
    seen_keys = (positions[None, :] <= positions[:, None]) & (positions[None, :] < length)
    exp_scores = jnp.where(seen_keys[None], jnp.exp(scores), 0.0)
    attn_probs = (exp_scores / jnp.sum(exp_scores, axis=-1, keepdims=True)).astype(jnp.bfloat16)
    attended = jnp.einsum(
        "hqk,khd->qhd", attn_probs, value_rows, preferred_element_type=jnp.float32
    )
    live_rows = (positions < length)[:, None, None]
    return jnp.where(live_rows, attended, 0.0).astype(jnp.bfloat16)


def contract_rows(lhs, rhs_t):
    return lax.dot_general(
        lhs, rhs_t, (((1,), (1,)), ((), ())), preferred_element_type=jnp.float32
    )


def gather_a2a(x, axis_name, axis):
    count = lax.axis_size(axis_name)
    copies = jnp.broadcast_to(x[None], (count,) + x.shape)
    got = lax.all_to_all(copies, axis_name, 0, 0, tiled=True)
    got = jnp.moveaxis(got, 0, axis)
    shape = list(x.shape)
    shape[axis] *= count
    return got.reshape(shape)


def scatter_sum_a2a(x, axis_name, axis):
    count = lax.axis_size(axis_name)
    shape = list(x.shape)
    split = shape[:axis] + [count, shape[axis] // count] + shape[axis + 1 :]
    got = lax.all_to_all(x.reshape(split), axis_name, axis, axis, tiled=True)
    return jnp.sum(got.astype(jnp.float32), axis=axis)


def swap_halves(x):
    return lax.ppermute(x, "zh", [(0, 1), (1, 0)])


def gather_col(x, axis):
    half = lax.axis_index("zh")
    other = swap_halves(x)
    pair = jnp.stack([jnp.where(half == 0, x, other), jnp.where(half == 0, other, x)])
    return gather_xx(pair, x, axis)


def gather_xx(pair, x, axis):
    count = lax.axis_size("xx")
    copies = jnp.broadcast_to(pair[None], (count,) + pair.shape)
    got = lax.all_to_all(copies, "xx", 0, 0, tiled=True)
    got = jnp.moveaxis(jnp.swapaxes(got, 0, 1).reshape((-1,) + x.shape), 0, axis)
    shape = list(x.shape)
    shape[axis] *= 2 * count
    return got.reshape(shape)


def scatter_sum_col(x, axis):
    count = lax.axis_size("xx")
    shape = list(x.shape)
    split = shape[:axis] + [2, count, shape[axis] // (2 * count)] + shape[axis + 1 :]
    got = lax.all_to_all(x.reshape(split), "xx", axis + 1, axis + 1, tiled=True)
    part = jnp.sum(got.astype(jnp.float32), axis=axis + 1)
    half = lax.axis_index("zh")
    mine = jnp.take(part, half, axis=axis)
    theirs = swap_halves(jnp.take(part, 1 - half, axis=axis))
    return mine + theirs


def gather_rows(x):
    pages = lax.axis_size("page")
    got = lax.all_to_all(jnp.broadcast_to(x[None], (pages,) + x.shape), "page", 0, 0, tiled=True)
    got = got.reshape((-1,) + x.shape[1:])
    chips = lax.axis_size("ry")
    got = lax.all_to_all(jnp.broadcast_to(got[None], (chips,) + got.shape), "ry", 0, 0, tiled=True)
    cores = lax.axis_size("rc")
    got = jnp.broadcast_to(got[:, None], (chips, cores) + got.shape[1:])
    got = lax.all_to_all(got, "rc", 1, 1, tiled=True)
    return got.reshape((-1,) + x.shape[1:])


def on_device(
    tokens,
    lengths,
    page_slot,
    w_query,
    w_keyval,
    w_out,
    w_gateup,
    w_down,
    attn_gain,
    ffn_gain,
    query_gain,
    key_gain,
):
    col_count = lax.axis_size(COL)
    col_index = lax.axis_index(COL)
    head_dim = query_gain.shape[0]
    local_width = w_query.shape[1]
    local_heads = local_width // head_dim
    kv_heads = w_keyval.shape[2] // head_dim
    group_size = local_heads * col_count // kv_heads
    assert group_size % local_heads == 0
    kv_head = (col_index * local_heads) // group_size
    unit_count = w_gateup.shape[2]
    kv_piece = lax.dynamic_slice_in_dim(w_keyval, kv_head * head_dim, head_dim, axis=2)
    pieces = [
        w_query.astype(jnp.bfloat16),
        jnp.transpose(kv_piece.astype(jnp.bfloat16), (1, 0, 2)).reshape(kv_piece.shape[1], -1),
        jnp.transpose(w_out.astype(jnp.bfloat16)),
        jnp.transpose(w_gateup.astype(jnp.bfloat16), (1, 0, 2)).reshape(w_gateup.shape[1], -1),
        jnp.transpose(w_down.astype(jnp.bfloat16)),
    ]
    widths = [p.shape[1] for p in pieces]
    offsets = [sum(widths[:i]) for i in range(len(widths) + 1)]
    attn_full = gather_rows(jnp.concatenate(pieces[:3], axis=1))
    ffn_full = lax.all_gather(jnp.concatenate(pieces[3:], axis=1), ROWPAGE, axis=0, tiled=True)
    qkv_w = attn_full[:, offsets[0] : offsets[2]]
    out_t = attn_full[:, offsets[2] : offsets[3]]
    gateup_w = ffn_full[:, : offsets[4] - offsets[3]]
    down_t = ffn_full[:, offsets[4] - offsets[3] :]

    prompt_count, seq_len, local_feat = tokens.shape
    gathered = gather_col(tokens, 2)
    model_width = gathered.shape[2]
    attn_in = normalize(gathered.astype(jnp.float32), attn_gain).astype(jnp.bfloat16)
    projected = jnp.dot(
        attn_in.reshape(-1, model_width), qkv_w, preferred_element_type=jnp.float32
    )
    projected = projected.reshape(prompt_count, seq_len, local_heads + 2, head_dim)
    queries = rotate(normalize(projected[:, :, :local_heads], query_gain)).astype(jnp.bfloat16)
    keys_one = rotate(normalize(projected[:, :, local_heads : local_heads + 1], key_gain)).astype(
        jnp.bfloat16
    )
    values_one = projected[:, :, local_heads + 1 : local_heads + 2].astype(jnp.bfloat16)
    keys_rot = jnp.broadcast_to(keys_one, queries.shape)
    values_in = jnp.broadcast_to(values_one, queries.shape)
    attended = jnp.stack(
        [
            attend(queries[i], keys_rot[i], values_in[i], lengths[i]).reshape(seq_len, local_width)
            for i in range(prompt_count)
        ]
    )
    attn_terms = contract_rows(attended.reshape(-1, local_width), out_t)
    attn_terms = attn_terms.reshape(prompt_count, seq_len, model_width).astype(jnp.bfloat16)
    xx_count = lax.axis_size("xx")
    xx_index = lax.axis_index("xx")
    block = local_feat
    split = (prompt_count, seq_len, 2, xx_count, block)
    got = lax.all_to_all(attn_terms.reshape(split), "xx", 3, 3, tiled=True)
    part = jnp.sum(got.astype(jnp.float32), axis=3)
    total = part + swap_halves(part)
    tok_pair = lax.dynamic_index_in_dim(gathered.reshape(split), xx_index, 3, keepdims=False)
    res_pair = (tok_pair.astype(jnp.float32) + total).astype(jnp.bfloat16)
    residual = lax.dynamic_index_in_dim(res_pair, lax.axis_index("zh"), 2, keepdims=False)
    residual_all = gather_xx(jnp.moveaxis(res_pair, 2, 0), residual, 2)
    ffn_in = normalize(residual_all.astype(jnp.float32), ffn_gain).astype(jnp.bfloat16)
    gate_up = jnp.dot(
        ffn_in.reshape(-1, model_width), gateup_w, preferred_element_type=jnp.float32
    )
    hidden = (jax.nn.silu(gate_up[:, :unit_count]) * gate_up[:, unit_count:]).astype(jnp.bfloat16)
    ffn_terms = contract_rows(hidden, down_t).reshape(prompt_count, seq_len, model_width)
    ffn_sum = scatter_sum_col(ffn_terms.astype(jnp.bfloat16), 2)
    layer_out = (residual.astype(jnp.float32) + ffn_sum).astype(jnp.bfloat16)
    page_count = lax.axis_size("page")
    page_index = lax.axis_index("page")
    blocks_each = prompt_count * (seq_len // PAGE_LEN)
    capacity = blocks_each // page_count
    owners = page_slot // blocks_each
    local_slot = page_slot % blocks_each
    same_owner = owners[:, :, None] == owners[:, None, :]
    earlier = (
        jnp.arange(blocks_each, dtype=jnp.int32)[None, :]
        < jnp.arange(blocks_each, dtype=jnp.int32)[:, None]
    )
    order_in = jnp.sum((same_owner & earlier[None]).astype(jnp.int32), axis=2)
    my_owners = lax.dynamic_index_in_dim(owners, page_index, 0, keepdims=False)
    my_order = lax.dynamic_index_in_dim(order_in, page_index, 0, keepdims=False)
    send_pos = my_owners * capacity + my_order
    live_rows = (jnp.arange(seq_len, dtype=jnp.int32)[None, :] < lengths[:, None])[:, :, None, None]
    page_keys = jnp.where(live_rows, keys_rot, jnp.zeros_like(keys_rot)).reshape(
        blocks_each, PAGE_LEN, local_width
    )
    page_values = jnp.where(live_rows, values_in, jnp.zeros_like(values_in)).reshape(
        blocks_each, PAGE_LEN, local_width
    )
    stacked = jnp.stack([page_keys, page_values])
    outgoing = jnp.zeros_like(stacked).at[:, send_pos].set(stacked)
    incoming = lax.all_to_all(outgoing, "page", split_axis=1, concat_axis=1, tiled=True)
    arrival_hit = (owners[:, None, :] == page_index) & (
        order_in[:, None, :] == jnp.arange(capacity, dtype=jnp.int32)[None, :, None]
    )
    arrival_slot = jnp.sum(jnp.where(arrival_hit, local_slot[:, None, :], 0), axis=2).reshape(
        blocks_each
    )
    kv_pages = jnp.zeros_like(incoming).at[:, arrival_slot].set(incoming)
    return (layer_out, kv_pages)


def solution(mesh):
    in_specs = (
        P(ROWPAGE, None, COL),
        P(ROWPAGE),
        P(ROW, None),
        P(ROWPAGE, COL),
        P(None, ROWPAGE, None),
        P(COL, ROWPAGE),
        P(None, ROWPAGE, COL),
        P(COL, ROWPAGE),
        P(),
        P(),
        P(),
        P(),
    )
    out_specs = (P(ROWPAGE, None, COL), P(None, ROWPAGE, None, COL))
    fine = Mesh(
        mesh.devices.reshape(
            mesh.shape["row"] // 2, 2, 2, mesh.shape["col"] // 2, mesh.shape["page"]
        ),
        ("ry", "rc", "zh", "xx", "page"),
    )
    return jax.shard_map(
        on_device, mesh=fine, in_specs=in_specs, out_specs=out_specs, check_vma=False
    )
```

```python
import jax
import jax.numpy as jnp
from jax import lax
from jax.sharding import Mesh, PartitionSpec as P

PAGE_LEN = 128
ROW = ("ry", "rc")
COL = ("zh", "xx")
ROWPAGE = ("ry", "rc", "page")


def normalize(values, norm_gain):
    mean_sq = jnp.mean(values * values, axis=-1, keepdims=True)
    return values * lax.rsqrt(mean_sq + 1e-06) * norm_gain


def rotate(values):
    row_count = values.shape[-3]
    head_dim = values.shape[-1]
    half_dim = head_dim // 2
    frequency = 10000.0 ** (-2.0 * jnp.arange(half_dim, dtype=jnp.float32) / head_dim)
    angles = jnp.arange(row_count, dtype=jnp.float32)[:, None] * frequency[None, :]
    cosine = jnp.cos(angles)[:, None, :]
    sine_table = jnp.sin(angles)[:, None, :]
    leading = values[..., :half_dim]
    trailing = values[..., half_dim:]
    return jnp.concatenate(
        [leading * cosine - trailing * sine_table, trailing * cosine + leading * sine_table],
        axis=-1,
    )


def attend(query_rows, key_rows, value_rows, length):
    row_count = query_rows.shape[0]
    scores = jnp.einsum(
        "qhd,khd->hqk", query_rows, key_rows, preferred_element_type=jnp.float32
    ) * query_rows.shape[2] ** (-0.5)
    positions = jnp.arange(row_count, dtype=jnp.int32)
    seen_keys = (positions[None, :] <= positions[:, None]) & (positions[None, :] < length)
    exp_scores = jnp.where(seen_keys[None], jnp.exp(scores), 0.0)
    attn_probs = (exp_scores / jnp.sum(exp_scores, axis=-1, keepdims=True)).astype(jnp.bfloat16)
    attended = jnp.einsum(
        "hqk,khd->qhd", attn_probs, value_rows, preferred_element_type=jnp.float32
    )
    live_rows = (positions < length)[:, None, None]
    return jnp.where(live_rows, attended, 0.0).astype(jnp.bfloat16)


def contract_rows(lhs, rhs_t):
    return lax.dot_general(
        lhs, rhs_t, (((1,), (1,)), ((), ())), preferred_element_type=jnp.float32
    )


def gather_a2a(x, axis_name, axis):
    count = lax.axis_size(axis_name)
    copies = jnp.broadcast_to(x[None], (count,) + x.shape)
    got = lax.all_to_all(copies, axis_name, 0, 0, tiled=True)
    got = jnp.moveaxis(got, 0, axis)
    shape = list(x.shape)
    shape[axis] *= count
    return got.reshape(shape)


def scatter_sum_a2a(x, axis_name, axis):
    count = lax.axis_size(axis_name)
    shape = list(x.shape)
    split = shape[:axis] + [count, shape[axis] // count] + shape[axis + 1 :]
    got = lax.all_to_all(x.reshape(split), axis_name, axis, axis, tiled=True)
    return jnp.sum(got.astype(jnp.float32), axis=axis)


def swap_halves(x):
    return lax.ppermute(x, "zh", [(0, 1), (1, 0)])


def gather_col(x, axis):
    half = lax.axis_index("zh")
    other = swap_halves(x)
    pair = jnp.stack([jnp.where(half == 0, x, other), jnp.where(half == 0, other, x)])
    count = lax.axis_size("xx")
    copies = jnp.broadcast_to(pair[None], (count,) + pair.shape)
    got = lax.all_to_all(copies, "xx", 0, 0, tiled=True)
    got = jnp.moveaxis(jnp.swapaxes(got, 0, 1).reshape((-1,) + x.shape), 0, axis)
    shape = list(x.shape)
    shape[axis] *= 2 * count
    return got.reshape(shape)


def scatter_sum_col(x, axis):
    count = lax.axis_size("xx")
    shape = list(x.shape)
    split = shape[:axis] + [2, count, shape[axis] // (2 * count)] + shape[axis + 1 :]
    got = lax.all_to_all(x.reshape(split), "xx", axis + 1, axis + 1, tiled=True)
    part = jnp.sum(got.astype(jnp.float32), axis=axis + 1)
    half = lax.axis_index("zh")
    mine = jnp.take(part, half, axis=axis)
    theirs = swap_halves(jnp.take(part, 1 - half, axis=axis).astype(jnp.bfloat16))
    return mine + theirs.astype(jnp.float32)


def gather_rows(x):
    pages = lax.axis_size("page")
    got = lax.all_to_all(jnp.broadcast_to(x[None], (pages,) + x.shape), "page", 0, 0, tiled=True)
    got = got.reshape((-1,) + x.shape[1:])
    chips = lax.axis_size("ry")
    got = lax.all_to_all(jnp.broadcast_to(got[None], (chips,) + got.shape), "ry", 0, 0, tiled=True)
    cores = lax.axis_size("rc")
    got = jnp.broadcast_to(got[:, None], (chips, cores) + got.shape[1:])
    got = lax.all_to_all(got, "rc", 1, 1, tiled=True)
    return got.reshape((-1,) + x.shape[1:])


def on_device(
    tokens,
    lengths,
    page_slot,
    w_query,
    w_keyval,
    w_out,
    w_gateup,
    w_down,
    attn_gain,
    ffn_gain,
    query_gain,
    key_gain,
):
    col_count = lax.axis_size(COL)
    col_index = lax.axis_index(COL)
    head_dim = query_gain.shape[0]
    local_width = w_query.shape[1]
    local_heads = local_width // head_dim
    kv_heads = w_keyval.shape[2] // head_dim
    group_size = local_heads * col_count // kv_heads
    assert group_size % local_heads == 0
    kv_head = (col_index * local_heads) // group_size
    unit_count = w_gateup.shape[2]
    kv_piece = lax.dynamic_slice_in_dim(w_keyval, kv_head * head_dim, head_dim, axis=2)
    pieces = [
        w_query.astype(jnp.bfloat16),
        jnp.transpose(kv_piece.astype(jnp.bfloat16), (1, 0, 2)).reshape(kv_piece.shape[1], -1),
        jnp.transpose(w_out.astype(jnp.bfloat16)),
        jnp.transpose(w_gateup.astype(jnp.bfloat16), (1, 0, 2)).reshape(w_gateup.shape[1], -1),
        jnp.transpose(w_down.astype(jnp.bfloat16)),
    ]
    widths = [p.shape[1] for p in pieces]
    offsets = [sum(widths[:i]) for i in range(len(widths) + 1)]
    attn_full = gather_rows(jnp.concatenate(pieces[:3], axis=1))
    ffn_full = lax.all_gather(jnp.concatenate(pieces[3:], axis=1), ROWPAGE, axis=0, tiled=True)
    qkv_w = attn_full[:, offsets[0] : offsets[2]]
    out_t = attn_full[:, offsets[2] : offsets[3]]
    gateup_w = ffn_full[:, : offsets[4] - offsets[3]]
    down_t = ffn_full[:, offsets[4] - offsets[3] :]

    prompt_count, seq_len, local_feat = tokens.shape
    gathered = gather_col(tokens, 2)
    model_width = gathered.shape[2]
    attn_in = normalize(gathered.astype(jnp.float32), attn_gain).astype(jnp.bfloat16)
    projected = jnp.dot(
        attn_in.reshape(-1, model_width), qkv_w, preferred_element_type=jnp.float32
    )
    projected = projected.reshape(prompt_count, seq_len, local_heads + 2, head_dim)
    queries = rotate(normalize(projected[:, :, :local_heads], query_gain)).astype(jnp.bfloat16)
    keys_one = rotate(normalize(projected[:, :, local_heads : local_heads + 1], key_gain)).astype(
        jnp.bfloat16
    )
    values_one = projected[:, :, local_heads + 1 : local_heads + 2].astype(jnp.bfloat16)
    keys_rot = jnp.broadcast_to(keys_one, queries.shape)
    values_in = jnp.broadcast_to(values_one, queries.shape)
    attended = jnp.stack(
        [
            attend(queries[i], keys_rot[i], values_in[i], lengths[i]).reshape(seq_len, local_width)
            for i in range(prompt_count)
        ]
    )
    attn_terms = contract_rows(attended.reshape(-1, local_width), out_t)
    attn_terms = attn_terms.reshape(prompt_count, seq_len, model_width).astype(jnp.bfloat16)
    attn_sum = scatter_sum_col(attn_terms, 2)
    residual = (tokens.astype(jnp.float32) + attn_sum).astype(jnp.bfloat16)
    residual_all = gather_col(residual, 2)
    ffn_in = normalize(residual_all.astype(jnp.float32), ffn_gain).astype(jnp.bfloat16)
    gate_up = jnp.dot(
        ffn_in.reshape(-1, model_width), gateup_w, preferred_element_type=jnp.float32
    )
    hidden = (jax.nn.silu(gate_up[:, :unit_count]) * gate_up[:, unit_count:]).astype(jnp.bfloat16)
    ffn_terms = contract_rows(hidden, down_t).reshape(prompt_count, seq_len, model_width)
    ffn_sum = scatter_sum_col(ffn_terms.astype(jnp.bfloat16), 2)
    layer_out = (residual.astype(jnp.float32) + ffn_sum).astype(jnp.bfloat16)
    page_count = lax.axis_size("page")
    page_index = lax.axis_index("page")
    blocks_each = prompt_count * (seq_len // PAGE_LEN)
    capacity = blocks_each // page_count
    owners = page_slot // blocks_each
    local_slot = page_slot % blocks_each
    same_owner = owners[:, :, None] == owners[:, None, :]
    earlier = (
        jnp.arange(blocks_each, dtype=jnp.int32)[None, :]
        < jnp.arange(blocks_each, dtype=jnp.int32)[:, None]
    )
    order_in = jnp.sum((same_owner & earlier[None]).astype(jnp.int32), axis=2)
    my_owners = lax.dynamic_index_in_dim(owners, page_index, 0, keepdims=False)
    my_order = lax.dynamic_index_in_dim(order_in, page_index, 0, keepdims=False)
    send_pos = my_owners * capacity + my_order
    live_rows = (jnp.arange(seq_len, dtype=jnp.int32)[None, :] < lengths[:, None])[:, :, None, None]
    page_keys = jnp.where(live_rows, keys_rot, jnp.zeros_like(keys_rot)).reshape(
        blocks_each, PAGE_LEN, local_width
    )
    page_values = jnp.where(live_rows, values_in, jnp.zeros_like(values_in)).reshape(
        blocks_each, PAGE_LEN, local_width
    )
    stacked = jnp.stack([page_keys, page_values])
    outgoing = jnp.zeros_like(stacked).at[:, send_pos].set(stacked)
    incoming = lax.all_to_all(outgoing, "page", split_axis=1, concat_axis=1, tiled=True)
    arrival_hit = (owners[:, None, :] == page_index) & (
        order_in[:, None, :] == jnp.arange(capacity, dtype=jnp.int32)[None, :, None]
    )
    arrival_slot = jnp.sum(jnp.where(arrival_hit, local_slot[:, None, :], 0), axis=2).reshape(
        blocks_each
    )
    kv_pages = jnp.zeros_like(incoming).at[:, arrival_slot].set(incoming)
    return (layer_out, kv_pages)


def solution(mesh):
    in_specs = (
        P(ROWPAGE, None, COL),
        P(ROWPAGE),
        P(ROW, None),
        P(ROWPAGE, COL),
        P(None, ROWPAGE, None),
        P(COL, ROWPAGE),
        P(None, ROWPAGE, COL),
        P(COL, ROWPAGE),
        P(),
        P(),
        P(),
        P(),
    )
    out_specs = (P(ROWPAGE, None, COL), P(None, ROWPAGE, None, COL))
    fine = Mesh(
        mesh.devices.reshape(
            mesh.shape["row"] // 2, 2, 2, mesh.shape["col"] // 2, mesh.shape["page"]
        ),
        ("ry", "rc", "zh", "xx", "page"),
    )
    return jax.shard_map(
        on_device, mesh=fine, in_specs=in_specs, out_specs=out_specs, check_vma=False
    )
```

```python
import jax
import jax.numpy as jnp
from jax import lax
from jax.sharding import Mesh, PartitionSpec as P

PAGE_LEN = 128
ROW = ("ry", "rc")
COL = ("zh", "xx")
ROWPAGE = ("ry", "rc", "page")


def normalize(values, norm_gain):
    mean_sq = jnp.mean(values * values, axis=-1, keepdims=True)
    return values * lax.rsqrt(mean_sq + 1e-06) * norm_gain


def rotate(values):
    row_count = values.shape[-3]
    head_dim = values.shape[-1]
    half_dim = head_dim // 2
    frequency = 10000.0 ** (-2.0 * jnp.arange(half_dim, dtype=jnp.float32) / head_dim)
    angles = jnp.arange(row_count, dtype=jnp.float32)[:, None] * frequency[None, :]
    cosine = jnp.cos(angles)[:, None, :]
    sine_table = jnp.sin(angles)[:, None, :]
    leading = values[..., :half_dim]
    trailing = values[..., half_dim:]
    return jnp.concatenate(
        [leading * cosine - trailing * sine_table, trailing * cosine + leading * sine_table],
        axis=-1,
    )


def attend(query_rows, key_rows, value_rows, length):
    row_count = query_rows.shape[0]
    scores = jnp.einsum(
        "qhd,khd->hqk", query_rows, key_rows, preferred_element_type=jnp.float32
    ) * query_rows.shape[2] ** (-0.5)
    positions = jnp.arange(row_count, dtype=jnp.int32)
    seen_keys = (positions[None, :] <= positions[:, None]) & (positions[None, :] < length)
    exp_scores = jnp.where(seen_keys[None], jnp.exp(scores), 0.0)
    attn_probs = (exp_scores / jnp.sum(exp_scores, axis=-1, keepdims=True)).astype(jnp.bfloat16)
    attended = jnp.einsum(
        "hqk,khd->qhd", attn_probs, value_rows, preferred_element_type=jnp.float32
    )
    live_rows = (positions < length)[:, None, None]
    return jnp.where(live_rows, attended, 0.0).astype(jnp.bfloat16)


def contract_rows(lhs, rhs_t):
    return lax.dot_general(
        lhs, rhs_t, (((1,), (1,)), ((), ())), preferred_element_type=jnp.float32
    )


def gather_a2a(x, axis_name, axis):
    count = lax.axis_size(axis_name)
    copies = jnp.broadcast_to(x[None], (count,) + x.shape)
    got = lax.all_to_all(copies, axis_name, 0, 0, tiled=True)
    got = jnp.moveaxis(got, 0, axis)
    shape = list(x.shape)
    shape[axis] *= count
    return got.reshape(shape)


def scatter_sum_a2a(x, axis_name, axis):
    count = lax.axis_size(axis_name)
    shape = list(x.shape)
    split = shape[:axis] + [count, shape[axis] // count] + shape[axis + 1 :]
    got = lax.all_to_all(x.reshape(split), axis_name, axis, axis, tiled=True)
    return jnp.sum(got.astype(jnp.float32), axis=axis)


def swap_halves(x):
    return lax.ppermute(x, "zh", [(0, 1), (1, 0)])


def gather_col(x, axis):
    half = lax.axis_index("zh")
    other = swap_halves(x)
    pair = jnp.stack([jnp.where(half == 0, x, other), jnp.where(half == 0, other, x)])
    count = lax.axis_size("xx")
    copies = jnp.broadcast_to(pair[None], (count,) + pair.shape)
    got = lax.all_to_all(copies, "xx", 0, 0, tiled=True)
    got = jnp.moveaxis(jnp.swapaxes(got, 0, 1).reshape((-1,) + x.shape), 0, axis)
    shape = list(x.shape)
    shape[axis] *= 2 * count
    return got.reshape(shape)


def scatter_sum_col(x, axis):
    count = lax.axis_size("xx")
    shape = list(x.shape)
    split = shape[:axis] + [2, count, shape[axis] // (2 * count)] + shape[axis + 1 :]
    got = lax.all_to_all(x.reshape(split), "xx", axis + 1, axis + 1, tiled=True)
    part = jnp.sum(got.astype(jnp.float32), axis=axis + 1)
    half = lax.axis_index("zh")
    mine = jnp.take(part, half, axis=axis)
    theirs = swap_halves(jnp.take(part, 1 - half, axis=axis).astype(jnp.bfloat16))
    return mine + theirs.astype(jnp.float32)


def gather_rows(x):
    pages = lax.axis_size("page")
    got = lax.all_to_all(jnp.broadcast_to(x[None], (pages,) + x.shape), "page", 0, 0, tiled=True)
    got = got.reshape((-1,) + x.shape[1:])
    chips = lax.axis_size("ry")
    got = lax.all_to_all(jnp.broadcast_to(got[None], (chips,) + got.shape), "ry", 0, 0, tiled=True)
    cores = lax.axis_size("rc")
    got = jnp.broadcast_to(got[:, None], (chips, cores) + got.shape[1:])
    got = lax.all_to_all(got, "rc", 1, 1, tiled=True)
    return got.reshape((-1,) + x.shape[1:])


def send_pages(keys_rot, values_in, lengths, page_slot):
    prompt_count, seq_len, local_heads, head_dim = keys_rot.shape
    local_width = local_heads * head_dim
    page_count = lax.axis_size("page")
    page_index = lax.axis_index("page")
    blocks_each = prompt_count * (seq_len // PAGE_LEN)
    capacity = blocks_each // page_count
    owners = page_slot // blocks_each
    local_slot = page_slot % blocks_each
    same_owner = owners[:, :, None] == owners[:, None, :]
    earlier = (
        jnp.arange(blocks_each, dtype=jnp.int32)[None, :]
        < jnp.arange(blocks_each, dtype=jnp.int32)[:, None]
    )
    order_in = jnp.sum((same_owner & earlier[None]).astype(jnp.int32), axis=2)
    my_owners = lax.dynamic_index_in_dim(owners, page_index, 0, keepdims=False)
    my_order = lax.dynamic_index_in_dim(order_in, page_index, 0, keepdims=False)
    send_pos = my_owners * capacity + my_order
    live_rows = (jnp.arange(seq_len, dtype=jnp.int32)[None, :] < lengths[:, None])[:, :, None, None]
    page_keys = jnp.where(live_rows, keys_rot, jnp.zeros_like(keys_rot)).reshape(
        blocks_each, PAGE_LEN, local_width
    )
    page_values = jnp.where(live_rows, values_in, jnp.zeros_like(values_in)).reshape(
        blocks_each, PAGE_LEN, local_width
    )
    stacked = jnp.stack([page_keys, page_values])
    outgoing = jnp.zeros_like(stacked).at[:, send_pos].set(stacked)
    incoming = lax.all_to_all(outgoing, "page", split_axis=1, concat_axis=1, tiled=True)
    return incoming


def on_device(
    tokens,
    lengths,
    page_slot,
    w_query,
    w_keyval,
    w_out,
    w_gateup,
    w_down,
    attn_gain,
    ffn_gain,
    query_gain,
    key_gain,
):
    col_count = lax.axis_size(COL)
    col_index = lax.axis_index(COL)
    head_dim = query_gain.shape[0]
    local_width = w_query.shape[1]
    local_heads = local_width // head_dim
    kv_heads = w_keyval.shape[2] // head_dim
    group_size = local_heads * col_count // kv_heads
    assert group_size % local_heads == 0
    kv_head = (col_index * local_heads) // group_size
    unit_count = w_gateup.shape[2]
    kv_piece = lax.dynamic_slice_in_dim(w_keyval, kv_head * head_dim, head_dim, axis=2)
    pieces = [
        w_query.astype(jnp.bfloat16),
        jnp.transpose(kv_piece.astype(jnp.bfloat16), (1, 0, 2)).reshape(kv_piece.shape[1], -1),
        jnp.transpose(w_out.astype(jnp.bfloat16)),
        jnp.transpose(w_gateup.astype(jnp.bfloat16), (1, 0, 2)).reshape(w_gateup.shape[1], -1),
        jnp.transpose(w_down.astype(jnp.bfloat16)),
    ]
    widths = [p.shape[1] for p in pieces]
    offsets = [sum(widths[:i]) for i in range(len(widths) + 1)]
    attn_full = gather_rows(jnp.concatenate(pieces[:3], axis=1))
    ffn_full = lax.all_gather(jnp.concatenate(pieces[3:], axis=1), ROWPAGE, axis=0, tiled=True)
    qkv_w = attn_full[:, offsets[0] : offsets[2]]
    out_t = attn_full[:, offsets[2] : offsets[3]]
    gateup_w = ffn_full[:, : offsets[4] - offsets[3]]
    down_t = ffn_full[:, offsets[4] - offsets[3] :]

    prompt_count, seq_len, local_feat = tokens.shape
    gathered = gather_col(tokens, 2)
    model_width = gathered.shape[2]
    attn_in = normalize(gathered.astype(jnp.float32), attn_gain).astype(jnp.bfloat16)
    projected = jnp.dot(
        attn_in.reshape(-1, model_width), qkv_w, preferred_element_type=jnp.float32
    )
    projected = projected.reshape(prompt_count, seq_len, local_heads + 2, head_dim)
    queries = rotate(normalize(projected[:, :, :local_heads], query_gain)).astype(jnp.bfloat16)
    keys_one = rotate(normalize(projected[:, :, local_heads : local_heads + 1], key_gain)).astype(
        jnp.bfloat16
    )
    values_one = projected[:, :, local_heads + 1 : local_heads + 2].astype(jnp.bfloat16)
    keys_rot = jnp.broadcast_to(keys_one, queries.shape)
    values_in = jnp.broadcast_to(values_one, queries.shape)
    attended = jnp.stack(
        [
            attend(queries[i], keys_rot[i], values_in[i], lengths[i]).reshape(seq_len, local_width)
            for i in range(prompt_count)
        ]
    )
    incoming = send_pages(keys_rot, values_in, lengths, page_slot)
    incoming, attended = lax.optimization_barrier((incoming, attended))
    attn_terms = contract_rows(attended.reshape(-1, local_width), out_t)
    attn_terms = attn_terms.reshape(prompt_count, seq_len, model_width).astype(jnp.bfloat16)
    attn_sum = scatter_sum_col(attn_terms, 2)
    residual = (tokens.astype(jnp.float32) + attn_sum).astype(jnp.bfloat16)
    residual_all = gather_col(residual, 2)
    ffn_in = normalize(residual_all.astype(jnp.float32), ffn_gain).astype(jnp.bfloat16)
    gate_up = jnp.dot(
        ffn_in.reshape(-1, model_width), gateup_w, preferred_element_type=jnp.float32
    )
    hidden = (jax.nn.silu(gate_up[:, :unit_count]) * gate_up[:, unit_count:]).astype(jnp.bfloat16)
    ffn_terms = contract_rows(hidden, down_t).reshape(prompt_count, seq_len, model_width)
    ffn_sum = scatter_sum_col(ffn_terms.astype(jnp.bfloat16), 2)
    layer_out = (residual.astype(jnp.float32) + ffn_sum).astype(jnp.bfloat16)
    page_index = lax.axis_index("page")
    page_count = lax.axis_size("page")
    blocks_each = prompt_count * (seq_len // PAGE_LEN)
    capacity = blocks_each // page_count
    owners = page_slot // blocks_each
    local_slot = page_slot % blocks_each
    same_owner = owners[:, :, None] == owners[:, None, :]
    earlier = (
        jnp.arange(blocks_each, dtype=jnp.int32)[None, :]
        < jnp.arange(blocks_each, dtype=jnp.int32)[:, None]
    )
    order_in = jnp.sum((same_owner & earlier[None]).astype(jnp.int32), axis=2)
    arrival_hit = (owners[:, None, :] == page_index) & (
        order_in[:, None, :] == jnp.arange(capacity, dtype=jnp.int32)[None, :, None]
    )
    arrival_slot = jnp.sum(jnp.where(arrival_hit, local_slot[:, None, :], 0), axis=2).reshape(
        blocks_each
    )
    kv_pages = jnp.zeros_like(incoming).at[:, arrival_slot].set(incoming)
    return (layer_out, kv_pages)


def solution(mesh):
    in_specs = (
        P(ROWPAGE, None, COL),
        P(ROWPAGE),
        P(ROW, None),
        P(ROWPAGE, COL),
        P(None, ROWPAGE, None),
        P(COL, ROWPAGE),
        P(None, ROWPAGE, COL),
        P(COL, ROWPAGE),
        P(),
        P(),
        P(),
        P(),
    )
    out_specs = (P(ROWPAGE, None, COL), P(None, ROWPAGE, None, COL))
    fine = Mesh(
        mesh.devices.reshape(
            mesh.shape["row"] // 2, 2, 2, mesh.shape["col"] // 2, mesh.shape["page"]
        ),
        ("ry", "rc", "zh", "xx", "page"),
    )
    return jax.shard_map(
        on_device, mesh=fine, in_specs=in_specs, out_specs=out_specs, check_vma=False
    )
```

```python
import jax
import jax.numpy as jnp
from jax import lax
from jax.sharding import Mesh, PartitionSpec as P

PAGE_LEN = 128
ROW = ("ry", "rc")
COL = ("zh", "xx")
ROWPAGE = ("ry", "rc", "page")


def normalize(values, norm_gain):
    mean_sq = jnp.mean(values * values, axis=-1, keepdims=True)
    return values * lax.rsqrt(mean_sq + 1e-06) * norm_gain


def rotate(values):
    row_count = values.shape[-3]
    head_dim = values.shape[-1]
    half_dim = head_dim // 2
    frequency = 10000.0 ** (-2.0 * jnp.arange(half_dim, dtype=jnp.float32) / head_dim)
    angles = jnp.arange(row_count, dtype=jnp.float32)[:, None] * frequency[None, :]
    cosine = jnp.cos(angles)[:, None, :]
    sine_table = jnp.sin(angles)[:, None, :]
    leading = values[..., :half_dim]
    trailing = values[..., half_dim:]
    return jnp.concatenate(
        [leading * cosine - trailing * sine_table, trailing * cosine + leading * sine_table],
        axis=-1,
    )


def attend(query_rows, key_rows, value_rows, length):
    row_count = query_rows.shape[0]
    scores = jnp.einsum(
        "qhd,khd->hqk", query_rows, key_rows, preferred_element_type=jnp.float32
    ) * query_rows.shape[2] ** (-0.5)
    positions = jnp.arange(row_count, dtype=jnp.int32)
    seen_keys = (positions[None, :] <= positions[:, None]) & (positions[None, :] < length)
    exp_scores = jnp.where(seen_keys[None], jnp.exp(scores), 0.0)
    attn_probs = (exp_scores / jnp.sum(exp_scores, axis=-1, keepdims=True)).astype(jnp.bfloat16)
    attended = jnp.einsum(
        "hqk,khd->qhd", attn_probs, value_rows, preferred_element_type=jnp.float32
    )
    live_rows = (positions < length)[:, None, None]
    return jnp.where(live_rows, attended, 0.0).astype(jnp.bfloat16)


def contract_rows(lhs, rhs_t):
    return lax.dot_general(
        lhs, rhs_t, (((1,), (1,)), ((), ())), preferred_element_type=jnp.float32
    )


def gather_a2a(x, axis_name, axis):
    count = lax.axis_size(axis_name)
    copies = jnp.broadcast_to(x[None], (count,) + x.shape)
    got = lax.all_to_all(copies, axis_name, 0, 0, tiled=True)
    got = jnp.moveaxis(got, 0, axis)
    shape = list(x.shape)
    shape[axis] *= count
    return got.reshape(shape)


def scatter_sum_a2a(x, axis_name, axis):
    count = lax.axis_size(axis_name)
    shape = list(x.shape)
    split = shape[:axis] + [count, shape[axis] // count] + shape[axis + 1 :]
    got = lax.all_to_all(x.reshape(split), axis_name, axis, axis, tiled=True)
    return jnp.sum(got.astype(jnp.float32), axis=axis)


def swap_halves(x):
    return lax.ppermute(x, "zh", [(0, 1), (1, 0)])


def gather_col(x):
    half = lax.axis_index("zh")
    other = swap_halves(x)
    pair = jnp.stack([jnp.where(half == 0, x, other), jnp.where(half == 0, other, x)])
    count = lax.axis_size("xx")
    copies = jnp.broadcast_to(pair[None], (count,) + pair.shape)
    return lax.all_to_all(copies, "xx", 0, 0, tiled=True)


def scatter_sum_col(terms):
    got = lax.all_to_all(terms, "xx", 0, 0, tiled=True)
    part = jnp.sum(got.astype(jnp.float32), axis=0)
    half = lax.axis_index("zh")
    mine = jnp.take(part, half, axis=-2)
    theirs = swap_halves(jnp.take(part, 1 - half, axis=-2).astype(jnp.bfloat16))
    return mine + theirs.astype(jnp.float32)


def normalize_blocks(values, norm_gain):
    xx_count, zh_count = values.shape[0], values.shape[1]
    gain = jnp.swapaxes(norm_gain.reshape(zh_count, xx_count, -1), 0, 1)[:, :, None, None, :]
    mean_sq = jnp.mean(values * values, axis=(0, 1, 4), keepdims=True)
    return values * lax.rsqrt(mean_sq + 1e-06) * gain


def project_blocks(values, weights):
    xx_count, zh_count, block = values.shape[0], values.shape[1], values.shape[4]
    w = weights.reshape(zh_count, xx_count, block, -1)
    return jnp.einsum("xzpse,zxen->psn", values, w, preferred_element_type=jnp.float32)


def terms_blocks(values, weights_t, xx_count, zh_count):
    w = weights_t.reshape(zh_count, xx_count, -1, weights_t.shape[1])
    return jnp.einsum("psk,zxek->xpsze", values, w, preferred_element_type=jnp.float32)


def gather_rows(x):
    pages = lax.axis_size("page")
    got = lax.all_to_all(jnp.broadcast_to(x[None], (pages,) + x.shape), "page", 0, 0, tiled=True)
    got = got.reshape((-1,) + x.shape[1:])
    chips = lax.axis_size("ry")
    got = lax.all_to_all(jnp.broadcast_to(got[None], (chips,) + got.shape), "ry", 0, 0, tiled=True)
    cores = lax.axis_size("rc")
    got = jnp.broadcast_to(got[:, None], (chips, cores) + got.shape[1:])
    got = lax.all_to_all(got, "rc", 1, 1, tiled=True)
    return got.reshape((-1,) + x.shape[1:])


def send_pages(keys_rot, values_in, lengths, page_slot):
    prompt_count, seq_len, local_heads, head_dim = keys_rot.shape
    local_width = local_heads * head_dim
    page_count = lax.axis_size("page")
    page_index = lax.axis_index("page")
    blocks_each = prompt_count * (seq_len // PAGE_LEN)
    capacity = blocks_each // page_count
    owners = page_slot // blocks_each
    local_slot = page_slot % blocks_each
    same_owner = owners[:, :, None] == owners[:, None, :]
    earlier = (
        jnp.arange(blocks_each, dtype=jnp.int32)[None, :]
        < jnp.arange(blocks_each, dtype=jnp.int32)[:, None]
    )
    order_in = jnp.sum((same_owner & earlier[None]).astype(jnp.int32), axis=2)
    my_owners = lax.dynamic_index_in_dim(owners, page_index, 0, keepdims=False)
    my_order = lax.dynamic_index_in_dim(order_in, page_index, 0, keepdims=False)
    send_pos = my_owners * capacity + my_order
    live_rows = (jnp.arange(seq_len, dtype=jnp.int32)[None, :] < lengths[:, None])[:, :, None, None]
    page_keys = jnp.where(live_rows, keys_rot, jnp.zeros_like(keys_rot)).reshape(
        blocks_each, PAGE_LEN, local_width
    )
    page_values = jnp.where(live_rows, values_in, jnp.zeros_like(values_in)).reshape(
        blocks_each, PAGE_LEN, local_width
    )
    stacked = jnp.stack([page_keys, page_values])
    outgoing = jnp.zeros_like(stacked).at[:, send_pos].set(stacked)
    incoming = lax.all_to_all(outgoing, "page", split_axis=1, concat_axis=1, tiled=True)
    return incoming


def on_device(
    tokens,
    lengths,
    page_slot,
    w_query,
    w_keyval,
    w_out,
    w_gateup,
    w_down,
    attn_gain,
    ffn_gain,
    query_gain,
    key_gain,
):
    col_count = lax.axis_size(COL)
    col_index = lax.axis_index(COL)
    head_dim = query_gain.shape[0]
    local_width = w_query.shape[1]
    local_heads = local_width // head_dim
    kv_heads = w_keyval.shape[2] // head_dim
    group_size = local_heads * col_count // kv_heads
    assert group_size % local_heads == 0
    kv_head = (col_index * local_heads) // group_size
    unit_count = w_gateup.shape[2]
    kv_piece = lax.dynamic_slice_in_dim(w_keyval, kv_head * head_dim, head_dim, axis=2)
    pieces = [
        w_query.astype(jnp.bfloat16),
        jnp.transpose(kv_piece.astype(jnp.bfloat16), (1, 0, 2)).reshape(kv_piece.shape[1], -1),
        jnp.transpose(w_out.astype(jnp.bfloat16)),
        jnp.transpose(w_gateup.astype(jnp.bfloat16), (1, 0, 2)).reshape(w_gateup.shape[1], -1),
        jnp.transpose(w_down.astype(jnp.bfloat16)),
    ]
    widths = [p.shape[1] for p in pieces]
    offsets = [sum(widths[:i]) for i in range(len(widths) + 1)]
    attn_full = gather_rows(jnp.concatenate(pieces[:3], axis=1))
    ffn_full = lax.all_gather(jnp.concatenate(pieces[3:], axis=1), ROWPAGE, axis=0, tiled=True)
    qkv_w = attn_full[:, offsets[0] : offsets[2]]
    out_t = attn_full[:, offsets[2] : offsets[3]]
    gateup_w = ffn_full[:, : offsets[4] - offsets[3]]
    down_t = ffn_full[:, offsets[4] - offsets[3] :]

    prompt_count, seq_len, local_feat = tokens.shape
    xx_count = lax.axis_size("xx")
    zh_count = lax.axis_size("zh")
    gathered = gather_col(tokens)
    attn_in = normalize_blocks(gathered.astype(jnp.float32), attn_gain).astype(jnp.bfloat16)
    projected = project_blocks(attn_in, qkv_w)
    projected = projected.reshape(prompt_count, seq_len, local_heads + 2, head_dim)
    queries = rotate(normalize(projected[:, :, :local_heads], query_gain)).astype(jnp.bfloat16)
    keys_one = rotate(normalize(projected[:, :, local_heads : local_heads + 1], key_gain)).astype(
        jnp.bfloat16
    )
    values_one = projected[:, :, local_heads + 1 : local_heads + 2].astype(jnp.bfloat16)
    keys_rot = jnp.broadcast_to(keys_one, queries.shape)
    values_in = jnp.broadcast_to(values_one, queries.shape)
    attended = jnp.stack(
        [
            attend(queries[i], keys_rot[i], values_in[i], lengths[i]).reshape(seq_len, local_width)
            for i in range(prompt_count)
        ]
    )
    incoming = send_pages(keys_rot, values_in, lengths, page_slot)
    incoming, attended = lax.optimization_barrier((incoming, attended))
    attn_terms = terms_blocks(attended, out_t, xx_count, zh_count).astype(jnp.bfloat16)
    attn_sum = scatter_sum_col(attn_terms)
    residual = (tokens.astype(jnp.float32) + attn_sum).astype(jnp.bfloat16)
    residual_all = gather_col(residual)
    ffn_in = normalize_blocks(residual_all.astype(jnp.float32), ffn_gain).astype(jnp.bfloat16)
    gate_up = project_blocks(ffn_in, gateup_w)
    hidden = (jax.nn.silu(gate_up[..., :unit_count]) * gate_up[..., unit_count:]).astype(jnp.bfloat16)
    ffn_terms = terms_blocks(hidden, down_t, xx_count, zh_count)
    ffn_sum = scatter_sum_col(ffn_terms.astype(jnp.bfloat16))
    layer_out = (residual.astype(jnp.float32) + ffn_sum).astype(jnp.bfloat16)
    page_index = lax.axis_index("page")
    page_count = lax.axis_size("page")
    blocks_each = prompt_count * (seq_len // PAGE_LEN)
    capacity = blocks_each // page_count
    owners = page_slot // blocks_each
    local_slot = page_slot % blocks_each
    same_owner = owners[:, :, None] == owners[:, None, :]
    earlier = (
        jnp.arange(blocks_each, dtype=jnp.int32)[None, :]
        < jnp.arange(blocks_each, dtype=jnp.int32)[:, None]
    )
    order_in = jnp.sum((same_owner & earlier[None]).astype(jnp.int32), axis=2)
    arrival_hit = (owners[:, None, :] == page_index) & (
        order_in[:, None, :] == jnp.arange(capacity, dtype=jnp.int32)[None, :, None]
    )
    arrival_slot = jnp.sum(jnp.where(arrival_hit, local_slot[:, None, :], 0), axis=2).reshape(
        blocks_each
    )
    kv_pages = jnp.zeros_like(incoming).at[:, arrival_slot].set(incoming)
    return (layer_out, kv_pages)


def solution(mesh):
    in_specs = (
        P(ROWPAGE, None, COL),
        P(ROWPAGE),
        P(ROW, None),
        P(ROWPAGE, COL),
        P(None, ROWPAGE, None),
        P(COL, ROWPAGE),
        P(None, ROWPAGE, COL),
        P(COL, ROWPAGE),
        P(),
        P(),
        P(),
        P(),
    )
    out_specs = (P(ROWPAGE, None, COL), P(None, ROWPAGE, None, COL))
    fine = Mesh(
        mesh.devices.reshape(
            mesh.shape["row"] // 2, 2, 2, mesh.shape["col"] // 2, mesh.shape["page"]
        ),
        ("ry", "rc", "zh", "xx", "page"),
    )
    return jax.shard_map(
        on_device, mesh=fine, in_specs=in_specs, out_specs=out_specs, check_vma=False
    )
```

```python
import jax
import jax.numpy as jnp
from jax import lax
from jax.sharding import Mesh, PartitionSpec as P

PAGE_LEN = 128
ROW = ("ry", "rc")
COL = ("zh", "xx")
ROWPAGE = ("ry", "rc", "page")


def normalize(values, norm_gain):
    mean_sq = jnp.mean(values * values, axis=-1, keepdims=True)
    return values * lax.rsqrt(mean_sq + 1e-06) * norm_gain


def rotate(values):
    row_count = values.shape[-3]
    head_dim = values.shape[-1]
    half_dim = head_dim // 2
    frequency = 10000.0 ** (-2.0 * jnp.arange(half_dim, dtype=jnp.float32) / head_dim)
    angles = jnp.arange(row_count, dtype=jnp.float32)[:, None] * frequency[None, :]
    cosine = jnp.cos(angles)[:, None, :]
    sine_table = jnp.sin(angles)[:, None, :]
    leading = values[..., :half_dim]
    trailing = values[..., half_dim:]
    return jnp.concatenate(
        [leading * cosine - trailing * sine_table, trailing * cosine + leading * sine_table],
        axis=-1,
    )


def attend(query_rows, key_rows, value_rows, length):
    row_count = query_rows.shape[0]
    scores = jnp.einsum(
        "qhd,khd->hqk", query_rows, key_rows, preferred_element_type=jnp.float32
    ) * query_rows.shape[2] ** (-0.5)
    positions = jnp.arange(row_count, dtype=jnp.int32)
    seen_keys = (positions[None, :] <= positions[:, None]) & (positions[None, :] < length)
    exp_scores = jnp.where(seen_keys[None], jnp.exp(scores), 0.0)
    attn_probs = (exp_scores / jnp.sum(exp_scores, axis=-1, keepdims=True)).astype(jnp.bfloat16)
    attended = jnp.einsum(
        "hqk,khd->qhd", attn_probs, value_rows, preferred_element_type=jnp.float32
    )
    live_rows = (positions < length)[:, None, None]
    return jnp.where(live_rows, attended, 0.0).astype(jnp.bfloat16)


def contract_rows(lhs, rhs_t):
    return lax.dot_general(
        lhs, rhs_t, (((1,), (1,)), ((), ())), preferred_element_type=jnp.float32
    )


def gather_a2a(x, axis_name, axis):
    count = lax.axis_size(axis_name)
    copies = jnp.broadcast_to(x[None], (count,) + x.shape)
    got = lax.all_to_all(copies, axis_name, 0, 0, tiled=True)
    got = jnp.moveaxis(got, 0, axis)
    shape = list(x.shape)
    shape[axis] *= count
    return got.reshape(shape)


def scatter_sum_a2a(x, axis_name, axis):
    count = lax.axis_size(axis_name)
    shape = list(x.shape)
    split = shape[:axis] + [count, shape[axis] // count] + shape[axis + 1 :]
    got = lax.all_to_all(x.reshape(split), axis_name, axis, axis, tiled=True)
    return jnp.sum(got.astype(jnp.float32), axis=axis)


def swap_halves(x):
    return lax.ppermute(x, "zh", [(0, 1), (1, 0)])


def gather_col(x):
    half = lax.axis_index("zh")
    other = swap_halves(x)
    pair = jnp.stack([jnp.where(half == 0, x, other), jnp.where(half == 0, other, x)])
    count = lax.axis_size("xx")
    copies = jnp.broadcast_to(pair[None], (count,) + pair.shape)
    return lax.all_to_all(copies, "xx", 0, 0, tiled=True)


def scatter_sum_col(terms):
    got = lax.all_to_all(terms, "xx", 0, 0, tiled=True)
    part = jnp.sum(got.astype(jnp.float32), axis=0)
    half = lax.axis_index("zh")
    mine = jnp.take(part, half, axis=-2)
    theirs = swap_halves(jnp.take(part, 1 - half, axis=-2).astype(jnp.bfloat16))
    return mine + theirs.astype(jnp.float32)


def normalize_blocks(values, norm_gain):
    xx_count, zh_count = values.shape[0], values.shape[1]
    gain = jnp.swapaxes(norm_gain.reshape(zh_count, xx_count, -1), 0, 1)[:, :, None, None, :]
    mean_sq = jnp.mean(values * values, axis=(0, 1, 4), keepdims=True)
    return values * lax.rsqrt(mean_sq + 1e-06) * gain


def project_blocks(values, weights):
    xx_count, zh_count, block = values.shape[0], values.shape[1], values.shape[4]
    w = weights.reshape(zh_count, xx_count, block, -1)
    return jnp.einsum("xzpse,zxen->psn", values, w, preferred_element_type=jnp.float32)


def terms_blocks(values, weights_t, xx_count, zh_count):
    w = weights_t.reshape(zh_count, xx_count, -1, weights_t.shape[1])
    return jnp.einsum("psk,zxek->xpsze", values, w, preferred_element_type=jnp.float32)


def gather_rows(x):
    pages = lax.axis_size("page")
    got = lax.all_to_all(jnp.broadcast_to(x[None], (pages,) + x.shape), "page", 0, 0, tiled=True)
    got = got.reshape((-1,) + x.shape[1:])
    chips = lax.axis_size("ry")
    got = lax.all_to_all(jnp.broadcast_to(got[None], (chips,) + got.shape), "ry", 0, 0, tiled=True)
    cores = lax.axis_size("rc")
    got = jnp.broadcast_to(got[:, None], (chips, cores) + got.shape[1:])
    got = lax.all_to_all(got, "rc", 1, 1, tiled=True)
    return got.reshape((-1,) + x.shape[1:])


def send_pages(keys_rot, values_in, lengths, page_slot):
    prompt_count, seq_len, local_heads, head_dim = keys_rot.shape
    local_width = local_heads * head_dim
    page_count = lax.axis_size("page")
    page_index = lax.axis_index("page")
    blocks_each = prompt_count * (seq_len // PAGE_LEN)
    capacity = blocks_each // page_count
    owners = page_slot // blocks_each
    local_slot = page_slot % blocks_each
    same_owner = owners[:, :, None] == owners[:, None, :]
    earlier = (
        jnp.arange(blocks_each, dtype=jnp.int32)[None, :]
        < jnp.arange(blocks_each, dtype=jnp.int32)[:, None]
    )
    order_in = jnp.sum((same_owner & earlier[None]).astype(jnp.int32), axis=2)
    my_owners = lax.dynamic_index_in_dim(owners, page_index, 0, keepdims=False)
    my_order = lax.dynamic_index_in_dim(order_in, page_index, 0, keepdims=False)
    send_pos = my_owners * capacity + my_order
    live_rows = (jnp.arange(seq_len, dtype=jnp.int32)[None, :] < lengths[:, None])[:, :, None, None]
    page_keys = jnp.where(live_rows, keys_rot, jnp.zeros_like(keys_rot)).reshape(
        blocks_each, PAGE_LEN, local_width
    )
    page_values = jnp.where(live_rows, values_in, jnp.zeros_like(values_in)).reshape(
        blocks_each, PAGE_LEN, local_width
    )
    stacked = jnp.stack([page_keys, page_values])
    outgoing = jnp.zeros_like(stacked).at[:, send_pos].set(stacked)
    incoming = lax.all_to_all(outgoing, "page", split_axis=1, concat_axis=1, tiled=True)
    return incoming


def on_device(
    tokens,
    lengths,
    page_slot,
    w_query,
    w_keyval,
    w_out,
    w_gateup,
    w_down,
    attn_gain,
    ffn_gain,
    query_gain,
    key_gain,
):
    col_count = lax.axis_size(COL)
    col_index = lax.axis_index(COL)
    head_dim = query_gain.shape[0]
    local_width = w_query.shape[1]
    local_heads = local_width // head_dim
    kv_heads = w_keyval.shape[2] // head_dim
    group_size = local_heads * col_count // kv_heads
    assert group_size % local_heads == 0
    kv_head = (col_index * local_heads) // group_size
    unit_count = w_gateup.shape[2]
    kv_piece = lax.dynamic_slice_in_dim(w_keyval, kv_head * head_dim, head_dim, axis=2)
    pieces = [
        w_query.astype(jnp.bfloat16),
        jnp.transpose(kv_piece.astype(jnp.bfloat16), (1, 0, 2)).reshape(kv_piece.shape[1], -1),
        jnp.transpose(w_out.astype(jnp.bfloat16)),
        jnp.transpose(w_gateup.astype(jnp.bfloat16), (1, 0, 2)).reshape(w_gateup.shape[1], -1),
        jnp.transpose(w_down.astype(jnp.bfloat16)),
    ]
    widths = [p.shape[1] for p in pieces]
    offsets = [sum(widths[:i]) for i in range(len(widths) + 1)]
    attn_full = gather_rows(jnp.concatenate(pieces[:3], axis=1))
    ffn_full = lax.all_gather(jnp.concatenate(pieces[3:], axis=1), ROWPAGE, axis=0, tiled=True)
    qkv_w = attn_full[:, offsets[0] : offsets[2]]
    out_t = attn_full[:, offsets[2] : offsets[3]]
    gateup_w = ffn_full[:, : offsets[4] - offsets[3]]
    down_t = ffn_full[:, offsets[4] - offsets[3] :]

    prompt_count, seq_len, local_feat = tokens.shape
    xx_count = lax.axis_size("xx")
    zh_count = lax.axis_size("zh")
    gathered = gather_col(tokens)
    attn_in = normalize_blocks(gathered.astype(jnp.float32), attn_gain).astype(jnp.bfloat16)
    projected = project_blocks(attn_in, qkv_w)
    projected = projected.reshape(prompt_count, seq_len, local_heads + 2, head_dim)
    queries = rotate(normalize(projected[:, :, :local_heads], query_gain)).astype(jnp.bfloat16)
    keys_one = rotate(normalize(projected[:, :, local_heads : local_heads + 1], key_gain)).astype(
        jnp.bfloat16
    )
    values_one = projected[:, :, local_heads + 1 : local_heads + 2].astype(jnp.bfloat16)
    keys_rot = jnp.broadcast_to(keys_one, queries.shape)
    values_in = jnp.broadcast_to(values_one, queries.shape)
    attended = jnp.stack(
        [
            attend(queries[i], keys_rot[i], values_in[i], lengths[i]).reshape(seq_len, local_width)
            for i in range(prompt_count)
        ]
    )
    incoming = send_pages(keys_rot, values_in, lengths, page_slot)
    attn_terms = terms_blocks(attended, out_t, xx_count, zh_count).astype(jnp.bfloat16)
    attn_sum = scatter_sum_col(attn_terms)
    residual = (tokens.astype(jnp.float32) + attn_sum).astype(jnp.bfloat16)
    incoming, residual = lax.optimization_barrier((incoming, residual))
    residual_all = gather_col(residual)
    ffn_in = normalize_blocks(residual_all.astype(jnp.float32), ffn_gain).astype(jnp.bfloat16)
    gate_up = project_blocks(ffn_in, gateup_w)
    hidden = (jax.nn.silu(gate_up[..., :unit_count]) * gate_up[..., unit_count:]).astype(jnp.bfloat16)
    ffn_terms = terms_blocks(hidden, down_t, xx_count, zh_count)
    ffn_sum = scatter_sum_col(ffn_terms.astype(jnp.bfloat16))
    layer_out = (residual.astype(jnp.float32) + ffn_sum).astype(jnp.bfloat16)
    page_index = lax.axis_index("page")
    page_count = lax.axis_size("page")
    blocks_each = prompt_count * (seq_len // PAGE_LEN)
    capacity = blocks_each // page_count
    owners = page_slot // blocks_each
    local_slot = page_slot % blocks_each
    same_owner = owners[:, :, None] == owners[:, None, :]
    earlier = (
        jnp.arange(blocks_each, dtype=jnp.int32)[None, :]
        < jnp.arange(blocks_each, dtype=jnp.int32)[:, None]
    )
    order_in = jnp.sum((same_owner & earlier[None]).astype(jnp.int32), axis=2)
    arrival_hit = (owners[:, None, :] == page_index) & (
        order_in[:, None, :] == jnp.arange(capacity, dtype=jnp.int32)[None, :, None]
    )
    arrival_slot = jnp.sum(jnp.where(arrival_hit, local_slot[:, None, :], 0), axis=2).reshape(
        blocks_each
    )
    kv_pages = jnp.zeros_like(incoming).at[:, arrival_slot].set(incoming)
    return (layer_out, kv_pages)


def solution(mesh):
    in_specs = (
        P(ROWPAGE, None, COL),
        P(ROWPAGE),
        P(ROW, None),
        P(ROWPAGE, COL),
        P(None, ROWPAGE, None),
        P(COL, ROWPAGE),
        P(None, ROWPAGE, COL),
        P(COL, ROWPAGE),
        P(),
        P(),
        P(),
        P(),
    )
    out_specs = (P(ROWPAGE, None, COL), P(None, ROWPAGE, None, COL))
    fine = Mesh(
        mesh.devices.reshape(
            mesh.shape["row"] // 2, 2, 2, mesh.shape["col"] // 2, mesh.shape["page"]
        ),
        ("ry", "rc", "zh", "xx", "page"),
    )
    return jax.shard_map(
        on_device, mesh=fine, in_specs=in_specs, out_specs=out_specs, check_vma=False
    )
```

```python
import jax
import jax.numpy as jnp
from jax import lax
from jax.sharding import Mesh, PartitionSpec as P

PAGE_LEN = 128
ROW = ("ry", "rc")
COL = ("zh", "xx")
ROWPAGE = ("ry", "rc", "page")


def normalize(values, norm_gain):
    mean_sq = jnp.mean(values * values, axis=-1, keepdims=True)
    return values * lax.rsqrt(mean_sq + 1e-06) * norm_gain


def rotate(values):
    row_count = values.shape[-3]
    head_dim = values.shape[-1]
    half_dim = head_dim // 2
    frequency = 10000.0 ** (-2.0 * jnp.arange(half_dim, dtype=jnp.float32) / head_dim)
    angles = jnp.arange(row_count, dtype=jnp.float32)[:, None] * frequency[None, :]
    cosine = jnp.cos(angles)[:, None, :]
    sine_table = jnp.sin(angles)[:, None, :]
    leading = values[..., :half_dim]
    trailing = values[..., half_dim:]
    return jnp.concatenate(
        [leading * cosine - trailing * sine_table, trailing * cosine + leading * sine_table],
        axis=-1,
    )


def attend(query_rows, key_rows, value_rows, length):
    row_count = query_rows.shape[0]
    scores = jnp.einsum(
        "qhd,khd->hqk", query_rows, key_rows, preferred_element_type=jnp.float32
    ) * query_rows.shape[2] ** (-0.5)
    positions = jnp.arange(row_count, dtype=jnp.int32)
    seen_keys = (positions[None, :] <= positions[:, None]) & (positions[None, :] < length)
    exp_scores = jnp.where(seen_keys[None], jnp.exp(scores), 0.0)
    attn_probs = (exp_scores / jnp.sum(exp_scores, axis=-1, keepdims=True)).astype(jnp.bfloat16)
    attended = jnp.einsum(
        "hqk,khd->qhd", attn_probs, value_rows, preferred_element_type=jnp.float32
    )
    live_rows = (positions < length)[:, None, None]
    return jnp.where(live_rows, attended, 0.0).astype(jnp.bfloat16)


def contract_rows(lhs, rhs_t):
    return lax.dot_general(
        lhs, rhs_t, (((1,), (1,)), ((), ())), preferred_element_type=jnp.float32
    )


def gather_a2a(x, axis_name, axis):
    count = lax.axis_size(axis_name)
    copies = jnp.broadcast_to(x[None], (count,) + x.shape)
    got = lax.all_to_all(copies, axis_name, 0, 0, tiled=True)
    got = jnp.moveaxis(got, 0, axis)
    shape = list(x.shape)
    shape[axis] *= count
    return got.reshape(shape)


def scatter_sum_a2a(x, axis_name, axis):
    count = lax.axis_size(axis_name)
    shape = list(x.shape)
    split = shape[:axis] + [count, shape[axis] // count] + shape[axis + 1 :]
    got = lax.all_to_all(x.reshape(split), axis_name, axis, axis, tiled=True)
    return jnp.sum(got.astype(jnp.float32), axis=axis)


def swap_halves(x):
    return lax.ppermute(x, "zh", [(0, 1), (1, 0)])


def gather_col(x):
    half = lax.axis_index("zh")
    other = swap_halves(x)
    pair = jnp.stack([jnp.where(half == 0, x, other), jnp.where(half == 0, other, x)])
    count = lax.axis_size("xx")
    copies = jnp.broadcast_to(pair[None], (count,) + pair.shape)
    return lax.all_to_all(copies, "xx", 0, 0, tiled=True)


def scatter_sum_col(terms):
    got = lax.all_to_all(terms, "xx", 0, 0, tiled=True)
    part = jnp.sum(got.astype(jnp.float32), axis=0)
    half = lax.axis_index("zh")
    mine = jnp.take(part, half, axis=-2)
    theirs = swap_halves(jnp.take(part, 1 - half, axis=-2).astype(jnp.bfloat16))
    return mine + theirs.astype(jnp.float32)


def normalize_blocks(values, norm_gain):
    xx_count, zh_count = values.shape[0], values.shape[1]
    gain = jnp.swapaxes(norm_gain.reshape(zh_count, xx_count, -1), 0, 1)[:, :, None, None, :]
    mean_sq = jnp.mean(values * values, axis=(0, 1, 4), keepdims=True)
    return values * lax.rsqrt(mean_sq + 1e-06) * gain


def project_blocks(values, weights):
    xx_count, zh_count, block = values.shape[0], values.shape[1], values.shape[4]
    w = weights.reshape(zh_count, xx_count, block, -1)
    return jnp.einsum("xzpse,zxen->psn", values, w, preferred_element_type=jnp.float32)


def terms_blocks(values, weights_t, xx_count, zh_count):
    w = weights_t.reshape(zh_count, xx_count, -1, weights_t.shape[1])
    return jnp.einsum("psk,zxek->xpsze", values, w, preferred_element_type=jnp.float32)


def gather_rows(x):
    pages = lax.axis_size("page")
    got = lax.all_to_all(jnp.broadcast_to(x[None], (pages,) + x.shape), "page", 0, 0, tiled=True)
    got = got.reshape((-1,) + x.shape[1:])
    chips = lax.axis_size("ry")
    got = lax.all_to_all(jnp.broadcast_to(got[None], (chips,) + got.shape), "ry", 0, 0, tiled=True)
    core = lax.axis_index("rc")
    other = lax.ppermute(got, "rc", [(0, 1), (1, 0)])
    got = jnp.stack([jnp.where(core == 0, got, other), jnp.where(core == 0, other, got)], axis=1)
    return got.reshape((-1,) + x.shape[1:])


def send_pages(keys_rot, values_in, lengths, page_slot):
    prompt_count, seq_len, local_heads, head_dim = keys_rot.shape
    local_width = local_heads * head_dim
    page_count = lax.axis_size("page")
    page_index = lax.axis_index("page")
    blocks_each = prompt_count * (seq_len // PAGE_LEN)
    capacity = blocks_each // page_count
    owners = page_slot // blocks_each
    local_slot = page_slot % blocks_each
    same_owner = owners[:, :, None] == owners[:, None, :]
    earlier = (
        jnp.arange(blocks_each, dtype=jnp.int32)[None, :]
        < jnp.arange(blocks_each, dtype=jnp.int32)[:, None]
    )
    order_in = jnp.sum((same_owner & earlier[None]).astype(jnp.int32), axis=2)
    my_owners = lax.dynamic_index_in_dim(owners, page_index, 0, keepdims=False)
    my_order = lax.dynamic_index_in_dim(order_in, page_index, 0, keepdims=False)
    send_pos = my_owners * capacity + my_order
    live_rows = (jnp.arange(seq_len, dtype=jnp.int32)[None, :] < lengths[:, None])[:, :, None, None]
    page_keys = jnp.where(live_rows, keys_rot, jnp.zeros_like(keys_rot)).reshape(
        blocks_each, PAGE_LEN, local_width
    )
    page_values = jnp.where(live_rows, values_in, jnp.zeros_like(values_in)).reshape(
        blocks_each, PAGE_LEN, local_width
    )
    stacked = jnp.stack([page_keys, page_values])
    outgoing = jnp.zeros_like(stacked).at[:, send_pos].set(stacked)
    incoming = lax.all_to_all(outgoing, "page", split_axis=1, concat_axis=1, tiled=True)
    return incoming


def on_device(
    tokens,
    lengths,
    page_slot,
    w_query,
    w_keyval,
    w_out,
    w_gateup,
    w_down,
    attn_gain,
    ffn_gain,
    query_gain,
    key_gain,
):
    col_count = lax.axis_size(COL)
    col_index = lax.axis_index(COL)
    head_dim = query_gain.shape[0]
    local_width = w_query.shape[1]
    local_heads = local_width // head_dim
    kv_heads = w_keyval.shape[2] // head_dim
    group_size = local_heads * col_count // kv_heads
    assert group_size % local_heads == 0
    kv_head = (col_index * local_heads) // group_size
    unit_count = w_gateup.shape[2]
    kv_piece = lax.dynamic_slice_in_dim(w_keyval, kv_head * head_dim, head_dim, axis=2)
    pieces = [
        w_query.astype(jnp.bfloat16),
        jnp.transpose(kv_piece.astype(jnp.bfloat16), (1, 0, 2)).reshape(kv_piece.shape[1], -1),
        jnp.transpose(w_out.astype(jnp.bfloat16)),
        jnp.transpose(w_gateup.astype(jnp.bfloat16), (1, 0, 2)).reshape(w_gateup.shape[1], -1),
        jnp.transpose(w_down.astype(jnp.bfloat16)),
    ]
    widths = [p.shape[1] for p in pieces]
    offsets = [sum(widths[:i]) for i in range(len(widths) + 1)]
    attn_full = gather_rows(jnp.concatenate(pieces[:3], axis=1))
    ffn_full = lax.all_gather(jnp.concatenate(pieces[3:], axis=1), ROWPAGE, axis=0, tiled=True)
    qkv_w = attn_full[:, offsets[0] : offsets[2]]
    out_t = attn_full[:, offsets[2] : offsets[3]]
    gateup_w = ffn_full[:, : offsets[4] - offsets[3]]
    down_t = ffn_full[:, offsets[4] - offsets[3] :]

    prompt_count, seq_len, local_feat = tokens.shape
    xx_count = lax.axis_size("xx")
    zh_count = lax.axis_size("zh")
    gathered = gather_col(tokens)
    attn_in = normalize_blocks(gathered.astype(jnp.float32), attn_gain).astype(jnp.bfloat16)
    projected = project_blocks(attn_in, qkv_w)
    projected = projected.reshape(prompt_count, seq_len, local_heads + 2, head_dim)
    queries = rotate(normalize(projected[:, :, :local_heads], query_gain)).astype(jnp.bfloat16)
    keys_one = rotate(normalize(projected[:, :, local_heads : local_heads + 1], key_gain)).astype(
        jnp.bfloat16
    )
    values_one = projected[:, :, local_heads + 1 : local_heads + 2].astype(jnp.bfloat16)
    keys_rot = jnp.broadcast_to(keys_one, queries.shape)
    values_in = jnp.broadcast_to(values_one, queries.shape)
    attended = jnp.stack(
        [
            attend(queries[i], keys_rot[i], values_in[i], lengths[i]).reshape(seq_len, local_width)
            for i in range(prompt_count)
        ]
    )
    incoming = send_pages(keys_rot, values_in, lengths, page_slot)
    attn_terms = terms_blocks(attended, out_t, xx_count, zh_count).astype(jnp.bfloat16)
    attn_sum = scatter_sum_col(attn_terms)
    residual = (tokens.astype(jnp.float32) + attn_sum).astype(jnp.bfloat16)
    incoming, residual = lax.optimization_barrier((incoming, residual))
    residual_all = gather_col(residual)
    ffn_in = normalize_blocks(residual_all.astype(jnp.float32), ffn_gain).astype(jnp.bfloat16)
    gate_up = project_blocks(ffn_in, gateup_w)
    hidden = (jax.nn.silu(gate_up[..., :unit_count]) * gate_up[..., unit_count:]).astype(jnp.bfloat16)
    ffn_terms = terms_blocks(hidden, down_t, xx_count, zh_count)
    ffn_sum = scatter_sum_col(ffn_terms.astype(jnp.bfloat16))
    layer_out = (residual.astype(jnp.float32) + ffn_sum).astype(jnp.bfloat16)
    page_index = lax.axis_index("page")
    page_count = lax.axis_size("page")
    blocks_each = prompt_count * (seq_len // PAGE_LEN)
    capacity = blocks_each // page_count
    owners = page_slot // blocks_each
    local_slot = page_slot % blocks_each
    same_owner = owners[:, :, None] == owners[:, None, :]
    earlier = (
        jnp.arange(blocks_each, dtype=jnp.int32)[None, :]
        < jnp.arange(blocks_each, dtype=jnp.int32)[:, None]
    )
    order_in = jnp.sum((same_owner & earlier[None]).astype(jnp.int32), axis=2)
    arrival_hit = (owners[:, None, :] == page_index) & (
        order_in[:, None, :] == jnp.arange(capacity, dtype=jnp.int32)[None, :, None]
    )
    arrival_slot = jnp.sum(jnp.where(arrival_hit, local_slot[:, None, :], 0), axis=2).reshape(
        blocks_each
    )
    kv_pages = jnp.zeros_like(incoming).at[:, arrival_slot].set(incoming)
    return (layer_out, kv_pages)


def solution(mesh):
    in_specs = (
        P(ROWPAGE, None, COL),
        P(ROWPAGE),
        P(ROW, None),
        P(ROWPAGE, COL),
        P(None, ROWPAGE, None),
        P(COL, ROWPAGE),
        P(None, ROWPAGE, COL),
        P(COL, ROWPAGE),
        P(),
        P(),
        P(),
        P(),
    )
    out_specs = (P(ROWPAGE, None, COL), P(None, ROWPAGE, None, COL))
    fine = Mesh(
        mesh.devices.reshape(
            mesh.shape["row"] // 2, 2, 2, mesh.shape["col"] // 2, mesh.shape["page"]
        ),
        ("ry", "rc", "zh", "xx", "page"),
    )
    return jax.shard_map(
        on_device, mesh=fine, in_specs=in_specs, out_specs=out_specs, check_vma=False
    )
```

```python
import jax
import jax.numpy as jnp
from jax import lax
from jax.sharding import Mesh, PartitionSpec as P

PAGE_LEN = 128
ROW = ("ry", "rc")
COL = ("zh", "xx")
ROWPAGE = ("ry", "rc", "page")


def normalize(values, norm_gain):
    mean_sq = jnp.mean(values * values, axis=-1, keepdims=True)
    return values * lax.rsqrt(mean_sq + 1e-06) * norm_gain


def rotate(values):
    row_count = values.shape[-3]
    head_dim = values.shape[-1]
    half_dim = head_dim // 2
    frequency = 10000.0 ** (-2.0 * jnp.arange(half_dim, dtype=jnp.float32) / head_dim)
    angles = jnp.arange(row_count, dtype=jnp.float32)[:, None] * frequency[None, :]
    cosine = jnp.cos(angles)[:, None, :]
    sine_table = jnp.sin(angles)[:, None, :]
    leading = values[..., :half_dim]
    trailing = values[..., half_dim:]
    return jnp.concatenate(
        [leading * cosine - trailing * sine_table, trailing * cosine + leading * sine_table],
        axis=-1,
    )


def attend(query_rows, key_rows, value_rows, length):
    row_count = query_rows.shape[0]
    scores = jnp.einsum(
        "qhd,khd->hqk", query_rows, key_rows, preferred_element_type=jnp.float32
    ) * query_rows.shape[2] ** (-0.5)
    positions = jnp.arange(row_count, dtype=jnp.int32)
    seen_keys = (positions[None, :] <= positions[:, None]) & (positions[None, :] < length)
    exp_scores = jnp.where(seen_keys[None], jnp.exp(scores), 0.0)
    attn_probs = (exp_scores / jnp.sum(exp_scores, axis=-1, keepdims=True)).astype(jnp.bfloat16)
    attended = jnp.einsum(
        "hqk,khd->qhd", attn_probs, value_rows, preferred_element_type=jnp.float32
    )
    live_rows = (positions < length)[:, None, None]
    return jnp.where(live_rows, attended, 0.0).astype(jnp.bfloat16)


def contract_rows(lhs, rhs_t):
    return lax.dot_general(
        lhs, rhs_t, (((1,), (1,)), ((), ())), preferred_element_type=jnp.float32
    )


def gather_a2a(x, axis_name, axis):
    count = lax.axis_size(axis_name)
    copies = jnp.broadcast_to(x[None], (count,) + x.shape)
    got = lax.all_to_all(copies, axis_name, 0, 0, tiled=True)
    got = jnp.moveaxis(got, 0, axis)
    shape = list(x.shape)
    shape[axis] *= count
    return got.reshape(shape)


def scatter_sum_a2a(x, axis_name, axis):
    count = lax.axis_size(axis_name)
    shape = list(x.shape)
    split = shape[:axis] + [count, shape[axis] // count] + shape[axis + 1 :]
    got = lax.all_to_all(x.reshape(split), axis_name, axis, axis, tiled=True)
    return jnp.sum(got.astype(jnp.float32), axis=axis)


def swap_halves(x):
    return lax.ppermute(x, "zh", [(0, 1), (1, 0)])


def gather_col(x):
    half = lax.axis_index("zh")
    other = swap_halves(x)
    pair = jnp.stack([jnp.where(half == 0, x, other), jnp.where(half == 0, other, x)])
    count = lax.axis_size("xx")
    copies = jnp.broadcast_to(pair[None], (count,) + pair.shape)
    return lax.all_to_all(copies, "xx", 0, 0, tiled=True)


def scatter_sum_col(terms):
    got = lax.all_to_all(terms, "xx", 0, 0, tiled=True)
    part = jnp.sum(got.astype(jnp.float32), axis=0)
    half = lax.axis_index("zh")
    mine = jnp.take(part, half, axis=-2)
    theirs = swap_halves(jnp.take(part, 1 - half, axis=-2).astype(jnp.bfloat16))
    return mine + theirs.astype(jnp.float32)


def normalize_blocks(values, norm_gain):
    xx_count, zh_count = values.shape[0], values.shape[1]
    gain = jnp.swapaxes(norm_gain.reshape(zh_count, xx_count, -1), 0, 1)[:, :, None, None, :]
    mean_sq = jnp.mean(values * values, axis=(0, 1, 4), keepdims=True)
    return values * lax.rsqrt(mean_sq + 1e-06) * gain


def project_blocks(values, weights):
    xx_count, zh_count, block = values.shape[0], values.shape[1], values.shape[4]
    w = weights.reshape(zh_count, xx_count, block, -1)
    return jnp.einsum("xzpse,zxen->psn", values, w, preferred_element_type=jnp.float32)


def terms_blocks(values, weights_t, xx_count, zh_count):
    w = weights_t.reshape(zh_count, xx_count, -1, weights_t.shape[1])
    return jnp.einsum("psk,zxek->xpsze", values, w, preferred_element_type=jnp.float32)


def gather_rows(x):
    pages = lax.axis_size("page")
    got = lax.all_to_all(jnp.broadcast_to(x[None], (pages,) + x.shape), "page", 0, 0, tiled=True)
    got = got.reshape((-1,) + x.shape[1:])
    chips = lax.axis_size("ry")
    chip = lax.axis_index("ry")
    shifted = [got] + [
        lax.ppermute(got, "ry", [(i, (i + k) % chips) for i in range(chips)]) for k in range(1, chips)
    ]
    source_shift = (chip - jnp.arange(chips, dtype=jnp.int32)) % chips
    got = jnp.take(jnp.stack(shifted), source_shift, axis=0)
    core = lax.axis_index("rc")
    other = lax.ppermute(got, "rc", [(0, 1), (1, 0)])
    got = jnp.stack([jnp.where(core == 0, got, other), jnp.where(core == 0, other, got)], axis=1)
    return got.reshape((-1,) + x.shape[1:])


def send_pages(keys_rot, values_in, lengths, page_slot):
    prompt_count, seq_len, local_heads, head_dim = keys_rot.shape
    local_width = local_heads * head_dim
    page_count = lax.axis_size("page")
    page_index = lax.axis_index("page")
    blocks_each = prompt_count * (seq_len // PAGE_LEN)
    capacity = blocks_each // page_count
    owners = page_slot // blocks_each
    local_slot = page_slot % blocks_each
    same_owner = owners[:, :, None] == owners[:, None, :]
    earlier = (
        jnp.arange(blocks_each, dtype=jnp.int32)[None, :]
        < jnp.arange(blocks_each, dtype=jnp.int32)[:, None]
    )
    order_in = jnp.sum((same_owner & earlier[None]).astype(jnp.int32), axis=2)
    my_owners = lax.dynamic_index_in_dim(owners, page_index, 0, keepdims=False)
    my_order = lax.dynamic_index_in_dim(order_in, page_index, 0, keepdims=False)
    send_pos = my_owners * capacity + my_order
    live_rows = (jnp.arange(seq_len, dtype=jnp.int32)[None, :] < lengths[:, None])[:, :, None, None]
    page_keys = jnp.where(live_rows, keys_rot, jnp.zeros_like(keys_rot)).reshape(
        blocks_each, PAGE_LEN, local_width
    )
    page_values = jnp.where(live_rows, values_in, jnp.zeros_like(values_in)).reshape(
        blocks_each, PAGE_LEN, local_width
    )
    stacked = jnp.stack([page_keys, page_values])
    outgoing = jnp.zeros_like(stacked).at[:, send_pos].set(stacked)
    incoming = lax.all_to_all(outgoing, "page", split_axis=1, concat_axis=1, tiled=True)
    return incoming


def on_device(
    tokens,
    lengths,
    page_slot,
    w_query,
    w_keyval,
    w_out,
    w_gateup,
    w_down,
    attn_gain,
    ffn_gain,
    query_gain,
    key_gain,
):
    col_count = lax.axis_size(COL)
    col_index = lax.axis_index(COL)
    head_dim = query_gain.shape[0]
    local_width = w_query.shape[1]
    local_heads = local_width // head_dim
    kv_heads = w_keyval.shape[2] // head_dim
    group_size = local_heads * col_count // kv_heads
    assert group_size % local_heads == 0
    kv_head = (col_index * local_heads) // group_size
    unit_count = w_gateup.shape[2]
    kv_piece = lax.dynamic_slice_in_dim(w_keyval, kv_head * head_dim, head_dim, axis=2)
    pieces = [
        w_query.astype(jnp.bfloat16),
        jnp.transpose(kv_piece.astype(jnp.bfloat16), (1, 0, 2)).reshape(kv_piece.shape[1], -1),
        jnp.transpose(w_out.astype(jnp.bfloat16)),
        jnp.transpose(w_gateup.astype(jnp.bfloat16), (1, 0, 2)).reshape(w_gateup.shape[1], -1),
        jnp.transpose(w_down.astype(jnp.bfloat16)),
    ]
    widths = [p.shape[1] for p in pieces]
    offsets = [sum(widths[:i]) for i in range(len(widths) + 1)]
    attn_full = gather_rows(jnp.concatenate(pieces[:3], axis=1))
    ffn_full = lax.all_gather(jnp.concatenate(pieces[3:], axis=1), ROWPAGE, axis=0, tiled=True)
    qkv_w = attn_full[:, offsets[0] : offsets[2]]
    out_t = attn_full[:, offsets[2] : offsets[3]]
    gateup_w = ffn_full[:, : offsets[4] - offsets[3]]
    down_t = ffn_full[:, offsets[4] - offsets[3] :]

    prompt_count, seq_len, local_feat = tokens.shape
    xx_count = lax.axis_size("xx")
    zh_count = lax.axis_size("zh")
    gathered = gather_col(tokens)
    attn_in = normalize_blocks(gathered.astype(jnp.float32), attn_gain).astype(jnp.bfloat16)
    projected = project_blocks(attn_in, qkv_w)
    projected = projected.reshape(prompt_count, seq_len, local_heads + 2, head_dim)
    queries = rotate(normalize(projected[:, :, :local_heads], query_gain)).astype(jnp.bfloat16)
    keys_one = rotate(normalize(projected[:, :, local_heads : local_heads + 1], key_gain)).astype(
        jnp.bfloat16
    )
    values_one = projected[:, :, local_heads + 1 : local_heads + 2].astype(jnp.bfloat16)
    keys_rot = jnp.broadcast_to(keys_one, queries.shape)
    values_in = jnp.broadcast_to(values_one, queries.shape)
    attended = jnp.stack(
        [
            attend(queries[i], keys_rot[i], values_in[i], lengths[i]).reshape(seq_len, local_width)
            for i in range(prompt_count)
        ]
    )
    incoming = send_pages(keys_rot, values_in, lengths, page_slot)
    attn_terms = terms_blocks(attended, out_t, xx_count, zh_count).astype(jnp.bfloat16)
    attn_sum = scatter_sum_col(attn_terms)
    residual = (tokens.astype(jnp.float32) + attn_sum).astype(jnp.bfloat16)
    incoming, residual = lax.optimization_barrier((incoming, residual))
    residual_all = gather_col(residual)
    ffn_in = normalize_blocks(residual_all.astype(jnp.float32), ffn_gain).astype(jnp.bfloat16)
    gate_up = project_blocks(ffn_in, gateup_w)
    hidden = (jax.nn.silu(gate_up[..., :unit_count]) * gate_up[..., unit_count:]).astype(jnp.bfloat16)
    ffn_terms = terms_blocks(hidden, down_t, xx_count, zh_count)
    ffn_sum = scatter_sum_col(ffn_terms.astype(jnp.bfloat16))
    layer_out = (residual.astype(jnp.float32) + ffn_sum).astype(jnp.bfloat16)
    page_index = lax.axis_index("page")
    page_count = lax.axis_size("page")
    blocks_each = prompt_count * (seq_len // PAGE_LEN)
    capacity = blocks_each // page_count
    owners = page_slot // blocks_each
    local_slot = page_slot % blocks_each
    same_owner = owners[:, :, None] == owners[:, None, :]
    earlier = (
        jnp.arange(blocks_each, dtype=jnp.int32)[None, :]
        < jnp.arange(blocks_each, dtype=jnp.int32)[:, None]
    )
    order_in = jnp.sum((same_owner & earlier[None]).astype(jnp.int32), axis=2)
    arrival_hit = (owners[:, None, :] == page_index) & (
        order_in[:, None, :] == jnp.arange(capacity, dtype=jnp.int32)[None, :, None]
    )
    arrival_slot = jnp.sum(jnp.where(arrival_hit, local_slot[:, None, :], 0), axis=2).reshape(
        blocks_each
    )
    kv_pages = jnp.zeros_like(incoming).at[:, arrival_slot].set(incoming)
    return (layer_out, kv_pages)


def solution(mesh):
    in_specs = (
        P(ROWPAGE, None, COL),
        P(ROWPAGE),
        P(ROW, None),
        P(ROWPAGE, COL),
        P(None, ROWPAGE, None),
        P(COL, ROWPAGE),
        P(None, ROWPAGE, COL),
        P(COL, ROWPAGE),
        P(),
        P(),
        P(),
        P(),
    )
    out_specs = (P(ROWPAGE, None, COL), P(None, ROWPAGE, None, COL))
    fine = Mesh(
        mesh.devices.reshape(
            mesh.shape["row"] // 2, 2, 2, mesh.shape["col"] // 2, mesh.shape["page"]
        ),
        ("ry", "rc", "zh", "xx", "page"),
    )
    return jax.shard_map(
        on_device, mesh=fine, in_specs=in_specs, out_specs=out_specs, check_vma=False
    )
```

```python
import jax
import jax.numpy as jnp
from jax import lax
from jax.sharding import Mesh, PartitionSpec as P

PAGE_LEN = 128
ROW = ("ry", "rc")
COL = ("zh", "xx")
ROWPAGE = ("ry", "rc", "page")


def normalize(values, norm_gain):
    mean_sq = jnp.mean(values * values, axis=-1, keepdims=True)
    return values * lax.rsqrt(mean_sq + 1e-06) * norm_gain


def rotate(values):
    row_count = values.shape[-3]
    head_dim = values.shape[-1]
    half_dim = head_dim // 2
    frequency = 10000.0 ** (-2.0 * jnp.arange(half_dim, dtype=jnp.float32) / head_dim)
    angles = jnp.arange(row_count, dtype=jnp.float32)[:, None] * frequency[None, :]
    cosine = jnp.cos(angles)[:, None, :]
    sine_table = jnp.sin(angles)[:, None, :]
    leading = values[..., :half_dim]
    trailing = values[..., half_dim:]
    return jnp.concatenate(
        [leading * cosine - trailing * sine_table, trailing * cosine + leading * sine_table],
        axis=-1,
    )


def attend(query_rows, key_rows, value_rows, length):
    row_count = query_rows.shape[0]
    scores = jnp.einsum(
        "qhd,khd->hqk", query_rows, key_rows, preferred_element_type=jnp.float32
    ) * query_rows.shape[2] ** (-0.5)
    positions = jnp.arange(row_count, dtype=jnp.int32)
    seen_keys = (positions[None, :] <= positions[:, None]) & (positions[None, :] < length)
    exp_scores = jnp.where(seen_keys[None], jnp.exp(scores), 0.0)
    attn_probs = (exp_scores / jnp.sum(exp_scores, axis=-1, keepdims=True)).astype(jnp.bfloat16)
    attended = jnp.einsum(
        "hqk,khd->qhd", attn_probs, value_rows, preferred_element_type=jnp.float32
    )
    live_rows = (positions < length)[:, None, None]
    return jnp.where(live_rows, attended, 0.0).astype(jnp.bfloat16)


def contract_rows(lhs, rhs_t):
    return lax.dot_general(
        lhs, rhs_t, (((1,), (1,)), ((), ())), preferred_element_type=jnp.float32
    )


def gather_a2a(x, axis_name, axis):
    count = lax.axis_size(axis_name)
    copies = jnp.broadcast_to(x[None], (count,) + x.shape)
    got = lax.all_to_all(copies, axis_name, 0, 0, tiled=True)
    got = jnp.moveaxis(got, 0, axis)
    shape = list(x.shape)
    shape[axis] *= count
    return got.reshape(shape)


def scatter_sum_a2a(x, axis_name, axis):
    count = lax.axis_size(axis_name)
    shape = list(x.shape)
    split = shape[:axis] + [count, shape[axis] // count] + shape[axis + 1 :]
    got = lax.all_to_all(x.reshape(split), axis_name, axis, axis, tiled=True)
    return jnp.sum(got.astype(jnp.float32), axis=axis)


def swap_halves(x):
    return lax.ppermute(x, "zh", [(0, 1), (1, 0)])


def gather_col(x):
    half = lax.axis_index("zh")
    other = swap_halves(x)
    pair = jnp.stack([jnp.where(half == 0, x, other), jnp.where(half == 0, other, x)])
    count = lax.axis_size("xx")
    copies = jnp.broadcast_to(pair[None], (count,) + pair.shape)
    return lax.all_to_all(copies, "xx", 0, 0, tiled=True)


def scatter_sum_col(terms):
    got = lax.all_to_all(terms, "xx", 0, 0, tiled=True)
    part = jnp.sum(got.astype(jnp.float32), axis=0)
    half = lax.axis_index("zh")
    mine = jnp.take(part, half, axis=-2)
    theirs = swap_halves(jnp.take(part, 1 - half, axis=-2).astype(jnp.bfloat16))
    return mine + theirs.astype(jnp.float32)


def normalize_blocks(values, norm_gain):
    xx_count, zh_count = values.shape[0], values.shape[1]
    gain = jnp.swapaxes(norm_gain.reshape(zh_count, xx_count, -1), 0, 1)[:, :, None, None, :]
    mean_sq = jnp.mean(values * values, axis=(0, 1, 4), keepdims=True)
    return values * lax.rsqrt(mean_sq + 1e-06) * gain


def project_blocks(values, weights):
    xx_count, zh_count, block = values.shape[0], values.shape[1], values.shape[4]
    w = weights.reshape(zh_count, xx_count, block, -1)
    return jnp.einsum("xzpse,zxen->psn", values, w, preferred_element_type=jnp.float32)


def terms_blocks(values, weights_t, xx_count, zh_count):
    w = weights_t.reshape(zh_count, xx_count, -1, weights_t.shape[1])
    return jnp.einsum("psk,zxek->xpsze", values, w, preferred_element_type=jnp.float32)


def gather_shifts(x, axis_name):
    count = lax.axis_size(axis_name)
    index = lax.axis_index(axis_name)
    shifted = [x] + [
        lax.ppermute(x, axis_name, [(i, (i + k) % count) for i in range(count)]) for k in range(1, count)
    ]
    source_shift = (index - jnp.arange(count, dtype=jnp.int32)) % count
    return jnp.take(jnp.stack(shifted), source_shift, axis=0)


def gather_rows(x):
    got = gather_shifts(x, "page").reshape((-1,) + x.shape[1:])
    got = gather_shifts(got, "ry")
    chips = lax.axis_size("ry")
    core = lax.axis_index("rc")
    other = lax.ppermute(got, "rc", [(0, 1), (1, 0)])
    got = jnp.stack([jnp.where(core == 0, got, other), jnp.where(core == 0, other, got)], axis=1)
    return got.reshape((-1,) + x.shape[1:])


def send_pages(keys_rot, values_in, lengths, page_slot):
    prompt_count, seq_len, local_heads, head_dim = keys_rot.shape
    local_width = local_heads * head_dim
    page_count = lax.axis_size("page")
    page_index = lax.axis_index("page")
    blocks_each = prompt_count * (seq_len // PAGE_LEN)
    capacity = blocks_each // page_count
    owners = page_slot // blocks_each
    local_slot = page_slot % blocks_each
    same_owner = owners[:, :, None] == owners[:, None, :]
    earlier = (
        jnp.arange(blocks_each, dtype=jnp.int32)[None, :]
        < jnp.arange(blocks_each, dtype=jnp.int32)[:, None]
    )
    order_in = jnp.sum((same_owner & earlier[None]).astype(jnp.int32), axis=2)
    my_owners = lax.dynamic_index_in_dim(owners, page_index, 0, keepdims=False)
    my_order = lax.dynamic_index_in_dim(order_in, page_index, 0, keepdims=False)
    send_pos = my_owners * capacity + my_order
    live_rows = (jnp.arange(seq_len, dtype=jnp.int32)[None, :] < lengths[:, None])[:, :, None, None]
    page_keys = jnp.where(live_rows, keys_rot, jnp.zeros_like(keys_rot)).reshape(
        blocks_each, PAGE_LEN, local_width
    )
    page_values = jnp.where(live_rows, values_in, jnp.zeros_like(values_in)).reshape(
        blocks_each, PAGE_LEN, local_width
    )
    stacked = jnp.stack([page_keys, page_values])
    outgoing = jnp.zeros_like(stacked).at[:, send_pos].set(stacked)
    incoming = lax.all_to_all(outgoing, "page", split_axis=1, concat_axis=1, tiled=True)
    return incoming


def on_device(
    tokens,
    lengths,
    page_slot,
    w_query,
    w_keyval,
    w_out,
    w_gateup,
    w_down,
    attn_gain,
    ffn_gain,
    query_gain,
    key_gain,
):
    col_count = lax.axis_size(COL)
    col_index = lax.axis_index(COL)
    head_dim = query_gain.shape[0]
    local_width = w_query.shape[1]
    local_heads = local_width // head_dim
    kv_heads = w_keyval.shape[2] // head_dim
    group_size = local_heads * col_count // kv_heads
    assert group_size % local_heads == 0
    kv_head = (col_index * local_heads) // group_size
    unit_count = w_gateup.shape[2]
    kv_piece = lax.dynamic_slice_in_dim(w_keyval, kv_head * head_dim, head_dim, axis=2)
    pieces = [
        w_query.astype(jnp.bfloat16),
        jnp.transpose(kv_piece.astype(jnp.bfloat16), (1, 0, 2)).reshape(kv_piece.shape[1], -1),
        jnp.transpose(w_out.astype(jnp.bfloat16)),
        jnp.transpose(w_gateup.astype(jnp.bfloat16), (1, 0, 2)).reshape(w_gateup.shape[1], -1),
        jnp.transpose(w_down.astype(jnp.bfloat16)),
    ]
    widths = [p.shape[1] for p in pieces]
    offsets = [sum(widths[:i]) for i in range(len(widths) + 1)]
    attn_full = gather_rows(jnp.concatenate(pieces[:3], axis=1))
    ffn_full = lax.all_gather(jnp.concatenate(pieces[3:], axis=1), ROWPAGE, axis=0, tiled=True)
    qkv_w = attn_full[:, offsets[0] : offsets[2]]
    out_t = attn_full[:, offsets[2] : offsets[3]]
    gateup_w = ffn_full[:, : offsets[4] - offsets[3]]
    down_t = ffn_full[:, offsets[4] - offsets[3] :]

    prompt_count, seq_len, local_feat = tokens.shape
    xx_count = lax.axis_size("xx")
    zh_count = lax.axis_size("zh")
    gathered = gather_col(tokens)
    attn_in = normalize_blocks(gathered.astype(jnp.float32), attn_gain).astype(jnp.bfloat16)
    projected = project_blocks(attn_in, qkv_w)
    projected = projected.reshape(prompt_count, seq_len, local_heads + 2, head_dim)
    queries = rotate(normalize(projected[:, :, :local_heads], query_gain)).astype(jnp.bfloat16)
    keys_one = rotate(normalize(projected[:, :, local_heads : local_heads + 1], key_gain)).astype(
        jnp.bfloat16
    )
    values_one = projected[:, :, local_heads + 1 : local_heads + 2].astype(jnp.bfloat16)
    keys_rot = jnp.broadcast_to(keys_one, queries.shape)
    values_in = jnp.broadcast_to(values_one, queries.shape)
    attended = jnp.stack(
        [
            attend(queries[i], keys_rot[i], values_in[i], lengths[i]).reshape(seq_len, local_width)
            for i in range(prompt_count)
        ]
    )
    incoming = send_pages(keys_rot, values_in, lengths, page_slot)
    attn_terms = terms_blocks(attended, out_t, xx_count, zh_count).astype(jnp.bfloat16)
    attn_sum = scatter_sum_col(attn_terms)
    residual = (tokens.astype(jnp.float32) + attn_sum).astype(jnp.bfloat16)
    incoming, residual = lax.optimization_barrier((incoming, residual))
    residual_all = gather_col(residual)
    ffn_in = normalize_blocks(residual_all.astype(jnp.float32), ffn_gain).astype(jnp.bfloat16)
    gate_up = project_blocks(ffn_in, gateup_w)
    hidden = (jax.nn.silu(gate_up[..., :unit_count]) * gate_up[..., unit_count:]).astype(jnp.bfloat16)
    ffn_terms = terms_blocks(hidden, down_t, xx_count, zh_count)
    ffn_sum = scatter_sum_col(ffn_terms.astype(jnp.bfloat16))
    layer_out = (residual.astype(jnp.float32) + ffn_sum).astype(jnp.bfloat16)
    page_index = lax.axis_index("page")
    page_count = lax.axis_size("page")
    blocks_each = prompt_count * (seq_len // PAGE_LEN)
    capacity = blocks_each // page_count
    owners = page_slot // blocks_each
    local_slot = page_slot % blocks_each
    same_owner = owners[:, :, None] == owners[:, None, :]
    earlier = (
        jnp.arange(blocks_each, dtype=jnp.int32)[None, :]
        < jnp.arange(blocks_each, dtype=jnp.int32)[:, None]
    )
    order_in = jnp.sum((same_owner & earlier[None]).astype(jnp.int32), axis=2)
    arrival_hit = (owners[:, None, :] == page_index) & (
        order_in[:, None, :] == jnp.arange(capacity, dtype=jnp.int32)[None, :, None]
    )
    arrival_slot = jnp.sum(jnp.where(arrival_hit, local_slot[:, None, :], 0), axis=2).reshape(
        blocks_each
    )
    kv_pages = jnp.zeros_like(incoming).at[:, arrival_slot].set(incoming)
    return (layer_out, kv_pages)


def solution(mesh):
    in_specs = (
        P(ROWPAGE, None, COL),
        P(ROWPAGE),
        P(ROW, None),
        P(ROWPAGE, COL),
        P(None, ROWPAGE, None),
        P(COL, ROWPAGE),
        P(None, ROWPAGE, COL),
        P(COL, ROWPAGE),
        P(),
        P(),
        P(),
        P(),
    )
    out_specs = (P(ROWPAGE, None, COL), P(None, ROWPAGE, None, COL))
    fine = Mesh(
        mesh.devices.reshape(
            mesh.shape["row"] // 2, 2, 2, mesh.shape["col"] // 2, mesh.shape["page"]
        ),
        ("ry", "rc", "zh", "xx", "page"),
    )
    return jax.shard_map(
        on_device, mesh=fine, in_specs=in_specs, out_specs=out_specs, check_vma=False
    )
```

```python
import jax
import jax.numpy as jnp
from jax import lax
from jax.sharding import Mesh, PartitionSpec as P

PAGE_LEN = 128
ROW = ("ry", "rc")
COL = ("zh", "xx")
ROWPAGE = ("ry", "rc", "page")


def normalize(values, norm_gain):
    mean_sq = jnp.mean(values * values, axis=-1, keepdims=True)
    return values * lax.rsqrt(mean_sq + 1e-06) * norm_gain


def rotate(values):
    row_count = values.shape[-3]
    head_dim = values.shape[-1]
    half_dim = head_dim // 2
    frequency = 10000.0 ** (-2.0 * jnp.arange(half_dim, dtype=jnp.float32) / head_dim)
    angles = jnp.arange(row_count, dtype=jnp.float32)[:, None] * frequency[None, :]
    cosine = jnp.cos(angles)[:, None, :]
    sine_table = jnp.sin(angles)[:, None, :]
    leading = values[..., :half_dim]
    trailing = values[..., half_dim:]
    return jnp.concatenate(
        [leading * cosine - trailing * sine_table, trailing * cosine + leading * sine_table],
        axis=-1,
    )


def attend(query_rows, key_rows, value_rows, length):
    row_count = query_rows.shape[0]
    scores = jnp.einsum(
        "qhd,khd->hqk", query_rows, key_rows, preferred_element_type=jnp.float32
    ) * query_rows.shape[2] ** (-0.5)
    positions = jnp.arange(row_count, dtype=jnp.int32)
    seen_keys = (positions[None, :] <= positions[:, None]) & (positions[None, :] < length)
    exp_scores = jnp.where(seen_keys[None], jnp.exp(scores), 0.0)
    attn_probs = (exp_scores / jnp.sum(exp_scores, axis=-1, keepdims=True)).astype(jnp.bfloat16)
    attended = jnp.einsum(
        "hqk,khd->qhd", attn_probs, value_rows, preferred_element_type=jnp.float32
    )
    live_rows = (positions < length)[:, None, None]
    return jnp.where(live_rows, attended, 0.0).astype(jnp.bfloat16)


def contract_rows(lhs, rhs_t):
    return lax.dot_general(
        lhs, rhs_t, (((1,), (1,)), ((), ())), preferred_element_type=jnp.float32
    )


def gather_a2a(x, axis_name, axis):
    count = lax.axis_size(axis_name)
    copies = jnp.broadcast_to(x[None], (count,) + x.shape)
    got = lax.all_to_all(copies, axis_name, 0, 0, tiled=True)
    got = jnp.moveaxis(got, 0, axis)
    shape = list(x.shape)
    shape[axis] *= count
    return got.reshape(shape)


def scatter_sum_a2a(x, axis_name, axis):
    count = lax.axis_size(axis_name)
    shape = list(x.shape)
    split = shape[:axis] + [count, shape[axis] // count] + shape[axis + 1 :]
    got = lax.all_to_all(x.reshape(split), axis_name, axis, axis, tiled=True)
    return jnp.sum(got.astype(jnp.float32), axis=axis)


def swap_halves(x):
    return lax.ppermute(x, "zh", [(0, 1), (1, 0)])


def gather_col(x):
    half = lax.axis_index("zh")
    other = swap_halves(x)
    pair = jnp.stack([jnp.where(half == 0, x, other), jnp.where(half == 0, other, x)])
    count = lax.axis_size("xx")
    copies = jnp.broadcast_to(pair[None], (count,) + pair.shape)
    return lax.all_to_all(copies, "xx", 0, 0, tiled=True)


def scatter_sum_col(terms):
    got = lax.all_to_all(terms, "xx", 0, 0, tiled=True)
    part = jnp.sum(got.astype(jnp.float32), axis=0)
    half = lax.axis_index("zh")
    mine = jnp.take(part, half, axis=-2)
    theirs = swap_halves(jnp.take(part, 1 - half, axis=-2).astype(jnp.bfloat16))
    return mine + theirs.astype(jnp.float32)


def normalize_blocks(values, norm_gain):
    xx_count, zh_count = values.shape[0], values.shape[1]
    gain = jnp.swapaxes(norm_gain.reshape(zh_count, xx_count, -1), 0, 1)[:, :, None, None, :]
    mean_sq = jnp.mean(values * values, axis=(0, 1, 4), keepdims=True)
    return values * lax.rsqrt(mean_sq + 1e-06) * gain


def project_blocks(values, weights):
    xx_count, zh_count, block = values.shape[0], values.shape[1], values.shape[4]
    w = weights.reshape(zh_count, xx_count, block, -1)
    return jnp.einsum("xzpse,zxen->psn", values, w, preferred_element_type=jnp.float32)


def terms_blocks(values, weights_t, xx_count, zh_count):
    w = weights_t.reshape(zh_count, xx_count, -1, weights_t.shape[1])
    return jnp.einsum("psk,zxek->xpsze", values, w, preferred_element_type=jnp.float32)


def gather_rows(x):
    pages = lax.axis_size("page")
    got = lax.all_to_all(jnp.broadcast_to(x[None], (pages,) + x.shape), "page", 0, 0, tiled=True)
    got = got.reshape((-1,) + x.shape[1:])
    chips = lax.axis_size("ry")
    chip = lax.axis_index("ry")
    shifted = [got] + [
        lax.ppermute(got, "ry", [(i, (i + k) % chips) for i in range(chips)]) for k in range(1, chips)
    ]
    source_shift = (chip - jnp.arange(chips, dtype=jnp.int32)) % chips
    got = jnp.take(jnp.stack(shifted), source_shift, axis=0)
    core = lax.axis_index("rc")
    other = lax.ppermute(got, "rc", [(0, 1), (1, 0)])
    got = jnp.stack([jnp.where(core == 0, got, other), jnp.where(core == 0, other, got)], axis=1)
    return got.reshape((-1,) + x.shape[1:])


def send_pages(keys_rot, values_in, lengths, page_slot):
    prompt_count, seq_len, local_heads, head_dim = keys_rot.shape
    local_width = local_heads * head_dim
    page_count = lax.axis_size("page")
    page_index = lax.axis_index("page")
    blocks_each = prompt_count * (seq_len // PAGE_LEN)
    capacity = blocks_each // page_count
    owners = page_slot // blocks_each
    local_slot = page_slot % blocks_each
    same_owner = owners[:, :, None] == owners[:, None, :]
    earlier = (
        jnp.arange(blocks_each, dtype=jnp.int32)[None, :]
        < jnp.arange(blocks_each, dtype=jnp.int32)[:, None]
    )
    order_in = jnp.sum((same_owner & earlier[None]).astype(jnp.int32), axis=2)
    my_owners = lax.dynamic_index_in_dim(owners, page_index, 0, keepdims=False)
    my_order = lax.dynamic_index_in_dim(order_in, page_index, 0, keepdims=False)
    send_pos = my_owners * capacity + my_order
    live_rows = (jnp.arange(seq_len, dtype=jnp.int32)[None, :] < lengths[:, None])[:, :, None, None]
    page_keys = jnp.where(live_rows, keys_rot, jnp.zeros_like(keys_rot)).reshape(
        blocks_each, PAGE_LEN, local_width
    )
    page_values = jnp.where(live_rows, values_in, jnp.zeros_like(values_in)).reshape(
        blocks_each, PAGE_LEN, local_width
    )
    stacked = jnp.stack([page_keys, page_values])
    outgoing = jnp.zeros_like(stacked).at[:, send_pos].set(stacked)
    incoming = lax.all_to_all(outgoing, "page", split_axis=1, concat_axis=1, tiled=True)
    return incoming


def on_device(
    tokens,
    lengths,
    page_slot,
    w_query,
    w_keyval,
    w_out,
    w_gateup,
    w_down,
    attn_gain,
    ffn_gain,
    query_gain,
    key_gain,
):
    col_count = lax.axis_size(COL)
    col_index = lax.axis_index(COL)
    head_dim = query_gain.shape[0]
    local_width = w_query.shape[1]
    local_heads = local_width // head_dim
    kv_heads = w_keyval.shape[2] // head_dim
    group_size = local_heads * col_count // kv_heads
    assert group_size % local_heads == 0
    kv_head = (col_index * local_heads) // group_size
    unit_count = w_gateup.shape[2]
    kv_piece = lax.dynamic_slice_in_dim(w_keyval, kv_head * head_dim, head_dim, axis=2)
    pieces = [
        w_query.astype(jnp.bfloat16),
        jnp.transpose(kv_piece.astype(jnp.bfloat16), (1, 0, 2)).reshape(kv_piece.shape[1], -1),
        jnp.transpose(w_out.astype(jnp.bfloat16)),
        jnp.transpose(w_gateup.astype(jnp.bfloat16), (1, 0, 2)).reshape(w_gateup.shape[1], -1),
        jnp.transpose(w_down.astype(jnp.bfloat16)),
    ]
    widths = [p.shape[1] for p in pieces]
    offsets = [sum(widths[:i]) for i in range(len(widths) + 1)]
    attn_full = gather_rows(jnp.concatenate(pieces[:3], axis=1))
    ffn_full = lax.all_gather(jnp.concatenate(pieces[3:], axis=1), ROWPAGE, axis=0, tiled=True)
    qkv_w = attn_full[:, offsets[0] : offsets[2]]
    out_t = attn_full[:, offsets[2] : offsets[3]]
    gateup_w = ffn_full[:, : offsets[4] - offsets[3]]
    down_t = ffn_full[:, offsets[4] - offsets[3] :]

    prompt_count, seq_len, local_feat = tokens.shape
    xx_count = lax.axis_size("xx")
    zh_count = lax.axis_size("zh")
    gathered = gather_col(tokens)
    attn_in = normalize_blocks(gathered.astype(jnp.float32), attn_gain).astype(jnp.bfloat16)
    projected = project_blocks(attn_in, qkv_w)
    projected = projected.reshape(prompt_count, seq_len, local_heads + 2, head_dim)
    queries = rotate(normalize(projected[:, :, :local_heads], query_gain)).astype(jnp.bfloat16)
    keys_one = rotate(normalize(projected[:, :, local_heads : local_heads + 1], key_gain)).astype(
        jnp.bfloat16
    )
    values_one = projected[:, :, local_heads + 1 : local_heads + 2].astype(jnp.bfloat16)
    keys_rot = jnp.broadcast_to(keys_one, queries.shape)
    values_in = jnp.broadcast_to(values_one, queries.shape)
    attended = jnp.stack(
        [
            attend(queries[i], keys_rot[i], values_in[i], lengths[i]).reshape(seq_len, local_width)
            for i in range(prompt_count)
        ]
    )
    incoming = send_pages(keys_rot, values_in, lengths, page_slot)
    attn_terms = terms_blocks(attended, out_t, xx_count, zh_count).astype(jnp.bfloat16)
    attn_sum = scatter_sum_col(attn_terms)
    residual = (tokens.astype(jnp.float32) + attn_sum).astype(jnp.bfloat16)
    incoming, residual = lax.optimization_barrier((incoming, residual))
    residual_all = gather_col(residual)
    ffn_in = normalize_blocks(residual_all.astype(jnp.float32), ffn_gain).astype(jnp.bfloat16)
    gate_up = project_blocks(ffn_in, gateup_w)
    hidden = (jax.nn.silu(gate_up[..., :unit_count]) * gate_up[..., unit_count:]).astype(jnp.bfloat16)
    ffn_terms = terms_blocks(hidden, down_t, xx_count, zh_count)
    ffn_terms = ffn_terms.astype(jnp.bfloat16)
    mid = seq_len // 2
    ffn_sum = jnp.concatenate(
        [scatter_sum_col(ffn_terms[:, :, :mid]), scatter_sum_col(ffn_terms[:, :, mid:])], axis=1
    )
    layer_out = (residual.astype(jnp.float32) + ffn_sum).astype(jnp.bfloat16)
    page_index = lax.axis_index("page")
    page_count = lax.axis_size("page")
    blocks_each = prompt_count * (seq_len // PAGE_LEN)
    capacity = blocks_each // page_count
    owners = page_slot // blocks_each
    local_slot = page_slot % blocks_each
    same_owner = owners[:, :, None] == owners[:, None, :]
    earlier = (
        jnp.arange(blocks_each, dtype=jnp.int32)[None, :]
        < jnp.arange(blocks_each, dtype=jnp.int32)[:, None]
    )
    order_in = jnp.sum((same_owner & earlier[None]).astype(jnp.int32), axis=2)
    arrival_hit = (owners[:, None, :] == page_index) & (
        order_in[:, None, :] == jnp.arange(capacity, dtype=jnp.int32)[None, :, None]
    )
    arrival_slot = jnp.sum(jnp.where(arrival_hit, local_slot[:, None, :], 0), axis=2).reshape(
        blocks_each
    )
    kv_pages = jnp.zeros_like(incoming).at[:, arrival_slot].set(incoming)
    return (layer_out, kv_pages)


def solution(mesh):
    in_specs = (
        P(ROWPAGE, None, COL),
        P(ROWPAGE),
        P(ROW, None),
        P(ROWPAGE, COL),
        P(None, ROWPAGE, None),
        P(COL, ROWPAGE),
        P(None, ROWPAGE, COL),
        P(COL, ROWPAGE),
        P(),
        P(),
        P(),
        P(),
    )
    out_specs = (P(ROWPAGE, None, COL), P(None, ROWPAGE, None, COL))
    fine = Mesh(
        mesh.devices.reshape(
            mesh.shape["row"] // 2, 2, 2, mesh.shape["col"] // 2, mesh.shape["page"]
        ),
        ("ry", "rc", "zh", "xx", "page"),
    )
    return jax.shard_map(
        on_device, mesh=fine, in_specs=in_specs, out_specs=out_specs, check_vma=False
    )
```
